128 devices in a mesh: lon: 16 (over y_hi, z, core), lat: 8 (over y_lo, x).
Axes of the slice: x: 4, y: 4 (y_hi: 2, y_lo: 2; y = y_hi * 2 + y_lo), z: 4, core: 2. Of those that a mesh axis runs over, the one named last changes fastest.
Arguments:
- temp_before: float32 [25, 512, 2048], P(None, 'lat', 'lon'), may hold values from -8 to 8
- temp_now: float32 [25, 512, 2048], P(None, 'lat', 'lon'), may hold values from -8 to 8
- salt_before: float32 [25, 512, 2048], P(None, 'lat', 'lon'), may hold values from -4 to 4
- salt_now: float32 [25, 512, 2048], P(None, 'lat', 'lon'), may hold values from -4 to 4
- east_velocity: float32 [25, 512, 2048], P(None, 'lat', 'lon'), may hold values from -0.3 to 0.3, as said below
- north_velocity: float32 [25, 512, 2048], P(None, 'lat', 'lon'), may hold values from -0.3 to 0.3, as said below
- bottom_level: int32 [512, 2048], P('lat', 'lon'), may hold values from 0 to 25, as said below
Outputs:
- temp_out: float32 [25, 512, 2048], P(None, 'lat', 'lon')
- salt_out: float32 [25, 512, 2048], P(None, 'lat', 'lon')
- density_out: float32 [25, 512, 2048], P(None, 'lat', 'lon')
The draws below stay inside these ranges and needn't reach their ends.
Inputs may be any that keep to these rules, and one draw needn't show every extreme that they name: `bottom_level`: cells at levels below a column's value are ocean, the others land; every column of row 0 is land. `east_velocity`: zero on every face that touches a land cell; the face east of column 2047 touches column 0. `north_velocity`: zero on every face that touches a land cell; on row 511 the north face of column i touches cell (511, 2047 - i) and carries the negative of that column's value.
All inputs are finite; a program needn't handle non-finite values.
Results may differ from the reference program's by a relative error of at most 0.00002.
Values sent between devices are 32-bit elements; how exact they have to be, the bound alone decides.
No kernel may reach another device: no remote copies, remote signals or barrier semaphores. Data moves between devices by JAX's collectives and lax.ppermute only.
A program may use at most 256 MiB of HBM per device.

```python
import jax
import jax.numpy as jnp
from jax import lax

K = 25
NI = 2048
NJ = 512


def column_levels(key):
    base = jax.random.fold_in(key, 11)
    land_draw = jax.random.randint(jax.random.fold_in(base, 1), (NJ, NI), 0, 10)
    depths = jax.random.randint(jax.random.fold_in(base, 2), (NJ, NI), 1, K + 1)
    levels = jnp.where(land_draw < 3, 0, depths)
    row_ids = lax.broadcasted_iota(jnp.int32, (NJ, NI), 0)
    col_ids = lax.broadcasted_iota(jnp.int32, (NJ, NI), 1)
    levels = jnp.where(row_ids == 0, 0, levels)
    levels = jnp.where((row_ids == NJ // 2) & (col_ids == 0), K, levels)
    return levels.astype(jnp.int32)


def wet_cells(key):
    levels = column_levels(key)
    return (jnp.arange(K, dtype=jnp.int32)[:, None, None] < levels[None]).astype(jnp.float32)


def face_sample(key, salt_value):
    sub_key = jax.random.fold_in(key, salt_value)
    sample = jnp.clip(0.12 * jax.random.normal(sub_key, (K, NJ, NI), jnp.float32), -0.3, 0.3)
    return sample


def draw_bottom_level(key, part):
    return column_levels(key)


def draw_east_velocity(key, part):
    wet_mask = wet_cells(key)
    sample = face_sample(key, 21)
    return sample * wet_mask * jnp.roll(wet_mask, -1, axis=2)


def draw_north_velocity(key, part):
    wet_mask = wet_cells(key)
    sample = face_sample(key, 31)
    partner = jnp.concatenate([wet_mask[:, 1:, :], wet_mask[:, -1:, ::-1]], 1)
    faces = sample * wet_mask * partner
    top_row = 0.5 * (faces[:, -1:, :] - faces[:, -1:, ::-1])
    return jnp.concatenate([faces[:, :-1, :], top_row], 1)


def block_scale(own_key, dims, shards, low, top_value):
    loudness = 1.0
    for axis_at, parts in shards:
        steps = jax.random.uniform(jax.random.fold_in(jax.random.fold_in(own_key, 6), axis_at), (parts,), jnp.float32, low / len(shards), top_value / len(shards))
        loudness = loudness * jnp.repeat(jnp.exp(steps), dims[axis_at] // parts).reshape((-1,) + (1,) * (len(dims) - 1 - axis_at))
    return loudness


def centred(key, extent, width, reach, cuts=(), held_as=jnp.bfloat16):
    gain = block_scale(key, extent, cuts, -0.22, 0.18) if cuts else 1.0
    entries = jax.random.normal(key, extent, jnp.float32) * width * gain
    return jnp.minimum(jnp.maximum(entries, -reach), reach).astype(held_as)


def setup_inputs(seed: int = 0) -> dict:
    splits = jax.random.split(jax.random.key(seed), 8)
    return {
        "temp_before": centred(splits[0], (K, NJ, NI), 1.5, 8.0, ((1, 8), (2, 16)), jnp.float32),
        "temp_now": centred(splits[1], (K, NJ, NI), 1.5, 8.0, ((1, 8), (2, 16)), jnp.float32),
        "salt_before": centred(splits[2], (K, NJ, NI), 0.6, 4.0, ((1, 8), (2, 16)), jnp.float32),
        "salt_now": centred(splits[3], (K, NJ, NI), 0.6, 4.0, ((1, 8), (2, 16)), jnp.float32),
        "east_velocity": draw_east_velocity(jax.random.fold_in(splits[7], 71), 0),
        "north_velocity": draw_north_velocity(jax.random.fold_in(splits[7], 71), 0),
        "bottom_level": draw_bottom_level(jax.random.fold_in(splits[7], 71), 0),
    }


asselin_gamma = 0.1
nu_base = 0.05
nu_conv = 0.2
level_depth = 160.0
alpha_zero = 0.16550
beta_zero = 0.76554
lambda_one = 0.059520
lambda_two = 5.4914e-4
mu_one = 1.4970e-4
mu_two = 1.1090e-5
nu_cross = 2.4341e-3


def density(temp, salt):
    depth = level_depth * (jnp.arange(temp.shape[0], dtype=jnp.float32) + 0.5)[:, None, None]
    warm = -alpha_zero * (1.0 + 0.5 * lambda_one * temp + mu_one * depth) * temp
    salty = beta_zero * (1.0 - 0.5 * lambda_two * salt - mu_two * depth) * salt
    return warm + salty - nu_cross * temp * salt


def divergence(extended, velocity, along):
    face_count = velocity.shape[along - 1]
    behind_far = lax.slice_in_dim(extended, 0, face_count, axis=along)
    behind = lax.slice_in_dim(extended, 1, face_count + 1, axis=along)
    ahead = lax.slice_in_dim(extended, 2, face_count + 2, axis=along)
    ahead_far = lax.slice_in_dim(extended, 3, face_count + 3, axis=along)
    flux = velocity * (7.0 * (behind + ahead) - (behind_far + ahead_far)) / 12.0
    flux = flux + jnp.abs(velocity) * ((ahead_far - behind_far) - 3.0 * (ahead - behind)) / 12.0
    return lax.slice_in_dim(flux, 1, face_count, axis=along) - lax.slice_in_dim(flux, 0, face_count - 1, axis=along)


def vertical_mixing(before, now, ocean_mask):
    density_now = density(now[0], now[1])
    density_jump = density_now[1:] - density_now[:-1]
    mixing_rates = (nu_base + nu_conv * jax.nn.sigmoid(-4.0 * density_jump)) * ocean_mask[1:]
    flux = mixing_rates * (before[:, 1:] - before[:, :-1])
    padding = jnp.zeros_like(flux[:, :1])
    return jnp.concatenate([flux, padding], 1) - jnp.concatenate([padding, flux], 1)


def advance(before, now, x_ext, y_ext, east_faces, north_faces, ocean_mask):
    change = -(divergence(x_ext, east_faces, 3) + divergence(y_ext, north_faces, 2))
    change = change + vertical_mixing(before, now, ocean_mask)
    after = (before + 2.0 * change) * ocean_mask
    filtered = now + asselin_gamma * (before - 2.0 * now + after)
    return filtered, after


def reference(temp_before, temp_now, salt_before, salt_now, east_velocity, north_velocity, bottom_level):
    ocean_mask = (jnp.arange(K, dtype=jnp.int32)[:, None, None] < bottom_level[None]).astype(jnp.float32)
    before = jnp.stack([temp_before, salt_before]) * ocean_mask
    now = jnp.stack([temp_now, salt_now]) * ocean_mask
    east_faces = jnp.concatenate([east_velocity[:, :, -1:], east_velocity], 2)
    north_faces = jnp.concatenate([jnp.zeros_like(north_velocity[:, :1, :]), north_velocity], 1)
    for step_index in range(2):
        x_ext = jnp.concatenate([now[..., -2:], now, now[..., :2]], 3)
        mirror = now[:, :, -2:, ::-1][:, :, ::-1, :]
        y_ext = jnp.concatenate([jnp.zeros_like(now[:, :, :2, :]), now, mirror], 2)
        before, now = advance(before, now, x_ext, y_ext, east_faces, north_faces, ocean_mask)
    final_density = density(now[0], now[1]) * ocean_mask
    return now[0], now[1], final_density
```

```python
import jax
import jax.numpy as jnp
from jax import lax
from jax.sharding import PartitionSpec as P

asselin_gamma = 0.1
nu_base = 0.05
nu_conv = 0.2
level_depth = 160.0
alpha_zero = 0.1655
beta_zero = 0.76554
lambda_one = 0.05952
lambda_two = 0.00054914
mu_one = 0.0001497
mu_two = 1.109e-05
nu_cross = 0.0024341


def extended_2(value, sides, width, wrap):
    for axis, dim in sides:
        count, length = (lax.axis_size(axis), value.shape[dim])
        up = [(i, (i + 1) % count) for i in range(count if wrap else count - 1)]
        down = [(j, i) for i, j in up]
        last = lax.slice_in_dim(value, length - width, length, axis=dim)
        leading = lax.slice_in_dim(value, 0, width, axis=dim)
        before = lax.ppermute(last, axis, up)
        after = lax.ppermute(leading, axis, down)
        value = jnp.concatenate([before, value, after], axis=dim)
    return value


def passed_along(block, axis, distance):
    devices = range(lax.axis_size(axis))
    route = [((i - distance) % len(devices), i) for i in devices]
    return lax.ppermute(block, axis, route)


def from_behind(value, axis, by):
    count = lax.axis_size(axis)
    pairs = [(i, i + by) for i in range(count) if 0 <= i + by < count]
    return lax.ppermute(value, axis, pairs)


def density(temp, salt):
    depth = level_depth * (jnp.arange(temp.shape[0], dtype=jnp.float32) + 0.5)[:, None, None]
    warm = -alpha_zero * (1.0 + 0.5 * lambda_one * temp + mu_one * depth) * temp
    salty = beta_zero * (1.0 - 0.5 * lambda_two * salt - mu_two * depth) * salt
    return warm + salty - nu_cross * temp * salt


def divergence(extended, velocity, along):
    face_count = velocity.shape[along - 1]
    behind_far = lax.slice_in_dim(extended, 0, face_count, axis=along)
    behind = lax.slice_in_dim(extended, 1, face_count + 1, axis=along)
    ahead = lax.slice_in_dim(extended, 2, face_count + 2, axis=along)
    ahead_far = lax.slice_in_dim(extended, 3, face_count + 3, axis=along)
    flux = velocity * (7.0 * (behind + ahead) - (behind_far + ahead_far)) / 12.0
    flux = flux + jnp.abs(velocity) * (ahead_far - behind_far - 3.0 * (ahead - behind)) / 12.0
    return lax.slice_in_dim(flux, 1, face_count, axis=along) - lax.slice_in_dim(
        flux, 0, face_count - 1, axis=along
    )


def vertical_mixing(before, now, ocean_mask):
    density_now = density(now[0], now[1])
    density_jump = density_now[1:] - density_now[:-1]
    mixing_rates = (nu_base + nu_conv * jax.nn.sigmoid(-4.0 * density_jump)) * ocean_mask[1:]
    flux = mixing_rates * (before[:, 1:] - before[:, :-1])
    padding = jnp.zeros_like(flux[:, :1])
    return jnp.concatenate([flux, padding], 1) - jnp.concatenate([padding, flux], 1)


def advance(before, now, x_ext, y_ext, east_faces, north_faces, ocean_mask):
    change = -(divergence(x_ext, east_faces, 3) + divergence(y_ext, north_faces, 2))
    change = change + vertical_mixing(before, now, ocean_mask)
    after = (before + 2.0 * change) * ocean_mask
    filtered = now + asselin_gamma * (before - 2.0 * now + after)
    return (filtered, after)


def extend_tracers(now, at_fold, columns):
    x_ext = extended_2(now, (("lon", 3),), 2, True)
    y_part = extended_2(now, (("lat", 2),), 2, False)
    edge_rows = now[:, :, -2:, :]
    lon_count, lat_count = (lax.axis_size("lon"), lax.axis_size("lat"))
    top = lat_count - 1
    pairs = [(d * lat_count + top, (lon_count - 1 - d) * lat_count + top) for d in range(lon_count)]
    partner_rows = lax.ppermute(edge_rows, ("lon", "lat"), pairs)
    mirror = partner_rows[:, :, ::-1, ::-1]
    north_rows = jnp.where(at_fold, mirror, y_part[:, :, -2:, :])
    y_ext = jnp.concatenate([y_part[:, :, :-2, :], north_rows], 2)
    return (x_ext, y_ext)


def on_device(
    temp_before, temp_now, salt_before, salt_now, east_velocity, north_velocity, bottom_level
):
    levels = temp_now.shape[0]
    columns = temp_now.shape[2]
    ocean_mask = (jnp.arange(levels, dtype=jnp.int32)[:, None, None] < bottom_level[None]).astype(
        jnp.float32
    )
    before = jnp.stack([temp_before, salt_before]) * ocean_mask
    now = jnp.stack([temp_now, salt_now]) * ocean_mask
    west_column = passed_along(east_velocity[:, :, -1:], "lon", 1)
    east_faces = jnp.concatenate([west_column, east_velocity], 2)
    south_row = from_behind(north_velocity[:, -1:, :], "lat", 1)
    north_faces = jnp.concatenate([south_row, north_velocity], 1)
    at_fold = lax.axis_index("lat") == lax.axis_size("lat") - 1
    for step_index in range(2):
        x_ext, y_ext = extend_tracers(now, at_fold, columns)
        before, now = advance(before, now, x_ext, y_ext, east_faces, north_faces, ocean_mask)
    final_density = density(now[0], now[1]) * ocean_mask
    return (now[0], now[1], final_density)


def solution(mesh):
    return jax.shard_map(
        on_device,
        mesh=mesh,
        in_specs=(
            P(None, "lat", "lon"),
            P(None, "lat", "lon"),
            P(None, "lat", "lon"),
            P(None, "lat", "lon"),
            P(None, "lat", "lon"),
            P(None, "lat", "lon"),
            P("lat", "lon"),
        ),
        out_specs=(P(None, "lat", "lon"), P(None, "lat", "lon"), P(None, "lat", "lon")),
        check_vma=False,
    )
```

```python
import functools
import jax
import jax.numpy as jnp
from jax import lax
from jax.experimental import pallas as pl
from jax.experimental.pallas import tpu as pltpu
from jax.sharding import PartitionSpec as P

asselin_gamma = 0.1
nu_base = 0.05
nu_conv = 0.2
level_depth = 160.0
alpha_zero = 0.1655
beta_zero = 0.76554
lambda_one = 0.05952
lambda_two = 0.00054914
mu_one = 0.0001497
mu_two = 1.109e-05
nu_cross = 0.0024341


def density_at(temp, salt, depth):
    warm = -alpha_zero * (1.0 + 0.5 * lambda_one * temp + mu_one * depth) * temp
    salty = beta_zero * (1.0 - 0.5 * lambda_two * salt - mu_two * depth) * salt
    return warm + salty - nu_cross * temp * salt


def face_flux(u, q1, q2, q3, q4):
    flux = u * (7.0 * (q2 + q3) - (q1 + q4)) / 12.0
    return flux + jnp.abs(u) * ((q4 - q1) - 3.0 * (q3 - q2)) / 12.0


def step_kernel(mask_inputs, final, bl_ref, nt_ref, ns_ref, bt_ref, bs_ref, h_ref, yh_ref,
                ue_ref, vn_ref, *rest):
    outs, fv = rest[:-1], rest[-1]
    levels, rows, cols = nt_ref.shape
    lane = lax.broadcasted_iota(jnp.int32, (rows, cols), 1)
    row = lax.broadcasted_iota(jnp.int32, (rows, cols), 0)
    now_refs, bef_refs = (nt_ref, ns_ref), (bt_ref, bs_ref)

    def mask(k):
        return (k < bl_ref[...]).astype(jnp.float32)

    def depth(k):
        return level_depth * (k.astype(jnp.float32) + 0.5)

    def load(ref, k, m):
        v = ref[k]
        return v * m if mask_inputs else v

    zero = jnp.zeros((rows, cols), jnp.float32)
    for f in range(2):
        fv[f, 0] = zero
        fv[f, levels] = zero

    def mixing(k, carry):
        m0, m1 = mask(k), mask(k + 1)
        e0 = density_at(load(nt_ref, k, m0), load(ns_ref, k, m0), depth(k))
        e1 = density_at(load(nt_ref, k + 1, m1), load(ns_ref, k + 1, m1), depth(k + 1))
        rates = (nu_base + nu_conv * jax.nn.sigmoid(-4.0 * (e1 - e0))) * m1
        for f in range(2):
            fv[f, k + 1] = rates * (load(bef_refs[f], k + 1, m1) - load(bef_refs[f], k, m0))
        return carry

    lax.fori_loop(0, levels - 1, mixing, 0)

    def level(k, carry):
        m = mask(k)
        ue, vn = ue_ref[k], vn_ref[k]
        uw = jnp.where(lane < 1, pltpu.roll(h_ref[0, k], cols - 4, 1), pltpu.roll(ue, 1, 1))
        vs = jnp.where(row < 1, jnp.broadcast_to(yh_ref[0, k][4:5], (rows, cols)), pltpu.roll(vn, 1, 0))
        afters = []
        for f in range(2):
            q = load(now_refs[f], k, m)
            b = load(bef_refs[f], k, m)
            h = h_ref[f, k]
            yh = yh_ref[f, k]
            qm1 = jnp.where(lane < 1, pltpu.roll(h, cols - 3, 1), pltpu.roll(q, 1, 1))
            qm2 = jnp.where(lane < 2, pltpu.roll(h, cols - 2, 1), pltpu.roll(q, 2, 1))
            qp1 = jnp.where(lane >= cols - 1, pltpu.roll(h, cols - 1, 1), pltpu.roll(q, cols - 1, 1))
            qp2 = jnp.where(lane >= cols - 2, pltpu.roll(h, cols - 2, 1), pltpu.roll(q, cols - 2, 1))
            div_x = face_flux(ue, qm1, q, qp1, qp2) - face_flux(uw, qm2, qm1, q, qp1)
            s2 = jnp.broadcast_to(yh[0:1], (rows, cols))
            s1 = jnp.broadcast_to(yh[1:2], (rows, cols))
            n1 = jnp.broadcast_to(yh[2:3], (rows, cols))
            n2 = jnp.broadcast_to(yh[3:4], (rows, cols))
            qs1 = jnp.where(row < 1, s1, pltpu.roll(q, 1, 0))
            qs2 = jnp.where(row < 1, s2, jnp.where(row < 2, s1, pltpu.roll(q, 2, 0)))
            qn1 = jnp.where(row >= rows - 1, n1, pltpu.roll(q, rows - 1, 0))
            qn2 = jnp.where(row >= rows - 1, n2, jnp.where(row >= rows - 2, n1, pltpu.roll(q, rows - 2, 0)))
            div_y = face_flux(vn, qs1, q, qn1, qn2) - face_flux(vs, qs2, qs1, q, qn1)
            change = -(div_x + div_y)
            change = change + (fv[f, k + 1] - fv[f, k])
            after = (b + 2.0 * change) * m
            afters.append(after)
            if not final:
                outs[f][k] = q + asselin_gamma * (b - 2.0 * q + after)
                outs[2 + f][k] = after
        if final:
            outs[0][k] = afters[0]
            outs[1][k] = afters[1]
            outs[2][k] = density_at(afters[0], afters[1], depth(k)) * m
        return carry

    lax.fori_loop(0, levels, level, 0)


def step_call(mask_inputs, final, bl, nt, ns, bt, bs, h, yh, ue, vn):
    levels, rows, cols = nt.shape
    field = jax.ShapeDtypeStruct(nt.shape, jnp.float32)
    n_out = 3 if final else 4
    vspec = pl.BlockSpec(memory_space=pltpu.VMEM)
    return pl.pallas_call(
        functools.partial(step_kernel, mask_inputs, final),
        out_shape=tuple([field] * n_out),
        in_specs=[vspec] * 9,
        out_specs=tuple([vspec] * n_out),
        scratch_shapes=[pltpu.VMEM((2, levels + 1, rows, cols), jnp.float32)],
        compiler_params=pltpu.CompilerParams(vmem_limit_bytes=48 * 1024 * 1024),
        cost_estimate=pl.CostEstimate(
            flops=400 * 2 * levels * rows * cols, transcendentals=levels * rows * cols,
            bytes_accessed=4 * levels * rows * cols * (9 + n_out)),
    )(bl, nt, ns, bt, bs, h, yh, ue, vn)


def exchange(t, s, west_column, south_row, at_fold):
    lon_count, lat_count = (lax.axis_size("lon"), lax.axis_size("lat"))
    cols_first = jnp.stack([t[..., :2], s[..., :2]])
    cols_last = jnp.stack([t[..., -2:], s[..., -2:]])
    rows_first = jnp.stack([t[:, :2], s[:, :2]])
    rows_last = jnp.stack([t[:, -2:], s[:, -2:]])
    east = lax.ppermute(cols_first, "lon", [(i, (i - 1) % lon_count) for i in range(lon_count)])
    west = lax.ppermute(cols_last, "lon", [(i, (i + 1) % lon_count) for i in range(lon_count)])
    north = lax.ppermute(rows_first, "lat", [(i, i - 1) for i in range(1, lat_count)])
    south = lax.ppermute(rows_last, "lat", [(i, i + 1) for i in range(lat_count - 1)])
    top = lat_count - 1
    fold_pairs = [(d * lat_count + top, (lon_count - 1 - d) * lat_count + top) for d in range(lon_count)]
    partner = lax.ppermute(rows_last, ("lon", "lat"), fold_pairs)[:, :, ::-1, :]
    cols = t.shape[-1]
    flip = (jnp.arange(cols)[:, None] + jnp.arange(cols)[None, :] == cols - 1).astype(jnp.float32)
    mirror = jnp.einsum("fkrc,cd->fkrd", partner, flip, precision=lax.Precision.HIGHEST)
    north = jnp.where(at_fold, mirror, north)
    shape = cols_first.shape
    halo_x = jnp.concatenate(
        [east, west, jnp.broadcast_to(west_column[None], shape[:3] + (1,)),
         jnp.zeros(shape[:3] + (cols - 5,), jnp.float32)], 3)
    halo_y = jnp.concatenate(
        [south, north, jnp.broadcast_to(south_row[None], (2,) + south_row.shape),
         jnp.zeros((2, t.shape[0], 3, cols), jnp.float32)], 2)
    return halo_x, halo_y


def on_device(
    temp_before, temp_now, salt_before, salt_now, east_velocity, north_velocity, bottom_level
):
    levels = temp_now.shape[0]
    ocean_mask = (jnp.arange(levels, dtype=jnp.int32)[:, None, None] < bottom_level[None]).astype(
        jnp.float32
    )
    lon_count, lat_count = (lax.axis_size("lon"), lax.axis_size("lat"))
    west_column = lax.ppermute(
        east_velocity[:, :, -1:], "lon", [(i, (i + 1) % lon_count) for i in range(lon_count)])
    south_row = lax.ppermute(
        north_velocity[:, -1:, :], "lat", [(i, i + 1) for i in range(lat_count - 1)])
    at_fold = lax.axis_index("lat") == lat_count - 1
    halo_x, halo_y = exchange(temp_now * ocean_mask, salt_now * ocean_mask, west_column, south_row, at_fold)
    ft, fs, at, as_ = step_call(True, False, bottom_level, temp_now, salt_now, temp_before, salt_before,
                                halo_x, halo_y, east_velocity, north_velocity)
    halo_x, halo_y = exchange(at, as_, west_column, south_row, at_fold)
    return step_call(False, True, bottom_level, at, as_, ft, fs, halo_x, halo_y,
                     east_velocity, north_velocity)


def solution(mesh):
    return jax.shard_map(
        on_device,
        mesh=mesh,
        in_specs=(
            P(None, "lat", "lon"),
            P(None, "lat", "lon"),
            P(None, "lat", "lon"),
            P(None, "lat", "lon"),
            P(None, "lat", "lon"),
            P(None, "lat", "lon"),
            P("lat", "lon"),
        ),
        out_specs=(P(None, "lat", "lon"), P(None, "lat", "lon"), P(None, "lat", "lon")),
        check_vma=False,
    )
```

```python
import functools
import jax
import jax.numpy as jnp
from jax import lax
from jax.experimental import pallas as pl
from jax.experimental.pallas import tpu as pltpu
from jax.sharding import PartitionSpec as P

asselin_gamma = 0.1
nu_base = 0.05
nu_conv = 0.2
level_depth = 160.0
alpha_zero = 0.1655
beta_zero = 0.76554
lambda_one = 0.05952
lambda_two = 0.00054914
mu_one = 0.0001497
mu_two = 1.109e-05
nu_cross = 0.0024341


def density_at(temp, salt, depth):
    warm = -alpha_zero * (1.0 + 0.5 * lambda_one * temp + mu_one * depth) * temp
    salty = beta_zero * (1.0 - 0.5 * lambda_two * salt - mu_two * depth) * salt
    return warm + salty - nu_cross * temp * salt


def face_flux(u, q1, q2, q3, q4):
    flux = u * (7.0 * (q2 + q3) - (q1 + q4)) / 12.0
    return flux + jnp.abs(u) * ((q4 - q1) - 3.0 * (q3 - q2)) / 12.0


def edge_tiles(rows, cols):
    r = lax.broadcasted_iota(jnp.int32, (8, cols), 0)
    c = lax.broadcasted_iota(jnp.int32, (8, cols), 1)
    picked = ((r == 0) & (c == 0)) | ((r == 1) & (c == 1))
    picked = picked | ((r == 2) & (c == cols - 2)) | ((r == 3) & (c == cols - 1))
    return picked.astype(jnp.float32), (r == c).astype(jnp.float32)


def write_packs(value, xpack_ref, ypack_ref, f, k, select):
    rows, cols = value.shape
    if select is not None:
        write_columns(value, xpack_ref, f, k, select)
    ypack_ref[f, k, 0:2, :] = value[0:2]
    ypack_ref[f, k, 2:4, :] = value[rows - 2:rows]
    ypack_ref[f, k, 4:8, :] = jnp.zeros((4, cols), jnp.float32)


def write_columns(value, xpack_ref, f, k, select):
    xpack_ref[f, k] = lax.dot_general(
        select, value, (((1,), (1,)), ((), ())), precision=lax.Precision.HIGHEST,
        preferred_element_type=jnp.float32)


def expand_columns(tile, spread):
    return lax.dot_general(
        tile, spread, (((0,), (0,)), ((), ())), precision=lax.Precision.HIGHEST,
        preferred_element_type=jnp.float32)


def edge_kernel(bl_ref, nt_ref, ns_ref, xpack_ref, ypack_ref):
    levels, rows, cols = nt_ref.shape
    select, _ = edge_tiles(rows, cols)

    def level(k, carry):
        m = (k < bl_ref[...]).astype(jnp.float32)
        for f, ref in enumerate((nt_ref, ns_ref)):
            write_packs(ref[k] * m, xpack_ref, ypack_ref, f, k, select)
        return carry

    lax.fori_loop(0, levels, level, 0)


def step_kernel(mask_inputs, final, bl_ref, nt_ref, ns_ref, bt_ref, bs_ref, xh_ref, yh_ref,
                ue_ref, vn_ref, *rest):
    outs, fv, hs = rest[:-2], rest[-2], rest[-1]
    levels, rows, cols = nt_ref.shape
    lane = lax.broadcasted_iota(jnp.int32, (rows, cols), 1)
    row = lax.broadcasted_iota(jnp.int32, (rows, cols), 0)
    select, spread = edge_tiles(rows, cols)
    now_refs, bef_refs = (nt_ref, ns_ref), (bt_ref, bs_ref)

    def mask(k):
        return (k < bl_ref[...]).astype(jnp.float32)

    def depth(k):
        return level_depth * (k.astype(jnp.float32) + 0.5)

    def load(ref, k, m):
        v = ref[k]
        return v * m if mask_inputs else v

    zero = jnp.zeros((rows, cols), jnp.float32)
    for f in range(2):
        fv[f, 0] = zero
        fv[f, levels] = zero

    def mixing(k, carry):
        m0, m1 = mask(k), mask(k + 1)
        e0 = density_at(load(nt_ref, k, m0), load(ns_ref, k, m0), depth(k))
        e1 = density_at(load(nt_ref, k + 1, m1), load(ns_ref, k + 1, m1), depth(k + 1))
        rates = (nu_base + nu_conv * jax.nn.sigmoid(-4.0 * (e1 - e0))) * m1
        for f in range(2):
            fv[f, k + 1] = rates * (load(bef_refs[f], k + 1, m1) - load(bef_refs[f], k, m0))
        return carry

    lax.fori_loop(0, levels - 1, mixing, 0)

    def expand(k, carry):
        for f in range(2):
            hs[f, k] = expand_columns(xh_ref[f, k], spread)
        return carry

    lax.fori_loop(0, levels, expand, 0, unroll=True)

    def level(k, carry):
        m = mask(k)
        ue, vn = ue_ref[k], vn_ref[k]
        afters = []
        for f in range(2):
            q = load(now_refs[f], k, m)
            b = load(bef_refs[f], k, m)
            h = hs[f, k]
            yh = yh_ref[f, k]
            if f == 0:
                uw = jnp.where(lane < 1, pltpu.roll(h, cols - 4, 1), pltpu.roll(ue, 1, 1))
                vs = jnp.where(row < 1, jnp.broadcast_to(yh[4:5], (rows, cols)), pltpu.roll(vn, 1, 0))
            qm1 = jnp.where(lane < 1, pltpu.roll(h, cols - 3, 1), pltpu.roll(q, 1, 1))
            qm2 = jnp.where(lane < 2, pltpu.roll(h, cols - 2, 1), pltpu.roll(q, 2, 1))
            qp1 = jnp.where(lane >= cols - 1, pltpu.roll(h, cols - 1, 1), pltpu.roll(q, cols - 1, 1))
            qp2 = jnp.where(lane >= cols - 2, pltpu.roll(h, cols - 2, 1), pltpu.roll(q, cols - 2, 1))
            div_x = face_flux(ue, qm1, q, qp1, qp2) - face_flux(uw, qm2, qm1, q, qp1)
            s2 = jnp.broadcast_to(yh[0:1], (rows, cols))
            s1 = jnp.broadcast_to(yh[1:2], (rows, cols))
            n1 = jnp.broadcast_to(yh[2:3], (rows, cols))
            n2 = jnp.broadcast_to(yh[3:4], (rows, cols))
            qs1 = jnp.where(row < 1, s1, pltpu.roll(q, 1, 0))
            qs2 = jnp.where(row < 1, s2, jnp.where(row < 2, s1, pltpu.roll(q, 2, 0)))
            qn1 = jnp.where(row >= rows - 1, n1, pltpu.roll(q, rows - 1, 0))
            qn2 = jnp.where(row >= rows - 1, n2, jnp.where(row >= rows - 2, n1, pltpu.roll(q, rows - 2, 0)))
            div_y = face_flux(vn, qs1, q, qn1, qn2) - face_flux(vs, qs2, qs1, q, qn1)
            change = -(div_x + div_y)
            change = change + (fv[f, k + 1] - fv[f, k])
            after = (b + 2.0 * change) * m
            afters.append(after)
            if not final:
                outs[f][k] = q + asselin_gamma * (b - 2.0 * q + after)
                outs[2 + f][k] = after
                write_packs(after, outs[4], outs[5], f, k, None)
        if final:
            outs[0][k] = afters[0]
            outs[1][k] = afters[1]
            outs[2][k] = density_at(afters[0], afters[1], depth(k)) * m
        return carry

    lax.fori_loop(0, levels, level, 0)

    if not final:
        def columns(k, carry):
            for f in range(2):
                write_columns(outs[2 + f][k], outs[4], f, k, select)
            return carry

        lax.fori_loop(0, levels, columns, 0, unroll=True)


VMEM_SPEC = pl.BlockSpec(memory_space=pltpu.VMEM)


def pack_shapes(levels, rows, cols):
    return (jax.ShapeDtypeStruct((2, levels, 8, rows), jnp.float32),
            jax.ShapeDtypeStruct((2, levels, 8, cols), jnp.float32))


def edge_call(bl, nt, ns):
    levels, rows, cols = nt.shape
    return pl.pallas_call(
        edge_kernel,
        out_shape=pack_shapes(levels, rows, cols),
        in_specs=[VMEM_SPEC] * 3,
        out_specs=(VMEM_SPEC, VMEM_SPEC),
        cost_estimate=pl.CostEstimate(
            flops=2 * 2 * levels * 8 * rows * cols, transcendentals=0,
            bytes_accessed=4 * levels * rows * cols * 3),
    )(bl, nt, ns)


def step_call(mask_inputs, final, bl, nt, ns, bt, bs, xh, yh, ue, vn):
    levels, rows, cols = nt.shape
    field = jax.ShapeDtypeStruct(nt.shape, jnp.float32)
    out_shape = (field,) * 3 if final else (field,) * 4 + pack_shapes(levels, rows, cols)
    return pl.pallas_call(
        functools.partial(step_kernel, mask_inputs, final),
        out_shape=out_shape,
        in_specs=[VMEM_SPEC] * 9,
        out_specs=tuple([VMEM_SPEC] * len(out_shape)),
        scratch_shapes=[pltpu.VMEM((2, levels + 1, rows, cols), jnp.float32),
                        pltpu.VMEM((2, levels, rows, cols), jnp.float32)],
        compiler_params=pltpu.CompilerParams(vmem_limit_bytes=48 * 1024 * 1024),
        cost_estimate=pl.CostEstimate(
            flops=400 * 2 * levels * rows * cols, transcendentals=levels * rows * cols,
            bytes_accessed=4 * levels * rows * cols * (9 + len(out_shape))),
    )(bl, nt, ns, bt, bs, xh, yh, ue, vn)


def exchange(xpack, ypack, west_column, south_row, at_fold):
    lon_count, lat_count = (lax.axis_size("lon"), lax.axis_size("lat"))
    from_east = lax.ppermute(xpack, "lon", [(i, (i - 1) % lon_count) for i in range(lon_count)])
    from_west = lax.ppermute(xpack, "lon", [(i, (i + 1) % lon_count) for i in range(lon_count)])
    from_north = lax.ppermute(ypack, "lat", [(i, i - 1) for i in range(1, lat_count)])
    from_south = lax.ppermute(ypack, "lat", [(i, i + 1) for i in range(lat_count - 1)])
    top = lat_count - 1
    fold_pairs = [(d * lat_count + top, (lon_count - 1 - d) * lat_count + top) for d in range(lon_count)]
    partner = lax.ppermute(ypack[:, :, 2:4], ("lon", "lat"), fold_pairs)
    cols = ypack.shape[-1]
    flip = (jnp.arange(cols)[:, None] + jnp.arange(cols)[None, :] == cols - 1).astype(jnp.float32)
    flipped = jnp.einsum("fkrc,cd->fkrd", partner, flip, precision=lax.Precision.HIGHEST)
    mirror = jnp.concatenate([flipped[:, :, 1:2], flipped[:, :, 0:1]], 2)
    north = jnp.where(at_fold, mirror, from_north[:, :, 0:2])
    two, levels, _, rows = xpack.shape
    halo_x = jnp.concatenate(
        [from_east[:, :, 0:2], from_west[:, :, 2:4],
         jnp.broadcast_to(west_column[None, :, None, :], (two, levels, 1, rows)),
         jnp.zeros((two, levels, 3, rows), jnp.float32)], 2)
    halo_y = jnp.concatenate(
        [from_south[:, :, 2:4], north,
         jnp.broadcast_to(south_row[None, :, None, :], (two, levels, 1, cols)),
         jnp.zeros((two, levels, 3, cols), jnp.float32)], 2)
    return halo_x, halo_y


def on_device(
    temp_before, temp_now, salt_before, salt_now, east_velocity, north_velocity, bottom_level
):
    lon_count, lat_count = (lax.axis_size("lon"), lax.axis_size("lat"))
    west_column = lax.ppermute(
        east_velocity[:, :, -1], "lon", [(i, (i + 1) % lon_count) for i in range(lon_count)])
    south_row = lax.ppermute(
        north_velocity[:, -1, :], "lat", [(i, i + 1) for i in range(lat_count - 1)])
    at_fold = lax.axis_index("lat") == lat_count - 1
    xpack, ypack = edge_call(bottom_level, temp_now, salt_now)
    halo_x, halo_y = exchange(xpack, ypack, west_column, south_row, at_fold)
    ft, fs, at, as_, xpack, ypack = step_call(
        True, False, bottom_level, temp_now, salt_now, temp_before, salt_before,
        halo_x, halo_y, east_velocity, north_velocity)
    halo_x, halo_y = exchange(xpack, ypack, west_column, south_row, at_fold)
    return step_call(False, True, bottom_level, at, as_, ft, fs, halo_x, halo_y,
                     east_velocity, north_velocity)


def solution(mesh):
    return jax.shard_map(
        on_device,
        mesh=mesh,
        in_specs=(
            P(None, "lat", "lon"),
            P(None, "lat", "lon"),
            P(None, "lat", "lon"),
            P(None, "lat", "lon"),
            P(None, "lat", "lon"),
            P(None, "lat", "lon"),
            P("lat", "lon"),
        ),
        out_specs=(P(None, "lat", "lon"), P(None, "lat", "lon"), P(None, "lat", "lon")),
        check_vma=False,
    )
```

```python
import functools
import jax
import jax.numpy as jnp
from jax import lax
from jax.experimental import pallas as pl
from jax.experimental.pallas import tpu as pltpu
from jax.sharding import PartitionSpec as P

asselin_gamma = 0.1
nu_base = 0.05
nu_conv = 0.2
level_depth = 160.0
alpha_zero = 0.1655
beta_zero = 0.76554
lambda_one = 0.05952
lambda_two = 0.00054914
mu_one = 0.0001497
mu_two = 1.109e-05
nu_cross = 0.0024341


def density_at(temp, salt, depth):
    warm = -alpha_zero * (1.0 + 0.5 * lambda_one * temp + mu_one * depth) * temp
    salty = beta_zero * (1.0 - 0.5 * lambda_two * salt - mu_two * depth) * salt
    return warm + salty - nu_cross * temp * salt


def face_flux(u, q1, q2, q3, q4):
    flux = u * (7.0 * (q2 + q3) - (q1 + q4)) / 12.0
    return flux + jnp.abs(u) * ((q4 - q1) - 3.0 * (q3 - q2)) / 12.0


def edge_tiles(rows, cols):
    r = lax.broadcasted_iota(jnp.int32, (8, cols), 0)
    c = lax.broadcasted_iota(jnp.int32, (8, cols), 1)
    picked = ((r == 0) & (c == 0)) | ((r == 1) & (c == 1))
    picked = picked | ((r == 2) & (c == cols - 2)) | ((r == 3) & (c == cols - 1))
    velocity = (r == 4) & (c == cols - 1)
    return picked.astype(jnp.float32), velocity.astype(jnp.float32), (r == c).astype(jnp.float32)


def write_columns(value, east_v, xpack_ref, f, k, select, select_v):
    dims = (((1,), (1,)), ((), ()))
    xpack_ref[f, k] = lax.dot_general(
        select, value, dims, precision=lax.Precision.HIGHEST,
        preferred_element_type=jnp.float32) + lax.dot_general(
        select_v, east_v, dims, precision=lax.Precision.HIGHEST,
        preferred_element_type=jnp.float32)


def write_rows(value, north_v, ypack_ref, f, k):
    rows, cols = value.shape
    ypack_ref[f, k, 0:2, :] = value[0:2]
    ypack_ref[f, k, 2:4, :] = value[rows - 2:rows]
    ypack_ref[f, k, 4:5, :] = north_v[rows - 1:rows]
    ypack_ref[f, k, 5:8, :] = jnp.zeros((3, cols), jnp.float32)


def expand_columns(tile, spread):
    return lax.dot_general(
        tile, spread, (((0,), (0,)), ((), ())), precision=lax.Precision.HIGHEST,
        preferred_element_type=jnp.float32)


def edge_kernel(bl_ref, nt_ref, ns_ref, ue_ref, vn_ref, xpack_ref, ypack_ref):
    levels, rows, cols = nt_ref.shape
    select, select_v, _ = edge_tiles(rows, cols)

    def level(k, carry):
        m = (k < bl_ref[...]).astype(jnp.float32)
        for f, ref in enumerate((nt_ref, ns_ref)):
            value = ref[k] * m
            write_columns(value, ue_ref[k], xpack_ref, f, k, select, select_v)
            write_rows(value, vn_ref[k], ypack_ref, f, k)
        return carry

    lax.fori_loop(0, levels, level, 0, unroll=True)


def step_kernel(mask_inputs, final, bl_ref, nt_ref, ns_ref, bt_ref, bs_ref, xh_ref, yh_ref,
                ue_ref, vn_ref, *rest):
    outs, fv, hs = rest[:-2], rest[-2], rest[-1]
    levels, rows, cols = nt_ref.shape
    lane = lax.broadcasted_iota(jnp.int32, (rows, cols), 1)
    row = lax.broadcasted_iota(jnp.int32, (rows, cols), 0)
    select, select_v, spread = edge_tiles(rows, cols)
    now_refs, bef_refs = (nt_ref, ns_ref), (bt_ref, bs_ref)

    def mask(k):
        return (k < bl_ref[...]).astype(jnp.float32)

    def depth(k):
        return level_depth * (k.astype(jnp.float32) + 0.5)

    def load(ref, k, m):
        v = ref[k]
        return v * m if mask_inputs else v

    zero = jnp.zeros((rows, cols), jnp.float32)
    for f in range(2):
        fv[f, 0] = zero
        fv[f, levels] = zero

    def mixing(k, carry):
        m0, m1 = mask(k), mask(k + 1)
        e0 = density_at(load(nt_ref, k, m0), load(ns_ref, k, m0), depth(k))
        e1 = density_at(load(nt_ref, k + 1, m1), load(ns_ref, k + 1, m1), depth(k + 1))
        rates = (nu_base + nu_conv * jax.nn.sigmoid(-4.0 * (e1 - e0))) * m1
        for f in range(2):
            fv[f, k + 1] = rates * (load(bef_refs[f], k + 1, m1) - load(bef_refs[f], k, m0))
        return carry

    lax.fori_loop(0, levels - 1, mixing, 0)

    def expand(k, carry):
        for f in range(2):
            hs[f, k] = expand_columns(xh_ref[f, k], spread)
        return carry

    lax.fori_loop(0, levels, expand, 0, unroll=True)

    def level(k, carry):
        m = mask(k)
        ue, vn = ue_ref[k], vn_ref[k]
        afters = []
        for f in range(2):
            q = load(now_refs[f], k, m)
            b = load(bef_refs[f], k, m)
            h = hs[f, k]
            yh = yh_ref[f, k]
            if f == 0:
                uw = jnp.where(lane < 1, pltpu.roll(h, cols - 4, 1), pltpu.roll(ue, 1, 1))
                vs = jnp.where(row < 1, jnp.broadcast_to(yh[4:5], (rows, cols)), pltpu.roll(vn, 1, 0))
            qm1 = jnp.where(lane < 1, pltpu.roll(h, cols - 3, 1), pltpu.roll(q, 1, 1))
            qm2 = jnp.where(lane < 2, pltpu.roll(h, cols - 2, 1), pltpu.roll(q, 2, 1))
            qp1 = jnp.where(lane >= cols - 1, pltpu.roll(h, cols - 1, 1), pltpu.roll(q, cols - 1, 1))
            qp2 = jnp.where(lane >= cols - 2, pltpu.roll(h, cols - 2, 1), pltpu.roll(q, cols - 2, 1))
            div_x = face_flux(ue, qm1, q, qp1, qp2) - face_flux(uw, qm2, qm1, q, qp1)
            s2 = jnp.broadcast_to(yh[0:1], (rows, cols))
            s1 = jnp.broadcast_to(yh[1:2], (rows, cols))
            n1 = jnp.broadcast_to(yh[2:3], (rows, cols))
            n2 = jnp.broadcast_to(yh[3:4], (rows, cols))
            qs1 = jnp.where(row < 1, s1, pltpu.roll(q, 1, 0))
            qs2 = jnp.where(row < 1, s2, jnp.where(row < 2, s1, pltpu.roll(q, 2, 0)))
            qn1 = jnp.where(row >= rows - 1, n1, pltpu.roll(q, rows - 1, 0))
            qn2 = jnp.where(row >= rows - 1, n2, jnp.where(row >= rows - 2, n1, pltpu.roll(q, rows - 2, 0)))
            div_y = face_flux(vn, qs1, q, qn1, qn2) - face_flux(vs, qs2, qs1, q, qn1)
            change = -(div_x + div_y)
            change = change + (fv[f, k + 1] - fv[f, k])
            after = (b + 2.0 * change) * m
            afters.append(after)
            if not final:
                outs[f][k] = q + asselin_gamma * (b - 2.0 * q + after)
                outs[2 + f][k] = after
                write_rows(after, vn, outs[5], f, k)
        if final:
            outs[0][k] = afters[0]
            outs[1][k] = afters[1]
            outs[2][k] = density_at(afters[0], afters[1], depth(k)) * m
        return carry

    lax.fori_loop(0, levels, level, 0)

    if not final:
        def columns(k, carry):
            for f in range(2):
                write_columns(outs[2 + f][k], ue_ref[k], outs[4], f, k, select, select_v)
            return carry

        lax.fori_loop(0, levels, columns, 0, unroll=True)


VMEM_SPEC = pl.BlockSpec(memory_space=pltpu.VMEM)


def pack_shapes(levels, rows, cols):
    return (jax.ShapeDtypeStruct((2, levels, 8, rows), jnp.float32),
            jax.ShapeDtypeStruct((2, levels, 8, cols), jnp.float32))


def edge_call(bl, nt, ns, ue, vn):
    levels, rows, cols = nt.shape
    return pl.pallas_call(
        edge_kernel,
        out_shape=pack_shapes(levels, rows, cols),
        in_specs=[VMEM_SPEC] * 5,
        out_specs=(VMEM_SPEC, VMEM_SPEC),
        cost_estimate=pl.CostEstimate(
            flops=2 * 2 * levels * 8 * rows * cols, transcendentals=0,
            bytes_accessed=4 * levels * rows * cols * 5),
    )(bl, nt, ns, ue, vn)


def step_call(mask_inputs, final, bl, nt, ns, bt, bs, xh, yh, ue, vn):
    levels, rows, cols = nt.shape
    field = jax.ShapeDtypeStruct(nt.shape, jnp.float32)
    out_shape = (field,) * 3 if final else (field,) * 4 + pack_shapes(levels, rows, cols)
    return pl.pallas_call(
        functools.partial(step_kernel, mask_inputs, final),
        out_shape=out_shape,
        in_specs=[VMEM_SPEC] * 9,
        out_specs=tuple([VMEM_SPEC] * len(out_shape)),
        scratch_shapes=[pltpu.VMEM((2, levels + 1, rows, cols), jnp.float32),
                        pltpu.VMEM((2, levels, rows, cols), jnp.float32)],
        compiler_params=pltpu.CompilerParams(vmem_limit_bytes=48 * 1024 * 1024),
        cost_estimate=pl.CostEstimate(
            flops=400 * 2 * levels * rows * cols, transcendentals=levels * rows * cols,
            bytes_accessed=4 * levels * rows * cols * (9 + len(out_shape))),
    )(bl, nt, ns, bt, bs, xh, yh, ue, vn)


def exchange(xpack, ypack, at_fold):
    lon_count, lat_count = (lax.axis_size("lon"), lax.axis_size("lat"))
    from_east = lax.ppermute(xpack, "lon", [(i, (i - 1) % lon_count) for i in range(lon_count)])
    from_west = lax.ppermute(xpack, "lon", [(i, (i + 1) % lon_count) for i in range(lon_count)])
    from_north = lax.ppermute(ypack, "lat", [(i, i - 1) for i in range(1, lat_count)])
    from_south = lax.ppermute(ypack, "lat", [(i, i + 1) for i in range(lat_count - 1)])
    top = lat_count - 1
    fold_pairs = [(d * lat_count + top, (lon_count - 1 - d) * lat_count + top) for d in range(lon_count)]
    partner = lax.ppermute(ypack[:, :, 2:4], ("lon", "lat"), fold_pairs)
    cols = ypack.shape[-1]
    flip = (jnp.arange(cols)[:, None] + jnp.arange(cols)[None, :] == cols - 1).astype(jnp.float32)
    flipped = jnp.einsum("fkrc,cd->fkrd", partner, flip, precision=lax.Precision.HIGHEST)
    mirror = jnp.concatenate([flipped[:, :, 1:2], flipped[:, :, 0:1]], 2)
    north = jnp.where(at_fold, mirror, from_north[:, :, 0:2])
    two, levels, _, rows = xpack.shape
    halo_x = jnp.concatenate(
        [from_east[:, :, 0:2], from_west[:, :, 2:4],
         from_west[:, :, 4:5], jnp.zeros((two, levels, 3, rows), jnp.float32)], 2)
    halo_y = jnp.concatenate(
        [from_south[:, :, 2:4], north,
         from_south[:, :, 4:5], jnp.zeros((two, levels, 3, cols), jnp.float32)], 2)
    return halo_x, halo_y


def on_device(
    temp_before, temp_now, salt_before, salt_now, east_velocity, north_velocity, bottom_level
):
    at_fold = lax.axis_index("lat") == lax.axis_size("lat") - 1
    xpack, ypack = edge_call(bottom_level, temp_now, salt_now, east_velocity, north_velocity)
    halo_x, halo_y = exchange(xpack, ypack, at_fold)
    ft, fs, at, as_, xpack, ypack = step_call(
        True, False, bottom_level, temp_now, salt_now, temp_before, salt_before,
        halo_x, halo_y, east_velocity, north_velocity)
    halo_x, halo_y = exchange(xpack, ypack, at_fold)
    return step_call(False, True, bottom_level, at, as_, ft, fs, halo_x, halo_y,
                     east_velocity, north_velocity)


def solution(mesh):
    return jax.shard_map(
        on_device,
        mesh=mesh,
        in_specs=(
            P(None, "lat", "lon"),
            P(None, "lat", "lon"),
            P(None, "lat", "lon"),
            P(None, "lat", "lon"),
            P(None, "lat", "lon"),
            P(None, "lat", "lon"),
            P("lat", "lon"),
        ),
        out_specs=(P(None, "lat", "lon"), P(None, "lat", "lon"), P(None, "lat", "lon")),
        check_vma=False,
    )
```

```python
import functools
import jax
import jax.numpy as jnp
from jax import lax
from jax.experimental import pallas as pl
from jax.experimental.pallas import tpu as pltpu
from jax.sharding import PartitionSpec as P

asselin_gamma = 0.1
nu_base = 0.05
nu_conv = 0.2
level_depth = 160.0
alpha_zero = 0.1655
beta_zero = 0.76554
lambda_one = 0.05952
lambda_two = 0.00054914
mu_one = 0.0001497
mu_two = 1.109e-05
nu_cross = 0.0024341


def density_at(temp, salt, depth):
    warm = -alpha_zero * (1.0 + 0.5 * lambda_one * temp + mu_one * depth) * temp
    salty = beta_zero * (1.0 - 0.5 * lambda_two * salt - mu_two * depth) * salt
    return warm + salty - nu_cross * temp * salt


def face_flux(u, q1, q2, q3, q4):
    flux = u * (7.0 * (q2 + q3) - (q1 + q4)) / 12.0
    return flux + jnp.abs(u) * ((q4 - q1) - 3.0 * (q3 - q2)) / 12.0


def lane_roll(value, shift):
    shift = shift % value.shape[-1]
    return value if shift == 0 else pltpu.roll(value, shift, 1)


def column_pack(value, east_v):
    rows, cols = value.shape
    lane = lax.broadcasted_iota(jnp.int32, (8, cols), 1)
    pack = jnp.zeros((8, cols), jnp.float32)
    for a in range(rows // 8):
        part = value[8 * a:8 * a + 8]
        pack = jnp.where((lane >= 4 * a) & (lane < 4 * a + 2), lane_roll(part, 4 * a), pack)
        pack = jnp.where((lane >= 4 * a + 2) & (lane < 4 * a + 4), lane_roll(part, 4 * a + 4), pack)
        pack = jnp.where(lane == 64 + 4 * a, lane_roll(east_v[8 * a:8 * a + 8], 4 * a + 65), pack)
    return pack


def column_unpack(from_east, from_west, with_velocity):
    cols = from_east.shape[-1]
    lane = lax.broadcasted_iota(jnp.int32, (8, cols), 1)
    both = jnp.where(lane % 4 < 2, from_east, from_west)
    parts = []
    for a in range(8):
        part = lane_roll(both, -4 * a)
        if with_velocity:
            part = jnp.where(lane == 4, lane_roll(from_west, 68 - 4 * a), part)
        parts.append(part)
    return jnp.concatenate(parts, 0)


def write_rows(value, north_v, ypack_ref, f, k):
    rows, cols = value.shape
    ypack_ref[f, k, 0:2, :] = value[0:2]
    ypack_ref[f, k, 2:4, :] = value[rows - 2:rows]
    ypack_ref[f, k, 4:5, :] = north_v[rows - 1:rows]
    ypack_ref[f, k, 5:8, :] = jnp.zeros((3, cols), jnp.float32)


def edge_kernel(bl_ref, nt_ref, ns_ref, ue_ref, vn_ref, xpack_ref, ypack_ref):
    levels, rows, cols = nt_ref.shape

    def level(k, carry):
        m = (k < bl_ref[...]).astype(jnp.float32)
        for f, ref in enumerate((nt_ref, ns_ref)):
            value = ref[k] * m
            xpack_ref[f, k] = column_pack(value, ue_ref[k])
            write_rows(value, vn_ref[k], ypack_ref, f, k)
        return carry

    lax.fori_loop(0, levels, level, 0, unroll=True)


def step_kernel(mask_inputs, final, bl_ref, nt_ref, ns_ref, bt_ref, bs_ref, xe_ref, xw_ref, yh_ref,
                ue_ref, vn_ref, *rest):
    outs, fv = rest[:-1], rest[-1]
    levels, rows, cols = nt_ref.shape
    lane = lax.broadcasted_iota(jnp.int32, (rows, cols), 1)
    row = lax.broadcasted_iota(jnp.int32, (rows, cols), 0)
    now_refs, bef_refs = (nt_ref, ns_ref), (bt_ref, bs_ref)

    def mask(k):
        return (k < bl_ref[...]).astype(jnp.float32)

    def depth(k):
        return level_depth * (k.astype(jnp.float32) + 0.5)

    def load(ref, k, m):
        v = ref[k]
        return v * m if mask_inputs else v

    zero = jnp.zeros((rows, cols), jnp.float32)
    for f in range(2):
        fv[f, 0] = zero
        fv[f, levels] = zero

    def mixing(k, carry):
        m0, m1 = mask(k), mask(k + 1)
        e0 = density_at(load(nt_ref, k, m0), load(ns_ref, k, m0), depth(k))
        e1 = density_at(load(nt_ref, k + 1, m1), load(ns_ref, k + 1, m1), depth(k + 1))
        rates = (nu_base + nu_conv * jax.nn.sigmoid(-4.0 * (e1 - e0))) * m1
        for f in range(2):
            fv[f, k + 1] = rates * (load(bef_refs[f], k + 1, m1) - load(bef_refs[f], k, m0))
        return carry

    lax.fori_loop(0, levels - 1, mixing, 0)

    def level(k, carry):
        m = mask(k)
        ue, vn = ue_ref[k], vn_ref[k]
        afters = []
        for f in range(2):
            q = load(now_refs[f], k, m)
            b = load(bef_refs[f], k, m)
            h = column_unpack(xe_ref[f, k], xw_ref[f, k], f == 0)
            yh = yh_ref[f, k]
            if f == 0:
                uw = jnp.where(lane < 1, pltpu.roll(h, cols - 4, 1), pltpu.roll(ue, 1, 1))
                vs = jnp.where(row < 1, jnp.broadcast_to(yh[4:5], (rows, cols)), pltpu.roll(vn, 1, 0))
            qm1 = jnp.where(lane < 1, pltpu.roll(h, cols - 3, 1), pltpu.roll(q, 1, 1))
            qm2 = jnp.where(lane < 2, pltpu.roll(h, cols - 2, 1), pltpu.roll(q, 2, 1))
            qp1 = jnp.where(lane >= cols - 1, pltpu.roll(h, cols - 1, 1), pltpu.roll(q, cols - 1, 1))
            qp2 = jnp.where(lane >= cols - 2, pltpu.roll(h, cols - 2, 1), pltpu.roll(q, cols - 2, 1))
            div_x = face_flux(ue, qm1, q, qp1, qp2) - face_flux(uw, qm2, qm1, q, qp1)
            s2 = jnp.broadcast_to(yh[0:1], (rows, cols))
            s1 = jnp.broadcast_to(yh[1:2], (rows, cols))
            n1 = jnp.broadcast_to(yh[2:3], (rows, cols))
            n2 = jnp.broadcast_to(yh[3:4], (rows, cols))
            qs1 = jnp.where(row < 1, s1, pltpu.roll(q, 1, 0))
            qs2 = jnp.where(row < 1, s2, jnp.where(row < 2, s1, pltpu.roll(q, 2, 0)))
            qn1 = jnp.where(row >= rows - 1, n1, pltpu.roll(q, rows - 1, 0))
            qn2 = jnp.where(row >= rows - 1, n2, jnp.where(row >= rows - 2, n1, pltpu.roll(q, rows - 2, 0)))
            div_y = face_flux(vn, qs1, q, qn1, qn2) - face_flux(vs, qs2, qs1, q, qn1)
            change = -(div_x + div_y)
            change = change + (fv[f, k + 1] - fv[f, k])
            after = (b + 2.0 * change) * m
            afters.append(after)
            if not final:
                outs[f][k] = q + asselin_gamma * (b - 2.0 * q + after)
                outs[2 + f][k] = after
                outs[4][f, k] = column_pack(after, ue)
                write_rows(after, vn, outs[5], f, k)
        if final:
            outs[0][k] = afters[0]
            outs[1][k] = afters[1]
            outs[2][k] = density_at(afters[0], afters[1], depth(k)) * m
        return carry

    lax.fori_loop(0, levels, level, 0)


VMEM_SPEC = pl.BlockSpec(memory_space=pltpu.VMEM)


def pack_shapes(levels, rows, cols):
    return (jax.ShapeDtypeStruct((2, levels, 8, cols), jnp.float32),
            jax.ShapeDtypeStruct((2, levels, 8, cols), jnp.float32))


def edge_call(bl, nt, ns, ue, vn):
    levels, rows, cols = nt.shape
    return pl.pallas_call(
        edge_kernel,
        out_shape=pack_shapes(levels, rows, cols),
        in_specs=[VMEM_SPEC] * 5,
        out_specs=(VMEM_SPEC, VMEM_SPEC),
        cost_estimate=pl.CostEstimate(
            flops=2 * 2 * levels * 8 * rows * cols, transcendentals=0,
            bytes_accessed=4 * levels * rows * cols * 5),
    )(bl, nt, ns, ue, vn)


def step_call(mask_inputs, final, bl, nt, ns, bt, bs, xe, xw, yh, ue, vn):
    levels, rows, cols = nt.shape
    field = jax.ShapeDtypeStruct(nt.shape, jnp.float32)
    out_shape = (field,) * 3 if final else (field,) * 4 + pack_shapes(levels, rows, cols)
    return pl.pallas_call(
        functools.partial(step_kernel, mask_inputs, final),
        out_shape=out_shape,
        in_specs=[VMEM_SPEC] * 10,
        out_specs=tuple([VMEM_SPEC] * len(out_shape)),
        scratch_shapes=[pltpu.VMEM((2, levels + 1, rows, cols), jnp.float32)],
        compiler_params=pltpu.CompilerParams(vmem_limit_bytes=48 * 1024 * 1024),
        cost_estimate=pl.CostEstimate(
            flops=400 * 2 * levels * rows * cols, transcendentals=levels * rows * cols,
            bytes_accessed=4 * levels * rows * cols * (9 + len(out_shape))),
    )(bl, nt, ns, bt, bs, xe, xw, yh, ue, vn)


def exchange(xpack, ypack, at_fold):
    lon_count, lat_count = (lax.axis_size("lon"), lax.axis_size("lat"))
    from_east = lax.ppermute(xpack, "lon", [(i, (i - 1) % lon_count) for i in range(lon_count)])
    from_west = lax.ppermute(xpack, "lon", [(i, (i + 1) % lon_count) for i in range(lon_count)])
    from_north = lax.ppermute(ypack, "lat", [(i, i - 1) for i in range(1, lat_count)])
    from_south = lax.ppermute(ypack, "lat", [(i, i + 1) for i in range(lat_count - 1)])
    top = lat_count - 1
    fold_pairs = [(d * lat_count + top, (lon_count - 1 - d) * lat_count + top) for d in range(lon_count)]
    partner = lax.ppermute(ypack[:, :, 2:4], ("lon", "lat"), fold_pairs)
    cols = ypack.shape[-1]
    flip = (jnp.arange(cols)[:, None] + jnp.arange(cols)[None, :] == cols - 1).astype(jnp.float32)
    flipped = jnp.einsum("fkrc,cd->fkrd", partner, flip, precision=lax.Precision.HIGHEST)
    mirror = jnp.concatenate([flipped[:, :, 1:2], flipped[:, :, 0:1]], 2)
    north = jnp.where(at_fold, mirror, from_north[:, :, 0:2])
    two, levels = xpack.shape[:2]
    halo_y = jnp.concatenate(
        [from_south[:, :, 2:4], north,
         from_south[:, :, 4:5], jnp.zeros((two, levels, 3, cols), jnp.float32)], 2)
    return from_east, from_west, halo_y


def on_device(
    temp_before, temp_now, salt_before, salt_now, east_velocity, north_velocity, bottom_level
):
    at_fold = lax.axis_index("lat") == lax.axis_size("lat") - 1
    xpack, ypack = edge_call(bottom_level, temp_now, salt_now, east_velocity, north_velocity)
    from_east, from_west, halo_y = exchange(xpack, ypack, at_fold)
    ft, fs, at, as_, xpack, ypack = step_call(
        True, False, bottom_level, temp_now, salt_now, temp_before, salt_before,
        from_east, from_west, halo_y, east_velocity, north_velocity)
    from_east, from_west, halo_y = exchange(xpack, ypack, at_fold)
    return step_call(False, True, bottom_level, at, as_, ft, fs, from_east, from_west, halo_y,
                     east_velocity, north_velocity)


def solution(mesh):
    return jax.shard_map(
        on_device,
        mesh=mesh,
        in_specs=(
            P(None, "lat", "lon"),
            P(None, "lat", "lon"),
            P(None, "lat", "lon"),
            P(None, "lat", "lon"),
            P(None, "lat", "lon"),
            P(None, "lat", "lon"),
            P("lat", "lon"),
        ),
        out_specs=(P(None, "lat", "lon"), P(None, "lat", "lon"), P(None, "lat", "lon")),
        check_vma=False,
    )
```

```python
import functools
import jax
import jax.numpy as jnp
from jax import lax
from jax.experimental import pallas as pl
from jax.experimental.pallas import tpu as pltpu
from jax.sharding import PartitionSpec as P

asselin_gamma = 0.1
nu_base = 0.05
nu_conv = 0.2
level_depth = 160.0
alpha_zero = 0.1655
beta_zero = 0.76554
lambda_one = 0.05952
lambda_two = 0.00054914
mu_one = 0.0001497
mu_two = 1.109e-05
nu_cross = 0.0024341


def density_at(temp, salt, depth):
    warm = -alpha_zero * (1.0 + 0.5 * lambda_one * temp + mu_one * depth) * temp
    salty = beta_zero * (1.0 - 0.5 * lambda_two * salt - mu_two * depth) * salt
    return warm + salty - nu_cross * temp * salt


def face_flux(u, q1, q2, q3, q4):
    flux = u * (7.0 * (q2 + q3) - (q1 + q4)) / 12.0
    return flux + jnp.abs(u) * ((q4 - q1) - 3.0 * (q3 - q2)) / 12.0


def lane_roll(value, shift):
    shift = shift % value.shape[-1]
    return value if shift == 0 else pltpu.roll(value, shift, 1)


def column_pack(value, east_v):
    rows, cols = value.shape
    lane = lax.broadcasted_iota(jnp.int32, (8, cols), 1)
    pack = jnp.zeros((8, cols), jnp.float32)
    for a in range(rows // 8):
        part = value[8 * a:8 * a + 8]
        pack = jnp.where((lane >= 4 * a) & (lane < 4 * a + 2), lane_roll(part, 4 * a), pack)
        pack = jnp.where((lane >= 4 * a + 2) & (lane < 4 * a + 4), lane_roll(part, 4 * a + 4), pack)
        pack = jnp.where(lane == 64 + 4 * a, lane_roll(east_v[8 * a:8 * a + 8], 4 * a + 65), pack)
    return pack


def column_unpack(from_east, from_west, with_velocity):
    cols = from_east.shape[-1]
    lane = lax.broadcasted_iota(jnp.int32, (8, cols), 1)
    both = jnp.where(lane % 4 < 2, from_east, from_west)
    parts = []
    for a in range(8):
        part = lane_roll(both, -4 * a)
        if with_velocity:
            part = jnp.where(lane == 4, lane_roll(from_west, 68 - 4 * a), part)
        parts.append(part)
    return parts


def sub_roll(value, shift):
    shift = shift % value.shape[0]
    return value if shift == 0 else pltpu.roll(value, shift, 0)


def write_rows(value, north_v, ypack_ref, f, k):
    rows, cols = value.shape
    ypack_ref[f, k, 0:2, :] = value[0:2]
    ypack_ref[f, k, 2:4, :] = value[rows - 2:rows]
    ypack_ref[f, k, 4:5, :] = north_v[rows - 1:rows]
    ypack_ref[f, k, 5:8, :] = jnp.zeros((3, cols), jnp.float32)


def edge_kernel(bl_ref, nt_ref, ns_ref, ue_ref, vn_ref, xpack_ref, ypack_ref):
    levels, rows, cols = nt_ref.shape

    def level(k, carry):
        m = (k < bl_ref[...]).astype(jnp.float32)
        for f, ref in enumerate((nt_ref, ns_ref)):
            value = ref[k] * m
            xpack_ref[f, k] = column_pack(value, ue_ref[k])
            write_rows(value, vn_ref[k], ypack_ref, f, k)
        return carry

    lax.fori_loop(0, levels, level, 0, unroll=True)


def step_kernel(mask_inputs, final, bl_ref, nt_ref, ns_ref, bt_ref, bs_ref, xe_ref, xw_ref, yh_ref,
                ue_ref, vn_ref, *rest):
    outs, fv = rest[:-1], rest[-1]
    levels, rows, cols = nt_ref.shape
    lane = lax.broadcasted_iota(jnp.int32, (rows, cols), 1)
    row = lax.broadcasted_iota(jnp.int32, (rows, cols), 0)
    now_refs, bef_refs = (nt_ref, ns_ref), (bt_ref, bs_ref)

    def mask(k):
        return (k < bl_ref[...]).astype(jnp.float32)

    def depth(k):
        return level_depth * (k.astype(jnp.float32) + 0.5)

    def load(ref, k, m):
        v = ref[k]
        return v * m if mask_inputs else v

    zero = jnp.zeros((rows, cols), jnp.float32)
    for f in range(2):
        fv[f, 0] = zero
        fv[f, levels] = zero

    def mixing(k, carry):
        m0, m1 = mask(k), mask(k + 1)
        e0 = density_at(load(nt_ref, k, m0), load(ns_ref, k, m0), depth(k))
        e1 = density_at(load(nt_ref, k + 1, m1), load(ns_ref, k + 1, m1), depth(k + 1))
        rates = (nu_base + nu_conv * jax.nn.sigmoid(-4.0 * (e1 - e0))) * m1
        for f in range(2):
            fv[f, k + 1] = rates * (load(bef_refs[f], k + 1, m1) - load(bef_refs[f], k, m0))
        return carry

    lax.fori_loop(0, levels - 1, mixing, 0)

    strips = rows // 8
    lane8 = lax.broadcasted_iota(jnp.int32, (8, cols), 1)
    sub8 = lax.broadcasted_iota(jnp.int32, (8, cols), 0)

    def split(value):
        return [value[8 * a:8 * a + 8] for a in range(strips)]

    def level(k, carry):
        m = split(mask(k))
        ue, vn = split(ue_ref[k]), split(vn_ref[k])
        yh0 = yh_ref[0, k]
        south_v = jnp.where(sub8 == 7, jnp.broadcast_to(yh0[4:5], (8, cols)), 0.0)
        depth_k = depth(k)
        afters = [[None] * strips for _ in range(2)]
        for f in range(2):
            q = split(load(now_refs[f], k, mask(k)))
            b = split(load(bef_refs[f], k, mask(k)))
            hs = column_unpack(xe_ref[f, k], xw_ref[f, k], f == 0)
            yh = yh_ref[f, k]
            below = jnp.where(sub8 == 6, jnp.broadcast_to(yh[0:1], (8, cols)),
                              jnp.broadcast_to(yh[1:2], (8, cols)))
            above = jnp.where(sub8 == 0, jnp.broadcast_to(yh[2:3], (8, cols)),
                              jnp.broadcast_to(yh[3:4], (8, cols)))
            qx = [below] + q + [above]
            fv_lo, fv_hi = split(fv[f, k]), split(fv[f, k + 1])
            pack = jnp.zeros((8, cols), jnp.float32)
            for a in range(strips):
                qa, ha = q[a], hs[a]
                if f == 0:
                    if a == 0:
                        uws, vss = [], []
                    uws.append(jnp.where(lane8 < 1, lane_roll(ha, cols - 4), lane_roll(ue[a], 1)))
                    prev_v = south_v if a == 0 else vn[a - 1]
                    vss.append(jnp.where(sub8 < 1, sub_roll(prev_v, 1), sub_roll(vn[a], 1)))
                uw, vs = uws[a], vss[a]
                qm1 = jnp.where(lane8 < 1, lane_roll(ha, cols - 3), lane_roll(qa, 1))
                qm2 = jnp.where(lane8 < 2, lane_roll(ha, cols - 2), lane_roll(qa, 2))
                qp1 = jnp.where(lane8 >= cols - 1, lane_roll(ha, cols - 1), lane_roll(qa, cols - 1))
                qp2 = jnp.where(lane8 >= cols - 2, lane_roll(ha, cols - 2), lane_roll(qa, cols - 2))
                div_x = face_flux(ue[a], qm1, qa, qp1, qp2) - face_flux(uw, qm2, qm1, qa, qp1)
                lo, hi = qx[a], qx[a + 2]
                qs1 = jnp.where(sub8 < 1, sub_roll(lo, 1), sub_roll(qa, 1))
                qs2 = jnp.where(sub8 < 2, sub_roll(lo, 2), sub_roll(qa, 2))
                qn1 = jnp.where(sub8 >= 7, sub_roll(hi, 7), sub_roll(qa, 7))
                qn2 = jnp.where(sub8 >= 6, sub_roll(hi, 6), sub_roll(qa, 6))
                div_y = face_flux(vn[a], qs1, qa, qn1, qn2) - face_flux(vs, qs2, qs1, qa, qn1)
                change = -(div_x + div_y)
                change = change + (fv_hi[a] - fv_lo[a])
                after = (b[a] + 2.0 * change) * m[a]
                afters[f][a] = after
                rs = pl.ds(8 * a, 8)
                if not final:
                    outs[f][k, rs, :] = qa + asselin_gamma * (b[a] - 2.0 * qa + after)
                    outs[2 + f][k, rs, :] = after
                else:
                    outs[f][k, rs, :] = after
            if not final:
                whole = jnp.concatenate(afters[f], 0)
                outs[4][f, k] = column_pack(whole, ue_ref[k])
                write_rows(whole, vn_ref[k], outs[5], f, k)
        if final:
            for a in range(strips):
                outs[2][k, pl.ds(8 * a, 8), :] = density_at(afters[0][a], afters[1][a], depth_k) * m[a]
        return carry

    lax.fori_loop(0, levels, level, 0)


VMEM_SPEC = pl.BlockSpec(memory_space=pltpu.VMEM)


def pack_shapes(levels, rows, cols):
    return (jax.ShapeDtypeStruct((2, levels, 8, cols), jnp.float32),
            jax.ShapeDtypeStruct((2, levels, 8, cols), jnp.float32))


def edge_call(bl, nt, ns, ue, vn):
    levels, rows, cols = nt.shape
    return pl.pallas_call(
        edge_kernel,
        out_shape=pack_shapes(levels, rows, cols),
        in_specs=[VMEM_SPEC] * 5,
        out_specs=(VMEM_SPEC, VMEM_SPEC),
        cost_estimate=pl.CostEstimate(
            flops=2 * 2 * levels * 8 * rows * cols, transcendentals=0,
            bytes_accessed=4 * levels * rows * cols * 5),
    )(bl, nt, ns, ue, vn)


def step_call(mask_inputs, final, bl, nt, ns, bt, bs, xe, xw, yh, ue, vn):
    levels, rows, cols = nt.shape
    field = jax.ShapeDtypeStruct(nt.shape, jnp.float32)
    out_shape = (field,) * 3 if final else (field,) * 4 + pack_shapes(levels, rows, cols)
    return pl.pallas_call(
        functools.partial(step_kernel, mask_inputs, final),
        out_shape=out_shape,
        in_specs=[VMEM_SPEC] * 10,
        out_specs=tuple([VMEM_SPEC] * len(out_shape)),
        scratch_shapes=[pltpu.VMEM((2, levels + 1, rows, cols), jnp.float32)],
        compiler_params=pltpu.CompilerParams(vmem_limit_bytes=48 * 1024 * 1024),
        cost_estimate=pl.CostEstimate(
            flops=400 * 2 * levels * rows * cols, transcendentals=levels * rows * cols,
            bytes_accessed=4 * levels * rows * cols * (9 + len(out_shape))),
    )(bl, nt, ns, bt, bs, xe, xw, yh, ue, vn)


def exchange(xpack, ypack, at_fold):
    lon_count, lat_count = (lax.axis_size("lon"), lax.axis_size("lat"))
    from_east = lax.ppermute(xpack, "lon", [(i, (i - 1) % lon_count) for i in range(lon_count)])
    from_west = lax.ppermute(xpack, "lon", [(i, (i + 1) % lon_count) for i in range(lon_count)])
    from_north = lax.ppermute(ypack, "lat", [(i, i - 1) for i in range(1, lat_count)])
    from_south = lax.ppermute(ypack, "lat", [(i, i + 1) for i in range(lat_count - 1)])
    top = lat_count - 1
    fold_pairs = [(d * lat_count + top, (lon_count - 1 - d) * lat_count + top) for d in range(lon_count)]
    partner = lax.ppermute(ypack[:, :, 2:4], ("lon", "lat"), fold_pairs)
    cols = ypack.shape[-1]
    flip = (jnp.arange(cols)[:, None] + jnp.arange(cols)[None, :] == cols - 1).astype(jnp.float32)
    flipped = jnp.einsum("fkrc,cd->fkrd", partner, flip, precision=lax.Precision.HIGHEST)
    mirror = jnp.concatenate([flipped[:, :, 1:2], flipped[:, :, 0:1]], 2)
    north = jnp.where(at_fold, mirror, from_north[:, :, 0:2])
    two, levels = xpack.shape[:2]
    halo_y = jnp.concatenate(
        [from_south[:, :, 2:4], north,
         from_south[:, :, 4:5], jnp.zeros((two, levels, 3, cols), jnp.float32)], 2)
    return from_east, from_west, halo_y


def on_device(
    temp_before, temp_now, salt_before, salt_now, east_velocity, north_velocity, bottom_level
):
    at_fold = lax.axis_index("lat") == lax.axis_size("lat") - 1
    xpack, ypack = edge_call(bottom_level, temp_now, salt_now, east_velocity, north_velocity)
    from_east, from_west, halo_y = exchange(xpack, ypack, at_fold)
    ft, fs, at, as_, xpack, ypack = step_call(
        True, False, bottom_level, temp_now, salt_now, temp_before, salt_before,
        from_east, from_west, halo_y, east_velocity, north_velocity)
    from_east, from_west, halo_y = exchange(xpack, ypack, at_fold)
    return step_call(False, True, bottom_level, at, as_, ft, fs, from_east, from_west, halo_y,
                     east_velocity, north_velocity)


def solution(mesh):
    return jax.shard_map(
        on_device,
        mesh=mesh,
        in_specs=(
            P(None, "lat", "lon"),
            P(None, "lat", "lon"),
            P(None, "lat", "lon"),
            P(None, "lat", "lon"),
            P(None, "lat", "lon"),
            P(None, "lat", "lon"),
            P("lat", "lon"),
        ),
        out_specs=(P(None, "lat", "lon"), P(None, "lat", "lon"), P(None, "lat", "lon")),
        check_vma=False,
    )
```

```python
import functools
import jax
import jax.numpy as jnp
from jax import lax
from jax.experimental import pallas as pl
from jax.experimental.pallas import tpu as pltpu
from jax.sharding import PartitionSpec as P

asselin_gamma = 0.1
nu_base = 0.05
nu_conv = 0.2
level_depth = 160.0
alpha_zero = 0.1655
beta_zero = 0.76554
lambda_one = 0.05952
lambda_two = 0.00054914
mu_one = 0.0001497
mu_two = 1.109e-05
nu_cross = 0.0024341


def density_at(temp, salt, depth):
    warm = -alpha_zero * (1.0 + 0.5 * lambda_one * temp + mu_one * depth) * temp
    salty = beta_zero * (1.0 - 0.5 * lambda_two * salt - mu_two * depth) * salt
    return warm + salty - nu_cross * temp * salt


def face_flux(u, q1, q2, q3, q4):
    flux = u * (7.0 * (q2 + q3) - (q1 + q4)) + jnp.abs(u) * ((q4 - q1) - 3.0 * (q3 - q2))
    return flux * (1.0 / 12.0)


def lane_roll(value, shift):
    shift = shift % value.shape[-1]
    return value if shift == 0 else pltpu.roll(value, shift, 1)


def column_pack(value, east_v):
    rows, cols = value.shape
    lane = lax.broadcasted_iota(jnp.int32, (8, cols), 1)
    pack = jnp.zeros((8, cols), jnp.float32)
    for a in range(rows // 8):
        part = lane_roll(value[8 * a:8 * a + 8], 4 * a)
        lo_lane = (4 * a - 2) % cols
        pack = jnp.where((lane >= 4 * a) & (lane < 4 * a + 2), part, pack)
        pack = jnp.where((lane >= lo_lane) & (lane < lo_lane + 2), part, pack)
        pack = jnp.where(lane == 64 + 4 * a, lane_roll(east_v[8 * a:8 * a + 8], 4 * a + 65), pack)
    return pack


def column_unpack(from_east, from_west, with_velocity):
    cols = from_east.shape[-1]
    lane = lax.broadcasted_iota(jnp.int32, (8, cols), 1)
    both = jnp.where(lane % 4 < 2, from_east, from_west)
    return both, [lane_roll(both, -4 * a) for a in range(8)]


def sub_roll(value, shift):
    shift = shift % value.shape[0]
    return value if shift == 0 else pltpu.roll(value, shift, 0)


def write_rows(value, north_v, ypack_ref, f, k):
    rows, cols = value.shape
    ypack_ref[f, k, 0:2, :] = value[0:2]
    ypack_ref[f, k, 2:4, :] = value[rows - 2:rows]
    ypack_ref[f, k, 4:5, :] = north_v[rows - 1:rows]
    ypack_ref[f, k, 5:8, :] = jnp.zeros((3, cols), jnp.float32)


def edge_kernel(bl_ref, nt_ref, ns_ref, ue_ref, vn_ref, xpack_ref, ypack_ref):
    levels, rows, cols = nt_ref.shape

    def level(k, carry):
        m = (k < bl_ref[...]).astype(jnp.float32)
        for f, ref in enumerate((nt_ref, ns_ref)):
            value = ref[k] * m
            xpack_ref[f, k] = column_pack(value, ue_ref[k])
            write_rows(value, vn_ref[k], ypack_ref, f, k)
        return carry

    lax.fori_loop(0, levels, level, 0, unroll=True)


def step_kernel(mask_inputs, final, bl_ref, nt_ref, ns_ref, bt_ref, bs_ref, xe_ref, xw_ref, yh_ref,
                ue_ref, vn_ref, *rest):
    outs, fv = rest[:-1], rest[-1]
    levels, rows, cols = nt_ref.shape
    lane = lax.broadcasted_iota(jnp.int32, (rows, cols), 1)
    row = lax.broadcasted_iota(jnp.int32, (rows, cols), 0)
    now_refs, bef_refs = (nt_ref, ns_ref), (bt_ref, bs_ref)

    def mask(k):
        return (k < bl_ref[...]).astype(jnp.float32)

    def depth(k):
        return level_depth * (k.astype(jnp.float32) + 0.5)

    def load(ref, k, m):
        v = ref[k]
        return v * m if mask_inputs else v

    zero = jnp.zeros((rows, cols), jnp.float32)
    for f in range(2):
        fv[f, 0] = zero
        fv[f, levels] = zero

    def mixing(k, carry):
        m0, m1 = mask(k), mask(k + 1)
        e0 = density_at(load(nt_ref, k, m0), load(ns_ref, k, m0), depth(k))
        e1 = density_at(load(nt_ref, k + 1, m1), load(ns_ref, k + 1, m1), depth(k + 1))
        rates = (nu_base + nu_conv * jax.nn.sigmoid(-4.0 * (e1 - e0))) * m1
        for f in range(2):
            fv[f, k + 1] = rates * (load(bef_refs[f], k + 1, m1) - load(bef_refs[f], k, m0))
        return carry

    lax.fori_loop(0, levels - 1, mixing, 0)

    strips = rows // 8
    lane8 = lax.broadcasted_iota(jnp.int32, (8, cols), 1)
    sub8 = lax.broadcasted_iota(jnp.int32, (8, cols), 0)

    def split(value):
        return [value[8 * a:8 * a + 8] for a in range(strips)]

    def level(k, carry):
        m = split(mask(k))
        ue, vn = split(ue_ref[k]), split(vn_ref[k])
        south_v = jnp.where(sub8 == 7, jnp.broadcast_to(yh_ref[0, k][4:5], (8, cols)), 0.0)
        depth_k = depth(k)
        afters = [[None] * strips for _ in range(2)]
        for f in range(2):
            q = split(load(now_refs[f], k, mask(k)))
            b = split(load(bef_refs[f], k, mask(k)))
            from_west = xw_ref[f, k]
            both, hs = column_unpack(xe_ref[f, k], from_west, False)
            own = jnp.zeros((8, cols), jnp.float32)
            for a in range(strips):
                own = jnp.where((lane8 >= 4 * a) & (lane8 < 4 * a + 2), lane_roll(q[a], 4 * a), own)
            west_face = face_flux(lane_roll(from_west, -64), lane_roll(both, 2), lane_roll(both, 1),
                                  own, lane_roll(own, -1))
            yh = yh_ref[f, k]
            below = jnp.where(sub8 == 6, jnp.broadcast_to(yh[0:1], (8, cols)),
                              jnp.broadcast_to(yh[1:2], (8, cols)))
            above = jnp.where(sub8 == 0, jnp.broadcast_to(yh[2:3], (8, cols)),
                              jnp.broadcast_to(yh[3:4], (8, cols)))
            qx = q + [above]
            north_prev = face_flux(south_v, sub_roll(below, 1), below, sub_roll(q[0], 7), sub_roll(q[0], 6))
            lo = below
            fv_lo, fv_hi = split(fv[f, k]), split(fv[f, k + 1])
            for a in range(strips):
                qa, ha, hi = q[a], hs[a], qx[a + 1]
                qm1 = lane_roll(jnp.where(lane8 == cols - 1, ha, qa), 1)
                qp1 = lane_roll(jnp.where(lane8 < 1, ha, qa), -1)
                qp2 = lane_roll(jnp.where(lane8 < 2, ha, qa), -2)
                east_f = face_flux(ue[a], qm1, qa, qp1, qp2)
                west_f = jnp.where(lane8 < 1, lane_roll(west_face, -4 * a), lane_roll(east_f, 1))
                qs1 = sub_roll(jnp.where(sub8 == 7, lo, qa), 1)
                qn1 = sub_roll(jnp.where(sub8 < 1, hi, qa), 7)
                qn2 = sub_roll(jnp.where(sub8 < 2, hi, qa), 6)
                north_f = face_flux(vn[a], qs1, qa, qn1, qn2)
                south_f = sub_roll(jnp.where(sub8 == 7, north_prev, north_f), 1)
                north_prev, lo = north_f, qa
                div_x = east_f - west_f
                div_y = north_f - south_f
                change = -(div_x + div_y)
                change = change + (fv_hi[a] - fv_lo[a])
                after = (b[a] + 2.0 * change) * m[a]
                afters[f][a] = after
                rs = pl.ds(8 * a, 8)
                if not final:
                    outs[f][k, rs, :] = qa + asselin_gamma * (b[a] - 2.0 * qa + after)
                    outs[2 + f][k, rs, :] = after
                else:
                    outs[f][k, rs, :] = after
            if not final:
                whole = jnp.concatenate(afters[f], 0)
                outs[4][f, k] = column_pack(whole, ue_ref[k])
                write_rows(whole, vn_ref[k], outs[5], f, k)
        if final:
            for a in range(strips):
                outs[2][k, pl.ds(8 * a, 8), :] = density_at(afters[0][a], afters[1][a], depth_k) * m[a]
        return carry

    lax.fori_loop(0, levels, level, 0)


VMEM_SPEC = pl.BlockSpec(memory_space=pltpu.VMEM)


def pack_shapes(levels, rows, cols):
    return (jax.ShapeDtypeStruct((2, levels, 8, cols), jnp.float32),
            jax.ShapeDtypeStruct((2, levels, 8, cols), jnp.float32))


def edge_call(bl, nt, ns, ue, vn):
    levels, rows, cols = nt.shape
    return pl.pallas_call(
        edge_kernel,
        out_shape=pack_shapes(levels, rows, cols),
        in_specs=[VMEM_SPEC] * 5,
        out_specs=(VMEM_SPEC, VMEM_SPEC),
        cost_estimate=pl.CostEstimate(
            flops=2 * 2 * levels * 8 * rows * cols, transcendentals=0,
            bytes_accessed=4 * levels * rows * cols * 5),
    )(bl, nt, ns, ue, vn)


def step_call(mask_inputs, final, bl, nt, ns, bt, bs, xe, xw, yh, ue, vn):
    levels, rows, cols = nt.shape
    field = jax.ShapeDtypeStruct(nt.shape, jnp.float32)
    out_shape = (field,) * 3 if final else (field,) * 4 + pack_shapes(levels, rows, cols)
    return pl.pallas_call(
        functools.partial(step_kernel, mask_inputs, final),
        out_shape=out_shape,
        in_specs=[VMEM_SPEC] * 10,
        out_specs=tuple([VMEM_SPEC] * len(out_shape)),
        scratch_shapes=[pltpu.VMEM((2, levels + 1, rows, cols), jnp.float32)],
        compiler_params=pltpu.CompilerParams(vmem_limit_bytes=48 * 1024 * 1024),
        cost_estimate=pl.CostEstimate(
            flops=400 * 2 * levels * rows * cols, transcendentals=levels * rows * cols,
            bytes_accessed=4 * levels * rows * cols * (9 + len(out_shape))),
    )(bl, nt, ns, bt, bs, xe, xw, yh, ue, vn)


def exchange(xpack, ypack, at_fold):
    lon_count, lat_count = (lax.axis_size("lon"), lax.axis_size("lat"))
    from_east = lax.ppermute(xpack, "lon", [(i, (i - 1) % lon_count) for i in range(lon_count)])
    from_west = lax.ppermute(xpack, "lon", [(i, (i + 1) % lon_count) for i in range(lon_count)])
    from_north = lax.ppermute(ypack, "lat", [(i, i - 1) for i in range(1, lat_count)])
    from_south = lax.ppermute(ypack, "lat", [(i, i + 1) for i in range(lat_count - 1)])
    top = lat_count - 1
    fold_pairs = [(d * lat_count + top, (lon_count - 1 - d) * lat_count + top) for d in range(lon_count)]
    partner = lax.ppermute(ypack[:, :, 2:4], ("lon", "lat"), fold_pairs)
    cols = ypack.shape[-1]
    flip = (jnp.arange(cols)[:, None] + jnp.arange(cols)[None, :] == cols - 1).astype(jnp.float32)
    flipped = jnp.einsum("fkrc,cd->fkrd", partner, flip, precision=lax.Precision.HIGHEST)
    mirror = jnp.concatenate([flipped[:, :, 1:2], flipped[:, :, 0:1]], 2)
    north = jnp.where(at_fold, mirror, from_north[:, :, 0:2])
    two, levels = xpack.shape[:2]
    halo_y = jnp.concatenate(
        [from_south[:, :, 2:4], north,
         from_south[:, :, 4:5], jnp.zeros((two, levels, 3, cols), jnp.float32)], 2)
    return from_east, from_west, halo_y


def on_device(
    temp_before, temp_now, salt_before, salt_now, east_velocity, north_velocity, bottom_level
):
    at_fold = lax.axis_index("lat") == lax.axis_size("lat") - 1
    xpack, ypack = edge_call(bottom_level, temp_now, salt_now, east_velocity, north_velocity)
    from_east, from_west, halo_y = exchange(xpack, ypack, at_fold)
    ft, fs, at, as_, xpack, ypack = step_call(
        True, False, bottom_level, temp_now, salt_now, temp_before, salt_before,
        from_east, from_west, halo_y, east_velocity, north_velocity)
    from_east, from_west, halo_y = exchange(xpack, ypack, at_fold)
    return step_call(False, True, bottom_level, at, as_, ft, fs, from_east, from_west, halo_y,
                     east_velocity, north_velocity)


def solution(mesh):
    return jax.shard_map(
        on_device,
        mesh=mesh,
        in_specs=(
            P(None, "lat", "lon"),
            P(None, "lat", "lon"),
            P(None, "lat", "lon"),
            P(None, "lat", "lon"),
            P(None, "lat", "lon"),
            P(None, "lat", "lon"),
            P("lat", "lon"),
        ),
        out_specs=(P(None, "lat", "lon"), P(None, "lat", "lon"), P(None, "lat", "lon")),
        check_vma=False,
    )
```

```python
import functools
import jax
import jax.numpy as jnp
from jax import lax
from jax.experimental import pallas as pl
from jax.experimental.pallas import tpu as pltpu
from jax.sharding import PartitionSpec as P

asselin_gamma = 0.1
nu_base = 0.05
nu_conv = 0.2
level_depth = 160.0
alpha_zero = 0.1655
beta_zero = 0.76554
lambda_one = 0.05952
lambda_two = 0.00054914
mu_one = 0.0001497
mu_two = 1.109e-05
nu_cross = 0.0024341


def density_at(temp, salt, depth):
    warm = -alpha_zero * (1.0 + 0.5 * lambda_one * temp + mu_one * depth) * temp
    salty = beta_zero * (1.0 - 0.5 * lambda_two * salt - mu_two * depth) * salt
    return warm + salty - nu_cross * temp * salt


def face_flux(u, q1, q2, q3, q4):
    flux = u * (7.0 * (q2 + q3) - (q1 + q4)) + jnp.abs(u) * ((q4 - q1) - 3.0 * (q3 - q2))
    return flux * (1.0 / 12.0)


def lane_roll(value, shift):
    shift = shift % value.shape[-1]
    return value if shift == 0 else pltpu.roll(value, shift, 1)


def column_pack(value, east_v):
    rows, cols = value.shape
    lane = lax.broadcasted_iota(jnp.int32, (8, cols), 1)
    pack = jnp.zeros((8, cols), jnp.float32)
    for a in range(rows // 8):
        part = lane_roll(value[8 * a:8 * a + 8], 4 * a)
        lo_lane = (4 * a - 2) % cols
        pack = jnp.where((lane >= 4 * a) & (lane < 4 * a + 2), part, pack)
        pack = jnp.where((lane >= lo_lane) & (lane < lo_lane + 2), part, pack)
        pack = jnp.where(lane == 64 + 4 * a, lane_roll(east_v[8 * a:8 * a + 8], 4 * a + 65), pack)
    return pack


def column_unpack(from_east, from_west, with_velocity):
    cols = from_east.shape[-1]
    lane = lax.broadcasted_iota(jnp.int32, (8, cols), 1)
    both = jnp.where(lane % 4 < 2, from_east, from_west)
    return both, [lane_roll(both, -4 * a) for a in range(8)]


def sub_roll(value, shift):
    shift = shift % value.shape[0]
    return value if shift == 0 else pltpu.roll(value, shift, 0)


def write_rows(value, north_v, ypack_ref, f, k):
    rows, cols = value.shape
    ypack_ref[f, k, 0:2, :] = value[0:2]
    ypack_ref[f, k, 2:4, :] = value[rows - 2:rows]
    ypack_ref[f, k, 4:5, :] = north_v[rows - 1:rows]
    ypack_ref[f, k, 5:8, :] = jnp.zeros((3, cols), jnp.float32)


def edge_kernel(bl_ref, nt_ref, ns_ref, ue_ref, vn_ref, xpack_ref, ypack_ref):
    levels, rows, cols = nt_ref.shape

    def level(k, carry):
        m = (k < bl_ref[...]).astype(jnp.float32)
        for f, ref in enumerate((nt_ref, ns_ref)):
            value = ref[k] * m
            xpack_ref[f, k] = column_pack(value, ue_ref[k])
            write_rows(value, vn_ref[k], ypack_ref, f, k)
        return carry

    lax.fori_loop(0, levels, level, 0, unroll=True)


def mixing_kernel(mask_inputs, bl_ref, nt_ref, ns_ref, bt_ref, bs_ref, fv):
    levels, rows, cols = nt_ref.shape
    bef_refs = (bt_ref, bs_ref)

    def mask(k):
        return (k < bl_ref[...]).astype(jnp.float32)

    def depth(k):
        return level_depth * (k.astype(jnp.float32) + 0.5)

    def load(ref, k, m):
        v = ref[k]
        return v * m if mask_inputs else v

    zero = jnp.zeros((rows, cols), jnp.float32)
    for f in range(2):
        fv[f, 0] = zero
        fv[f, levels] = zero

    def mixing(k, carry):
        m0, m1 = mask(k), mask(k + 1)
        e0 = density_at(load(nt_ref, k, m0), load(ns_ref, k, m0), depth(k))
        e1 = density_at(load(nt_ref, k + 1, m1), load(ns_ref, k + 1, m1), depth(k + 1))
        rates = (nu_base + nu_conv * jax.nn.sigmoid(-4.0 * (e1 - e0))) * m1
        for f in range(2):
            fv[f, k + 1] = rates * (load(bef_refs[f], k + 1, m1) - load(bef_refs[f], k, m0))
        return carry

    lax.fori_loop(0, levels - 1, mixing, 0)


def step_kernel(mask_inputs, final, bl_ref, nt_ref, ns_ref, bt_ref, bs_ref, xe_ref, xw_ref, yh_ref,
                ue_ref, vn_ref, fv, *outs):
    levels, rows, cols = nt_ref.shape
    lane = lax.broadcasted_iota(jnp.int32, (rows, cols), 1)
    row = lax.broadcasted_iota(jnp.int32, (rows, cols), 0)
    now_refs, bef_refs = (nt_ref, ns_ref), (bt_ref, bs_ref)

    def mask(k):
        return (k < bl_ref[...]).astype(jnp.float32)

    def depth(k):
        return level_depth * (k.astype(jnp.float32) + 0.5)

    def load(ref, k, m):
        v = ref[k]
        return v * m if mask_inputs else v

    strips = rows // 8
    lane8 = lax.broadcasted_iota(jnp.int32, (8, cols), 1)
    sub8 = lax.broadcasted_iota(jnp.int32, (8, cols), 0)

    def split(value):
        return [value[8 * a:8 * a + 8] for a in range(strips)]

    def level(k, carry):
        m = split(mask(k))
        ue, vn = split(ue_ref[k]), split(vn_ref[k])
        south_v = jnp.where(sub8 == 7, jnp.broadcast_to(yh_ref[0, k][4:5], (8, cols)), 0.0)
        depth_k = depth(k)
        afters = [[None] * strips for _ in range(2)]
        for f in range(2):
            q = split(load(now_refs[f], k, mask(k)))
            b = split(load(bef_refs[f], k, mask(k)))
            from_west = xw_ref[f, k]
            both, hs = column_unpack(xe_ref[f, k], from_west, False)
            own = jnp.zeros((8, cols), jnp.float32)
            for a in range(strips):
                own = jnp.where((lane8 >= 4 * a) & (lane8 < 4 * a + 2), lane_roll(q[a], 4 * a), own)
            west_face = face_flux(lane_roll(from_west, -64), lane_roll(both, 2), lane_roll(both, 1),
                                  own, lane_roll(own, -1))
            yh = yh_ref[f, k]
            below = jnp.where(sub8 == 6, jnp.broadcast_to(yh[0:1], (8, cols)),
                              jnp.broadcast_to(yh[1:2], (8, cols)))
            above = jnp.where(sub8 == 0, jnp.broadcast_to(yh[2:3], (8, cols)),
                              jnp.broadcast_to(yh[3:4], (8, cols)))
            qx = q + [above]
            north_prev = face_flux(south_v, sub_roll(below, 1), below, sub_roll(q[0], 7), sub_roll(q[0], 6))
            lo = below
            fv_lo, fv_hi = split(fv[f, k]), split(fv[f, k + 1])
            for a in range(strips):
                qa, ha, hi = q[a], hs[a], qx[a + 1]
                qm1 = lane_roll(jnp.where(lane8 == cols - 1, ha, qa), 1)
                qp1 = lane_roll(jnp.where(lane8 < 1, ha, qa), -1)
                qp2 = lane_roll(jnp.where(lane8 < 2, ha, qa), -2)
                east_f = face_flux(ue[a], qm1, qa, qp1, qp2)
                west_f = jnp.where(lane8 < 1, lane_roll(west_face, -4 * a), lane_roll(east_f, 1))
                qs1 = sub_roll(jnp.where(sub8 == 7, lo, qa), 1)
                qn1 = sub_roll(jnp.where(sub8 < 1, hi, qa), 7)
                qn2 = sub_roll(jnp.where(sub8 < 2, hi, qa), 6)
                north_f = face_flux(vn[a], qs1, qa, qn1, qn2)
                south_f = sub_roll(jnp.where(sub8 == 7, north_prev, north_f), 1)
                north_prev, lo = north_f, qa
                div_x = east_f - west_f
                div_y = north_f - south_f
                change = -(div_x + div_y)
                change = change + (fv_hi[a] - fv_lo[a])
                after = (b[a] + 2.0 * change) * m[a]
                afters[f][a] = after
                rs = pl.ds(8 * a, 8)
                if not final:
                    outs[f][k, rs, :] = qa + asselin_gamma * (b[a] - 2.0 * qa + after)
                    outs[2 + f][k, rs, :] = after
                else:
                    outs[f][k, rs, :] = after
            if not final:
                whole = jnp.concatenate(afters[f], 0)
                outs[4][f, k] = column_pack(whole, ue_ref[k])
                write_rows(whole, vn_ref[k], outs[5], f, k)
        if final:
            for a in range(strips):
                outs[2][k, pl.ds(8 * a, 8), :] = density_at(afters[0][a], afters[1][a], depth_k) * m[a]
        return carry

    lax.fori_loop(0, levels, level, 0)


VMEM_SPEC = pl.BlockSpec(memory_space=pltpu.VMEM)


def pack_shapes(levels, rows, cols):
    return (jax.ShapeDtypeStruct((2, levels, 8, cols), jnp.float32),
            jax.ShapeDtypeStruct((2, levels, 8, cols), jnp.float32))


def edge_call(bl, nt, ns, ue, vn):
    levels, rows, cols = nt.shape
    return pl.pallas_call(
        edge_kernel,
        out_shape=pack_shapes(levels, rows, cols),
        in_specs=[VMEM_SPEC] * 5,
        out_specs=(VMEM_SPEC, VMEM_SPEC),
        cost_estimate=pl.CostEstimate(
            flops=2 * 2 * levels * 8 * rows * cols, transcendentals=0,
            bytes_accessed=4 * levels * rows * cols * 5),
    )(bl, nt, ns, ue, vn)


def mixing_call(mask_inputs, bl, nt, ns, bt, bs):
    levels, rows, cols = nt.shape
    return pl.pallas_call(
        functools.partial(mixing_kernel, mask_inputs),
        out_shape=jax.ShapeDtypeStruct((2, levels + 1, rows, cols), jnp.float32),
        in_specs=[VMEM_SPEC] * 5,
        out_specs=VMEM_SPEC,
        cost_estimate=pl.CostEstimate(
            flops=60 * levels * rows * cols, transcendentals=levels * rows * cols,
            bytes_accessed=4 * levels * rows * cols * 7),
    )(bl, nt, ns, bt, bs)


def step_call(mask_inputs, final, bl, nt, ns, bt, bs, xe, xw, yh, ue, vn):
    levels, rows, cols = nt.shape
    fv = mixing_call(mask_inputs, bl, nt, ns, bt, bs)
    field = jax.ShapeDtypeStruct(nt.shape, jnp.float32)
    out_shape = (field,) * 3 if final else (field,) * 4 + pack_shapes(levels, rows, cols)
    return pl.pallas_call(
        functools.partial(step_kernel, mask_inputs, final),
        out_shape=out_shape,
        in_specs=[VMEM_SPEC] * 11,
        out_specs=tuple([VMEM_SPEC] * len(out_shape)),
        compiler_params=pltpu.CompilerParams(vmem_limit_bytes=48 * 1024 * 1024),
        cost_estimate=pl.CostEstimate(
            flops=300 * 2 * levels * rows * cols, transcendentals=0,
            bytes_accessed=4 * levels * rows * cols * (9 + len(out_shape))),
    )(bl, nt, ns, bt, bs, xe, xw, yh, ue, vn, fv)


def exchange(xpack, ypack, at_fold):
    lon_count, lat_count = (lax.axis_size("lon"), lax.axis_size("lat"))
    from_east = lax.ppermute(xpack, "lon", [(i, (i - 1) % lon_count) for i in range(lon_count)])
    from_west = lax.ppermute(xpack, "lon", [(i, (i + 1) % lon_count) for i in range(lon_count)])
    from_north = lax.ppermute(ypack, "lat", [(i, i - 1) for i in range(1, lat_count)])
    from_south = lax.ppermute(ypack, "lat", [(i, i + 1) for i in range(lat_count - 1)])
    top = lat_count - 1
    fold_pairs = [(d * lat_count + top, (lon_count - 1 - d) * lat_count + top) for d in range(lon_count)]
    partner = lax.ppermute(ypack[:, :, 2:4], ("lon", "lat"), fold_pairs)
    cols = ypack.shape[-1]
    flip = (jnp.arange(cols)[:, None] + jnp.arange(cols)[None, :] == cols - 1).astype(jnp.float32)
    flipped = jnp.einsum("fkrc,cd->fkrd", partner, flip, precision=lax.Precision.HIGHEST)
    mirror = jnp.concatenate([flipped[:, :, 1:2], flipped[:, :, 0:1]], 2)
    north = jnp.where(at_fold, mirror, from_north[:, :, 0:2])
    two, levels = xpack.shape[:2]
    halo_y = jnp.concatenate(
        [from_south[:, :, 2:4], north,
         from_south[:, :, 4:5], jnp.zeros((two, levels, 3, cols), jnp.float32)], 2)
    return from_east, from_west, halo_y


def on_device(
    temp_before, temp_now, salt_before, salt_now, east_velocity, north_velocity, bottom_level
):
    at_fold = lax.axis_index("lat") == lax.axis_size("lat") - 1
    xpack, ypack = edge_call(bottom_level, temp_now, salt_now, east_velocity, north_velocity)
    from_east, from_west, halo_y = exchange(xpack, ypack, at_fold)
    ft, fs, at, as_, xpack, ypack = step_call(
        True, False, bottom_level, temp_now, salt_now, temp_before, salt_before,
        from_east, from_west, halo_y, east_velocity, north_velocity)
    from_east, from_west, halo_y = exchange(xpack, ypack, at_fold)
    return step_call(False, True, bottom_level, at, as_, ft, fs, from_east, from_west, halo_y,
                     east_velocity, north_velocity)


def solution(mesh):
    return jax.shard_map(
        on_device,
        mesh=mesh,
        in_specs=(
            P(None, "lat", "lon"),
            P(None, "lat", "lon"),
            P(None, "lat", "lon"),
            P(None, "lat", "lon"),
            P(None, "lat", "lon"),
            P(None, "lat", "lon"),
            P("lat", "lon"),
        ),
        out_specs=(P(None, "lat", "lon"), P(None, "lat", "lon"), P(None, "lat", "lon")),
        check_vma=False,
    )
```

```python
import functools
import jax
import jax.numpy as jnp
from jax import lax
from jax.experimental import pallas as pl
from jax.experimental.pallas import tpu as pltpu
from jax.sharding import PartitionSpec as P

asselin_gamma = 0.1
nu_base = 0.05
nu_conv = 0.2
level_depth = 160.0
alpha_zero = 0.1655
beta_zero = 0.76554
lambda_one = 0.05952
lambda_two = 0.00054914
mu_one = 0.0001497
mu_two = 1.109e-05
nu_cross = 0.0024341


def density_at(temp, salt, depth):
    warm = -alpha_zero * (1.0 + 0.5 * lambda_one * temp + mu_one * depth) * temp
    salty = beta_zero * (1.0 - 0.5 * lambda_two * salt - mu_two * depth) * salt
    return warm + salty - nu_cross * temp * salt


def face_flux(u, q1, q2, q3, q4):
    flux = u * (7.0 * (q2 + q3) - (q1 + q4)) + jnp.abs(u) * ((q4 - q1) - 3.0 * (q3 - q2))
    return flux * (1.0 / 12.0)


def lane_roll(value, shift):
    shift = shift % value.shape[-1]
    return value if shift == 0 else pltpu.roll(value, shift, 1)


def column_pack(values, east_v):
    rows, cols = values[0].shape
    lane = lax.broadcasted_iota(jnp.int32, (8, cols), 1)
    pack = jnp.zeros((8, cols), jnp.float32)
    for f, value in enumerate(values):
        for a in range(rows // 8):
            part = lane_roll(value[8 * a:8 * a + 8], 4 * a + 32 * f)
            hi_lane = 4 * a + 32 * f
            lo_lane = (hi_lane - 2) % cols
            pack = jnp.where((lane >= hi_lane) & (lane < hi_lane + 2), part, pack)
            pack = jnp.where((lane >= lo_lane) & (lane < lo_lane + 2), part, pack)
    for a in range(rows // 8):
        pack = jnp.where(lane == 64 + 4 * a, lane_roll(east_v[8 * a:8 * a + 8], 4 * a + 65), pack)
    return pack


def column_unpack(from_east, from_west, with_velocity):
    cols = from_east.shape[-1]
    lane = lax.broadcasted_iota(jnp.int32, (8, cols), 1)
    both = jnp.where(lane % 4 < 2, from_east, from_west)
    return both, [lane_roll(both, -4 * a) for a in range(8)]


def sub_roll(value, shift):
    shift = shift % value.shape[0]
    return value if shift == 0 else pltpu.roll(value, shift, 0)


def write_rows(values, north_v, north_ref, south_ref, k):
    rows, cols = values[0].shape
    for f, value in enumerate(values):
        north_ref[k, 2 * f:2 * f + 2, :] = value[rows - 2:rows]
        south_ref[k, 2 * f:2 * f + 2, :] = value[0:2]
    north_ref[k, 4:5, :] = north_v[rows - 1:rows]
    north_ref[k, 5:8, :] = jnp.zeros((3, cols), jnp.float32)
    south_ref[k, 4:8, :] = jnp.zeros((4, cols), jnp.float32)


def edge_kernel(bl_ref, nt_ref, ns_ref, ue_ref, vn_ref, xpack_ref, north_ref, south_ref):
    levels, rows, cols = nt_ref.shape

    def level(k, carry):
        m = (k < bl_ref[...]).astype(jnp.float32)
        values = (nt_ref[k] * m, ns_ref[k] * m)
        xpack_ref[k] = column_pack(values, ue_ref[k])
        write_rows(values, vn_ref[k], north_ref, south_ref, k)
        return carry

    lax.fori_loop(0, levels, level, 0, unroll=True)


def step_kernel(mask_inputs, final, bl_ref, nt_ref, ns_ref, bt_ref, bs_ref, xe_ref, xw_ref, yh_ref,
                ue_ref, vn_ref, *rest):
    outs, fv = rest[:-1], rest[-1]
    levels, rows, cols = nt_ref.shape
    lane = lax.broadcasted_iota(jnp.int32, (rows, cols), 1)
    row = lax.broadcasted_iota(jnp.int32, (rows, cols), 0)
    now_refs, bef_refs = (nt_ref, ns_ref), (bt_ref, bs_ref)

    def mask(k):
        return (k < bl_ref[...]).astype(jnp.float32)

    def depth(k):
        return level_depth * (k.astype(jnp.float32) + 0.5)

    def load(ref, k, m):
        v = ref[k]
        return v * m if mask_inputs else v

    zero = jnp.zeros((rows, cols), jnp.float32)
    for f in range(2):
        fv[f, 0] = zero
        fv[f, levels] = zero

    def mixing(k, carry):
        m0, m1 = mask(k), mask(k + 1)
        e0 = density_at(load(nt_ref, k, m0), load(ns_ref, k, m0), depth(k))
        e1 = density_at(load(nt_ref, k + 1, m1), load(ns_ref, k + 1, m1), depth(k + 1))
        rates = (nu_base + nu_conv * jax.nn.sigmoid(-4.0 * (e1 - e0))) * m1
        for f in range(2):
            fv[f, k + 1] = rates * (load(bef_refs[f], k + 1, m1) - load(bef_refs[f], k, m0))
        return carry

    lax.fori_loop(0, levels - 1, mixing, 0)

    strips = rows // 8
    lane8 = lax.broadcasted_iota(jnp.int32, (8, cols), 1)
    sub8 = lax.broadcasted_iota(jnp.int32, (8, cols), 0)

    def split(value):
        return [value[8 * a:8 * a + 8] for a in range(strips)]

    def level(k, carry):
        m = split(mask(k))
        ue, vn = split(ue_ref[k]), split(vn_ref[k])
        south_v = jnp.where(sub8 == 7, jnp.broadcast_to(yh_ref[0, k][4:5], (8, cols)), 0.0)
        east_all, west_all = xe_ref[k], xw_ref[k]
        west_v = lane_roll(west_all, -64)
        depth_k = depth(k)
        afters = [[None] * strips for _ in range(2)]
        for f in range(2):
            q = split(load(now_refs[f], k, mask(k)))
            b = split(load(bef_refs[f], k, mask(k)))
            both, hs = column_unpack(lane_roll(east_all, -32 * f), lane_roll(west_all, -32 * f), False)
            own = jnp.zeros((8, cols), jnp.float32)
            for a in range(strips):
                own = jnp.where((lane8 >= 4 * a) & (lane8 < 4 * a + 2), lane_roll(q[a], 4 * a), own)
            west_face = face_flux(west_v, lane_roll(both, 2), lane_roll(both, 1),
                                  own, lane_roll(own, -1))
            yh = yh_ref[f, k]
            below = jnp.where(sub8 == 6, jnp.broadcast_to(yh[0:1], (8, cols)),
                              jnp.broadcast_to(yh[1:2], (8, cols)))
            above = jnp.where(sub8 == 0, jnp.broadcast_to(yh[2:3], (8, cols)),
                              jnp.broadcast_to(yh[3:4], (8, cols)))
            qx = q + [above]
            north_prev = face_flux(south_v, sub_roll(below, 1), below, sub_roll(q[0], 7), sub_roll(q[0], 6))
            lo = below
            fv_lo, fv_hi = split(fv[f, k]), split(fv[f, k + 1])
            for a in range(strips):
                qa, ha, hi = q[a], hs[a], qx[a + 1]
                qm1 = lane_roll(jnp.where(lane8 == cols - 1, ha, qa), 1)
                qp1 = lane_roll(jnp.where(lane8 < 1, ha, qa), -1)
                qp2 = lane_roll(jnp.where(lane8 < 2, ha, qa), -2)
                east_f = face_flux(ue[a], qm1, qa, qp1, qp2)
                west_f = jnp.where(lane8 < 1, lane_roll(west_face, -4 * a), lane_roll(east_f, 1))
                qs1 = sub_roll(jnp.where(sub8 == 7, lo, qa), 1)
                qn1 = sub_roll(jnp.where(sub8 < 1, hi, qa), 7)
                qn2 = sub_roll(jnp.where(sub8 < 2, hi, qa), 6)
                north_f = face_flux(vn[a], qs1, qa, qn1, qn2)
                south_f = sub_roll(jnp.where(sub8 == 7, north_prev, north_f), 1)
                north_prev, lo = north_f, qa
                div_x = east_f - west_f
                div_y = north_f - south_f
                change = -(div_x + div_y)
                change = change + (fv_hi[a] - fv_lo[a])
                after = (b[a] + 2.0 * change) * m[a]
                afters[f][a] = after
                rs = pl.ds(8 * a, 8)
                if not final:
                    outs[f][k, rs, :] = qa + asselin_gamma * (b[a] - 2.0 * qa + after)
                    outs[2 + f][k, rs, :] = after
                else:
                    outs[f][k, rs, :] = after
        if not final:
            wholes = [jnp.concatenate(afters[f], 0) for f in range(2)]
            outs[4][k] = column_pack(wholes, ue_ref[k])
            write_rows(wholes, vn_ref[k], outs[5], outs[6], k)
        if final:
            for a in range(strips):
                outs[2][k, pl.ds(8 * a, 8), :] = density_at(afters[0][a], afters[1][a], depth_k) * m[a]
        return carry

    lax.fori_loop(0, levels, level, 0)


VMEM_SPEC = pl.BlockSpec(memory_space=pltpu.VMEM)


def pack_shapes(levels, rows, cols):
    return (jax.ShapeDtypeStruct((levels, 8, cols), jnp.float32),) * 3


def edge_call(bl, nt, ns, ue, vn):
    levels, rows, cols = nt.shape
    return pl.pallas_call(
        edge_kernel,
        out_shape=pack_shapes(levels, rows, cols),
        in_specs=[VMEM_SPEC] * 5,
        out_specs=(VMEM_SPEC,) * 3,
        cost_estimate=pl.CostEstimate(
            flops=2 * 2 * levels * 8 * rows * cols, transcendentals=0,
            bytes_accessed=4 * levels * rows * cols * 5),
    )(bl, nt, ns, ue, vn)


def step_call(mask_inputs, final, bl, nt, ns, bt, bs, xe, xw, yh, ue, vn):
    levels, rows, cols = nt.shape
    field = jax.ShapeDtypeStruct(nt.shape, jnp.float32)
    out_shape = (field,) * 3 if final else (field,) * 4 + pack_shapes(levels, rows, cols)
    return pl.pallas_call(
        functools.partial(step_kernel, mask_inputs, final),
        out_shape=out_shape,
        in_specs=[VMEM_SPEC] * 10,
        out_specs=tuple([VMEM_SPEC] * len(out_shape)),
        scratch_shapes=[pltpu.VMEM((2, levels + 1, rows, cols), jnp.float32)],
        compiler_params=pltpu.CompilerParams(vmem_limit_bytes=48 * 1024 * 1024),
        cost_estimate=pl.CostEstimate(
            flops=400 * 2 * levels * rows * cols, transcendentals=levels * rows * cols,
            bytes_accessed=4 * levels * rows * cols * (9 + len(out_shape))),
    )(bl, nt, ns, bt, bs, xe, xw, yh, ue, vn)


def exchange(xpack, north_pack, south_pack, at_fold):
    lon_count, lat_count = (lax.axis_size("lon"), lax.axis_size("lat"))
    from_east = lax.ppermute(xpack, "lon", [(i, (i - 1) % lon_count) for i in range(lon_count)])
    from_west = lax.ppermute(xpack, "lon", [(i, (i + 1) % lon_count) for i in range(lon_count)])
    from_north = lax.ppermute(south_pack, "lat", [(i, i - 1) for i in range(1, lat_count)])
    from_south = lax.ppermute(north_pack, "lat", [(i, i + 1) for i in range(lat_count - 1)])
    top = lat_count - 1
    fold_pairs = [(d * lat_count + top, (lon_count - 1 - d) * lat_count + top) for d in range(lon_count)]
    partner = lax.ppermute(north_pack[:, 0:4], ("lon", "lat"), fold_pairs)
    cols = xpack.shape[-1]
    flip = (jnp.arange(cols)[:, None] + jnp.arange(cols)[None, :] == cols - 1).astype(jnp.float32)
    flipped = jnp.einsum("krc,cd->krd", partner, flip, precision=lax.Precision.HIGHEST)
    levels = xpack.shape[0]
    halo_y = []
    for f in range(2):
        mirror = jnp.concatenate([flipped[:, 2 * f + 1:2 * f + 2], flipped[:, 2 * f:2 * f + 1]], 1)
        north = jnp.where(at_fold, mirror, from_north[:, 2 * f:2 * f + 2])
        halo_y.append(jnp.concatenate(
            [from_south[:, 2 * f:2 * f + 2], north, from_south[:, 4:5],
             jnp.zeros((levels, 3, cols), jnp.float32)], 1))
    return from_east, from_west, jnp.stack(halo_y)


def on_device(
    temp_before, temp_now, salt_before, salt_now, east_velocity, north_velocity, bottom_level
):
    at_fold = lax.axis_index("lat") == lax.axis_size("lat") - 1
    packs = edge_call(bottom_level, temp_now, salt_now, east_velocity, north_velocity)
    from_east, from_west, halo_y = exchange(*packs, at_fold)
    ft, fs, at, as_, *packs = step_call(
        True, False, bottom_level, temp_now, salt_now, temp_before, salt_before,
        from_east, from_west, halo_y, east_velocity, north_velocity)
    from_east, from_west, halo_y = exchange(*packs, at_fold)
    return step_call(False, True, bottom_level, at, as_, ft, fs, from_east, from_west, halo_y,
                     east_velocity, north_velocity)


def solution(mesh):
    return jax.shard_map(
        on_device,
        mesh=mesh,
        in_specs=(
            P(None, "lat", "lon"),
            P(None, "lat", "lon"),
            P(None, "lat", "lon"),
            P(None, "lat", "lon"),
            P(None, "lat", "lon"),
            P(None, "lat", "lon"),
            P("lat", "lon"),
        ),
        out_specs=(P(None, "lat", "lon"), P(None, "lat", "lon"), P(None, "lat", "lon")),
        check_vma=False,
    )
```

```python
import functools
import jax
import jax.numpy as jnp
from jax import lax
from jax.experimental import pallas as pl
from jax.experimental.pallas import tpu as pltpu
from jax.sharding import PartitionSpec as P

asselin_gamma = 0.1
nu_base = 0.05
nu_conv = 0.2
level_depth = 160.0
alpha_zero = 0.1655
beta_zero = 0.76554
lambda_one = 0.05952
lambda_two = 0.00054914
mu_one = 0.0001497
mu_two = 1.109e-05
nu_cross = 0.0024341


def density_at(temp, salt, depth):
    warm = -alpha_zero * (1.0 + 0.5 * lambda_one * temp + mu_one * depth) * temp
    salty = beta_zero * (1.0 - 0.5 * lambda_two * salt - mu_two * depth) * salt
    return warm + salty - nu_cross * temp * salt


def face_flux(u, q1, q2, q3, q4):
    flux = u * (7.0 * (q2 + q3) - (q1 + q4)) + jnp.abs(u) * ((q4 - q1) - 3.0 * (q3 - q2))
    return flux * (1.0 / 12.0)


def lane_roll(value, shift):
    shift = shift % value.shape[-1]
    return value if shift == 0 else pltpu.roll(value, shift, 1)


def column_pack(value, east_v):
    rows, cols = value.shape
    lane = lax.broadcasted_iota(jnp.int32, (8, cols), 1)
    pack = jnp.zeros((8, cols), jnp.float32)
    for a in range(rows // 8):
        part = lane_roll(value[8 * a:8 * a + 8], 4 * a)
        lo_lane = (4 * a - 2) % cols
        pack = jnp.where((lane >= 4 * a) & (lane < 4 * a + 2), part, pack)
        pack = jnp.where((lane >= lo_lane) & (lane < lo_lane + 2), part, pack)
        pack = jnp.where(lane == 64 + 4 * a, lane_roll(east_v[8 * a:8 * a + 8], 4 * a + 65), pack)
    return pack


def column_unpack(from_east, from_west, with_velocity):
    cols = from_east.shape[-1]
    lane = lax.broadcasted_iota(jnp.int32, (8, cols), 1)
    both = jnp.where(lane % 4 < 2, from_east, from_west)
    return both, [lane_roll(both, -4 * a) for a in range(8)]


def sub_roll(value, shift):
    shift = shift % value.shape[0]
    return value if shift == 0 else pltpu.roll(value, shift, 0)


def write_rows(value, north_v, ypack_ref, f, k):
    rows, cols = value.shape
    ypack_ref[f, k, 0:2, :] = value[0:2]
    ypack_ref[f, k, 2:4, :] = value[rows - 2:rows]
    ypack_ref[f, k, 4:5, :] = north_v[rows - 1:rows]
    ypack_ref[f, k, 5:8, :] = jnp.zeros((3, cols), jnp.float32)


def edge_kernel(bl_ref, nt_ref, ns_ref, ue_ref, vn_ref, xpack_ref, ypack_ref):
    levels, rows, cols = nt_ref.shape

    def level(k, carry):
        m = (k < bl_ref[...]).astype(jnp.float32)
        for f, ref in enumerate((nt_ref, ns_ref)):
            value = ref[k] * m
            xpack_ref[f, k] = column_pack(value, ue_ref[k])
            write_rows(value, vn_ref[k], ypack_ref, f, k)
        return carry

    lax.fori_loop(0, levels, level, 0, unroll=True)


def step_kernel(mask_inputs, final, bl_ref, nt_ref, ns_ref, bt_ref, bs_ref, xe_ref, xw_ref, yh_ref,
                ue_ref, vn_ref, *rest):
    outs, fv = rest[:-1], rest[-1]
    levels, rows, cols = nt_ref.shape
    lane = lax.broadcasted_iota(jnp.int32, (rows, cols), 1)
    row = lax.broadcasted_iota(jnp.int32, (rows, cols), 0)
    now_refs, bef_refs = (nt_ref, ns_ref), (bt_ref, bs_ref)

    def mask(k):
        return (k < bl_ref[...]).astype(jnp.float32)

    def depth(k):
        return level_depth * (k.astype(jnp.float32) + 0.5)

    def load(ref, k, m):
        v = ref[k]
        return v * m if mask_inputs else v

    zero = jnp.zeros((rows, cols), jnp.float32)
    for f in range(2):
        fv[f, 0] = zero
        fv[f, levels] = zero

    def mixing(k, carry):
        m0, m1 = mask(k), mask(k + 1)
        e0 = density_at(load(nt_ref, k, m0), load(ns_ref, k, m0), depth(k))
        e1 = density_at(load(nt_ref, k + 1, m1), load(ns_ref, k + 1, m1), depth(k + 1))
        rates = (nu_base + nu_conv * jax.nn.sigmoid(-4.0 * (e1 - e0))) * m1
        for f in range(2):
            fv[f, k + 1] = rates * (load(bef_refs[f], k + 1, m1) - load(bef_refs[f], k, m0))
        return carry

    lax.fori_loop(0, levels - 1, mixing, 0)

    strips = rows // 8
    lane8 = lax.broadcasted_iota(jnp.int32, (8, cols), 1)
    sub8 = lax.broadcasted_iota(jnp.int32, (8, cols), 0)

    def split(value):
        return [value[8 * a:8 * a + 8] for a in range(strips)]

    def level(k, carry):
        m = split(mask(k))
        ue, vn = split(ue_ref[k]), split(vn_ref[k])
        south_v = jnp.where(sub8 == 7, jnp.broadcast_to(yh_ref[0, k][4:5], (8, cols)), 0.0)
        depth_k = depth(k)
        afters = [[None] * strips for _ in range(2)]
        for f in range(2):
            q = split(load(now_refs[f], k, mask(k)))
            b = split(load(bef_refs[f], k, mask(k)))
            from_west = xw_ref[f, k]
            both, hs = column_unpack(xe_ref[f, k], from_west, False)
            own = jnp.zeros((8, cols), jnp.float32)
            for a in range(strips):
                own = jnp.where((lane8 >= 4 * a) & (lane8 < 4 * a + 2), lane_roll(q[a], 4 * a), own)
            west_face = face_flux(lane_roll(from_west, -64), lane_roll(both, 2), lane_roll(both, 1),
                                  own, lane_roll(own, -1))
            yh = yh_ref[f, k]
            below = jnp.where(sub8 == 6, jnp.broadcast_to(yh[0:1], (8, cols)),
                              jnp.broadcast_to(yh[1:2], (8, cols)))
            above = jnp.where(sub8 == 0, jnp.broadcast_to(yh[2:3], (8, cols)),
                              jnp.broadcast_to(yh[3:4], (8, cols)))
            qx = q + [above]
            north_prev = face_flux(south_v, sub_roll(below, 1), below, sub_roll(q[0], 7), sub_roll(q[0], 6))
            lo = below
            fv_lo, fv_hi = split(fv[f, k]), split(fv[f, k + 1])
            for a in range(strips):
                qa, ha, hi = q[a], hs[a], qx[a + 1]
                qm1 = lane_roll(jnp.where(lane8 == cols - 1, ha, qa), 1)
                qp1 = lane_roll(jnp.where(lane8 < 1, ha, qa), -1)
                qp2 = lane_roll(jnp.where(lane8 < 2, ha, qa), -2)
                east_f = face_flux(ue[a], qm1, qa, qp1, qp2)
                west_f = jnp.where(lane8 < 1, lane_roll(west_face, -4 * a), lane_roll(east_f, 1))
                qs1 = sub_roll(jnp.where(sub8 == 7, lo, qa), 1)
                qn1 = sub_roll(jnp.where(sub8 < 1, hi, qa), 7)
                qn2 = sub_roll(jnp.where(sub8 < 2, hi, qa), 6)
                north_f = face_flux(vn[a], qs1, qa, qn1, qn2)
                south_f = sub_roll(jnp.where(sub8 == 7, north_prev, north_f), 1)
                north_prev, lo = north_f, qa
                div_x = east_f - west_f
                div_y = north_f - south_f
                change = -(div_x + div_y)
                change = change + (fv_hi[a] - fv_lo[a])
                after = (b[a] + 2.0 * change) * m[a]
                afters[f][a] = after
                rs = pl.ds(8 * a, 8)
                if not final:
                    outs[f][k, rs, :] = qa + asselin_gamma * (b[a] - 2.0 * qa + after)
                    outs[2 + f][k, rs, :] = after
                else:
                    outs[f][k, rs, :] = after
            if not final:
                whole = jnp.concatenate(afters[f], 0)
                outs[4][f, k] = column_pack(whole, ue_ref[k])
                write_rows(whole, vn_ref[k], outs[5], f, k)
        if final:
            for a in range(strips):
                outs[2][k, pl.ds(8 * a, 8), :] = density_at(afters[0][a], afters[1][a], depth_k) * m[a]
        return carry

    lax.fori_loop(0, levels, level, 0, unroll=2)


VMEM_SPEC = pl.BlockSpec(memory_space=pltpu.VMEM)


def pack_shapes(levels, rows, cols):
    return (jax.ShapeDtypeStruct((2, levels, 8, cols), jnp.float32),
            jax.ShapeDtypeStruct((2, levels, 8, cols), jnp.float32))


def edge_call(bl, nt, ns, ue, vn):
    levels, rows, cols = nt.shape
    return pl.pallas_call(
        edge_kernel,
        out_shape=pack_shapes(levels, rows, cols),
        in_specs=[VMEM_SPEC] * 5,
        out_specs=(VMEM_SPEC, VMEM_SPEC),
        cost_estimate=pl.CostEstimate(
            flops=2 * 2 * levels * 8 * rows * cols, transcendentals=0,
            bytes_accessed=4 * levels * rows * cols * 5),
    )(bl, nt, ns, ue, vn)


def step_call(mask_inputs, final, bl, nt, ns, bt, bs, xe, xw, yh, ue, vn):
    levels, rows, cols = nt.shape
    field = jax.ShapeDtypeStruct(nt.shape, jnp.float32)
    out_shape = (field,) * 3 if final else (field,) * 4 + pack_shapes(levels, rows, cols)
    return pl.pallas_call(
        functools.partial(step_kernel, mask_inputs, final),
        out_shape=out_shape,
        in_specs=[VMEM_SPEC] * 10,
        out_specs=tuple([VMEM_SPEC] * len(out_shape)),
        scratch_shapes=[pltpu.VMEM((2, levels + 1, rows, cols), jnp.float32)],
        compiler_params=pltpu.CompilerParams(vmem_limit_bytes=48 * 1024 * 1024),
        cost_estimate=pl.CostEstimate(
            flops=400 * 2 * levels * rows * cols, transcendentals=levels * rows * cols,
            bytes_accessed=4 * levels * rows * cols * (9 + len(out_shape))),
    )(bl, nt, ns, bt, bs, xe, xw, yh, ue, vn)


def exchange(xpack, ypack, at_fold):
    lon_count, lat_count = (lax.axis_size("lon"), lax.axis_size("lat"))
    from_east = lax.ppermute(xpack, "lon", [(i, (i - 1) % lon_count) for i in range(lon_count)])
    from_west = lax.ppermute(xpack, "lon", [(i, (i + 1) % lon_count) for i in range(lon_count)])
    from_north = lax.ppermute(ypack, "lat", [(i, i - 1) for i in range(1, lat_count)])
    from_south = lax.ppermute(ypack, "lat", [(i, i + 1) for i in range(lat_count - 1)])
    top = lat_count - 1
    fold_pairs = [(d * lat_count + top, (lon_count - 1 - d) * lat_count + top) for d in range(lon_count)]
    partner = lax.ppermute(ypack[:, :, 2:4], ("lon", "lat"), fold_pairs)
    cols = ypack.shape[-1]
    flip = (jnp.arange(cols)[:, None] + jnp.arange(cols)[None, :] == cols - 1).astype(jnp.float32)
    flipped = jnp.einsum("fkrc,cd->fkrd", partner, flip, precision=lax.Precision.HIGHEST)
    mirror = jnp.concatenate([flipped[:, :, 1:2], flipped[:, :, 0:1]], 2)
    north = jnp.where(at_fold, mirror, from_north[:, :, 0:2])
    two, levels = xpack.shape[:2]
    halo_y = jnp.concatenate(
        [from_south[:, :, 2:4], north,
         from_south[:, :, 4:5], jnp.zeros((two, levels, 3, cols), jnp.float32)], 2)
    return from_east, from_west, halo_y


def on_device(
    temp_before, temp_now, salt_before, salt_now, east_velocity, north_velocity, bottom_level
):
    at_fold = lax.axis_index("lat") == lax.axis_size("lat") - 1
    xpack, ypack = edge_call(bottom_level, temp_now, salt_now, east_velocity, north_velocity)
    from_east, from_west, halo_y = exchange(xpack, ypack, at_fold)
    ft, fs, at, as_, xpack, ypack = step_call(
        True, False, bottom_level, temp_now, salt_now, temp_before, salt_before,
        from_east, from_west, halo_y, east_velocity, north_velocity)
    from_east, from_west, halo_y = exchange(xpack, ypack, at_fold)
    return step_call(False, True, bottom_level, at, as_, ft, fs, from_east, from_west, halo_y,
                     east_velocity, north_velocity)


def solution(mesh):
    return jax.shard_map(
        on_device,
        mesh=mesh,
        in_specs=(
            P(None, "lat", "lon"),
            P(None, "lat", "lon"),
            P(None, "lat", "lon"),
            P(None, "lat", "lon"),
            P(None, "lat", "lon"),
            P(None, "lat", "lon"),
            P("lat", "lon"),
        ),
        out_specs=(P(None, "lat", "lon"), P(None, "lat", "lon"), P(None, "lat", "lon")),
        check_vma=False,
    )
```

```python
import functools
import jax
import jax.numpy as jnp
from jax import lax
from jax.experimental import pallas as pl
from jax.experimental.pallas import tpu as pltpu
from jax.sharding import PartitionSpec as P

asselin_gamma = 0.1
nu_base = 0.05
nu_conv = 0.2
level_depth = 160.0
alpha_zero = 0.1655
beta_zero = 0.76554
lambda_one = 0.05952
lambda_two = 0.00054914
mu_one = 0.0001497
mu_two = 1.109e-05
nu_cross = 0.0024341


def density_at(temp, salt, depth):
    warm = -alpha_zero * (1.0 + 0.5 * lambda_one * temp + mu_one * depth) * temp
    salty = beta_zero * (1.0 - 0.5 * lambda_two * salt - mu_two * depth) * salt
    return warm + salty - nu_cross * temp * salt


def face_flux(u, q1, q2, q3, q4):
    flux = u * (7.0 * (q2 + q3) - (q1 + q4)) + jnp.abs(u) * ((q4 - q1) - 3.0 * (q3 - q2))
    return flux * (1.0 / 12.0)


def lane_roll(value, shift):
    shift = shift % value.shape[-1]
    return value if shift == 0 else pltpu.roll(value, shift, 1)


def column_pack(value, east_v):
    rows, cols = value.shape
    lane = lax.broadcasted_iota(jnp.int32, (8, cols), 1)
    pack = jnp.zeros((8, cols), jnp.float32)
    for a in range(rows // 8):
        part = lane_roll(value[8 * a:8 * a + 8], 4 * a)
        lo_lane = (4 * a - 2) % cols
        pack = jnp.where((lane >= 4 * a) & (lane < 4 * a + 2), part, pack)
        pack = jnp.where((lane >= lo_lane) & (lane < lo_lane + 2), part, pack)
        pack = jnp.where(lane == 64 + 4 * a, lane_roll(east_v[8 * a:8 * a + 8], 4 * a + 65), pack)
    return pack


def column_unpack(from_east, from_west, with_velocity):
    cols = from_east.shape[-1]
    lane = lax.broadcasted_iota(jnp.int32, (8, cols), 1)
    both = jnp.where(lane % 4 < 2, from_east, from_west)
    return both, [lane_roll(both, -4 * a) for a in range(8)]


def sub_roll(value, shift):
    shift = shift % value.shape[0]
    return value if shift == 0 else pltpu.roll(value, shift, 0)


def write_rows(value, north_v, ypack_ref, f, k):
    rows, cols = value.shape
    ypack_ref[f, k, 0:2, :] = value[0:2]
    ypack_ref[f, k, 2:4, :] = value[rows - 2:rows]
    ypack_ref[f, k, 4:5, :] = north_v[rows - 1:rows]
    ypack_ref[f, k, 5:8, :] = jnp.zeros((3, cols), jnp.float32)


def edge_kernel(bl_ref, nt_ref, ns_ref, ue_ref, vn_ref, xpack_ref, ypack_ref):
    levels, rows, cols = nt_ref.shape

    def level(k, carry):
        m = (k < bl_ref[...]).astype(jnp.float32)
        for f, ref in enumerate((nt_ref, ns_ref)):
            value = ref[k] * m
            xpack_ref[f, k] = column_pack(value, ue_ref[k])
            write_rows(value, vn_ref[k], ypack_ref, f, k)
        return carry

    lax.fori_loop(0, levels, level, 0, unroll=True)


def step_kernel(mask_inputs, final, bl_ref, nt_ref, ns_ref, bt_ref, bs_ref, xe_ref, xw_ref, yh_ref,
                ue_ref, vn_ref, *rest):
    outs, fv = rest[:-1], rest[-1]
    levels, rows, cols = nt_ref.shape
    lane = lax.broadcasted_iota(jnp.int32, (rows, cols), 1)
    row = lax.broadcasted_iota(jnp.int32, (rows, cols), 0)
    now_refs, bef_refs = (nt_ref, ns_ref), (bt_ref, bs_ref)

    def mask(k):
        return (k < bl_ref[...]).astype(jnp.float32)

    def depth(k):
        return level_depth * (k.astype(jnp.float32) + 0.5)

    def load(ref, k, m):
        v = ref[k]
        return v * m if mask_inputs else v

    zero = jnp.zeros((rows, cols), jnp.float32)
    for f in range(2):
        fv[f, 0] = zero
        fv[f, levels] = zero

    def mixing(k, carry):
        m0, m1 = mask(k), mask(k + 1)
        e0 = density_at(load(nt_ref, k, m0), load(ns_ref, k, m0), depth(k))
        e1 = density_at(load(nt_ref, k + 1, m1), load(ns_ref, k + 1, m1), depth(k + 1))
        rates = (nu_base + nu_conv * jax.nn.sigmoid(-4.0 * (e1 - e0))) * m1
        for f in range(2):
            fv[f, k + 1] = rates * (load(bef_refs[f], k + 1, m1) - load(bef_refs[f], k, m0))
        return carry

    lax.fori_loop(0, levels - 1, mixing, 0)

    strips = rows // 8
    lane8 = lax.broadcasted_iota(jnp.int32, (8, cols), 1)
    sub8 = lax.broadcasted_iota(jnp.int32, (8, cols), 0)

    def split(value):
        return [value[8 * a:8 * a + 8] for a in range(strips)]

    def level(k, carry, fields=(0, 1)):
        m = split(mask(k))
        ue, vn = split(ue_ref[k]), split(vn_ref[k])
        south_v = jnp.where(sub8 == 7, jnp.broadcast_to(yh_ref[0, k][4:5], (8, cols)), 0.0)
        depth_k = depth(k)
        afters = [[None] * strips for _ in range(2)]
        for f in fields:
            q = split(load(now_refs[f], k, mask(k)))
            b = split(load(bef_refs[f], k, mask(k)))
            from_west = xw_ref[f, k]
            both, hs = column_unpack(xe_ref[f, k], from_west, False)
            own = jnp.zeros((8, cols), jnp.float32)
            for a in range(strips):
                own = jnp.where((lane8 >= 4 * a) & (lane8 < 4 * a + 2), lane_roll(q[a], 4 * a), own)
            west_face = face_flux(lane_roll(from_west, -64), lane_roll(both, 2), lane_roll(both, 1),
                                  own, lane_roll(own, -1))
            yh = yh_ref[f, k]
            below = jnp.where(sub8 == 6, jnp.broadcast_to(yh[0:1], (8, cols)),
                              jnp.broadcast_to(yh[1:2], (8, cols)))
            above = jnp.where(sub8 == 0, jnp.broadcast_to(yh[2:3], (8, cols)),
                              jnp.broadcast_to(yh[3:4], (8, cols)))
            qx = q + [above]
            north_prev = face_flux(south_v, sub_roll(below, 1), below, sub_roll(q[0], 7), sub_roll(q[0], 6))
            lo = below
            fv_lo, fv_hi = split(fv[f, k]), split(fv[f, k + 1])
            for a in range(strips):
                qa, ha, hi = q[a], hs[a], qx[a + 1]
                qm1 = lane_roll(jnp.where(lane8 == cols - 1, ha, qa), 1)
                qp1 = lane_roll(jnp.where(lane8 < 1, ha, qa), -1)
                qp2 = lane_roll(jnp.where(lane8 < 2, ha, qa), -2)
                east_f = face_flux(ue[a], qm1, qa, qp1, qp2)
                west_f = jnp.where(lane8 < 1, lane_roll(west_face, -4 * a), lane_roll(east_f, 1))
                qs1 = sub_roll(jnp.where(sub8 == 7, lo, qa), 1)
                qn1 = sub_roll(jnp.where(sub8 < 1, hi, qa), 7)
                qn2 = sub_roll(jnp.where(sub8 < 2, hi, qa), 6)
                north_f = face_flux(vn[a], qs1, qa, qn1, qn2)
                south_f = sub_roll(jnp.where(sub8 == 7, north_prev, north_f), 1)
                north_prev, lo = north_f, qa
                div_x = east_f - west_f
                div_y = north_f - south_f
                change = -(div_x + div_y)
                change = change + (fv_hi[a] - fv_lo[a])
                after = (b[a] + 2.0 * change) * m[a]
                afters[f][a] = after
                rs = pl.ds(8 * a, 8)
                if not final:
                    outs[f][k, rs, :] = qa + asselin_gamma * (b[a] - 2.0 * qa + after)
                    outs[2 + f][k, rs, :] = after
                else:
                    outs[f][k, rs, :] = after
            if not final:
                whole = jnp.concatenate(afters[f], 0)
                outs[4][f, k] = column_pack(whole, ue_ref[k])
                write_rows(whole, vn_ref[k], outs[5], f, k)
        if final:
            for a in range(strips):
                outs[2][k, pl.ds(8 * a, 8), :] = density_at(afters[0][a], afters[1][a], depth_k) * m[a]
        return carry

    if final:
        lax.fori_loop(0, levels, level, 0, unroll=2)
    else:
        for f in range(2):
            lax.fori_loop(0, levels, functools.partial(level, fields=(f,)), 0, unroll=3)


VMEM_SPEC = pl.BlockSpec(memory_space=pltpu.VMEM)


def pack_shapes(levels, rows, cols):
    return (jax.ShapeDtypeStruct((2, levels, 8, cols), jnp.float32),
            jax.ShapeDtypeStruct((2, levels, 8, cols), jnp.float32))


def edge_call(bl, nt, ns, ue, vn):
    levels, rows, cols = nt.shape
    return pl.pallas_call(
        edge_kernel,
        out_shape=pack_shapes(levels, rows, cols),
        in_specs=[VMEM_SPEC] * 5,
        out_specs=(VMEM_SPEC, VMEM_SPEC),
        cost_estimate=pl.CostEstimate(
            flops=2 * 2 * levels * 8 * rows * cols, transcendentals=0,
            bytes_accessed=4 * levels * rows * cols * 5),
    )(bl, nt, ns, ue, vn)


def step_call(mask_inputs, final, bl, nt, ns, bt, bs, xe, xw, yh, ue, vn):
    levels, rows, cols = nt.shape
    field = jax.ShapeDtypeStruct(nt.shape, jnp.float32)
    out_shape = (field,) * 3 if final else (field,) * 4 + pack_shapes(levels, rows, cols)
    return pl.pallas_call(
        functools.partial(step_kernel, mask_inputs, final),
        out_shape=out_shape,
        in_specs=[VMEM_SPEC] * 10,
        out_specs=tuple([VMEM_SPEC] * len(out_shape)),
        scratch_shapes=[pltpu.VMEM((2, levels + 1, rows, cols), jnp.float32)],
        compiler_params=pltpu.CompilerParams(vmem_limit_bytes=48 * 1024 * 1024),
        cost_estimate=pl.CostEstimate(
            flops=400 * 2 * levels * rows * cols, transcendentals=levels * rows * cols,
            bytes_accessed=4 * levels * rows * cols * (9 + len(out_shape))),
    )(bl, nt, ns, bt, bs, xe, xw, yh, ue, vn)


def exchange(xpack, ypack, at_fold):
    lon_count, lat_count = (lax.axis_size("lon"), lax.axis_size("lat"))
    from_east = lax.ppermute(xpack, "lon", [(i, (i - 1) % lon_count) for i in range(lon_count)])
    from_west = lax.ppermute(xpack, "lon", [(i, (i + 1) % lon_count) for i in range(lon_count)])
    from_north = lax.ppermute(ypack, "lat", [(i, i - 1) for i in range(1, lat_count)])
    from_south = lax.ppermute(ypack, "lat", [(i, i + 1) for i in range(lat_count - 1)])
    top = lat_count - 1
    fold_pairs = [(d * lat_count + top, (lon_count - 1 - d) * lat_count + top) for d in range(lon_count)]
    partner = lax.ppermute(ypack[:, :, 2:4], ("lon", "lat"), fold_pairs)
    cols = ypack.shape[-1]
    flip = (jnp.arange(cols)[:, None] + jnp.arange(cols)[None, :] == cols - 1).astype(jnp.float32)
    flipped = jnp.einsum("fkrc,cd->fkrd", partner, flip, precision=lax.Precision.HIGHEST)
    mirror = jnp.concatenate([flipped[:, :, 1:2], flipped[:, :, 0:1]], 2)
    north = jnp.where(at_fold, mirror, from_north[:, :, 0:2])
    two, levels = xpack.shape[:2]
    halo_y = jnp.concatenate(
        [from_south[:, :, 2:4], north,
         from_south[:, :, 4:5], jnp.zeros((two, levels, 3, cols), jnp.float32)], 2)
    return from_east, from_west, halo_y


def on_device(
    temp_before, temp_now, salt_before, salt_now, east_velocity, north_velocity, bottom_level
):
    at_fold = lax.axis_index("lat") == lax.axis_size("lat") - 1
    xpack, ypack = edge_call(bottom_level, temp_now, salt_now, east_velocity, north_velocity)
    from_east, from_west, halo_y = exchange(xpack, ypack, at_fold)
    ft, fs, at, as_, xpack, ypack = step_call(
        True, False, bottom_level, temp_now, salt_now, temp_before, salt_before,
        from_east, from_west, halo_y, east_velocity, north_velocity)
    from_east, from_west, halo_y = exchange(xpack, ypack, at_fold)
    return step_call(False, True, bottom_level, at, as_, ft, fs, from_east, from_west, halo_y,
                     east_velocity, north_velocity)


def solution(mesh):
    return jax.shard_map(
        on_device,
        mesh=mesh,
        in_specs=(
            P(None, "lat", "lon"),
            P(None, "lat", "lon"),
            P(None, "lat", "lon"),
            P(None, "lat", "lon"),
            P(None, "lat", "lon"),
            P(None, "lat", "lon"),
            P("lat", "lon"),
        ),
        out_specs=(P(None, "lat", "lon"), P(None, "lat", "lon"), P(None, "lat", "lon")),
        check_vma=False,
    )
```

```python
import functools
import jax
import jax.numpy as jnp
from jax import lax
from jax.experimental import pallas as pl
from jax.experimental.pallas import tpu as pltpu
from jax.sharding import PartitionSpec as P

asselin_gamma = 0.1
nu_base = 0.05
nu_conv = 0.2
level_depth = 160.0
alpha_zero = 0.1655
beta_zero = 0.76554
lambda_one = 0.05952
lambda_two = 0.00054914
mu_one = 0.0001497
mu_two = 1.109e-05
nu_cross = 0.0024341


def density_at(temp, salt, depth):
    warm = -alpha_zero * (1.0 + 0.5 * lambda_one * temp + mu_one * depth) * temp
    salty = beta_zero * (1.0 - 0.5 * lambda_two * salt - mu_two * depth) * salt
    return warm + salty - nu_cross * temp * salt


def face_flux(u, q1, q2, q3, q4):
    flux = u * (7.0 * (q2 + q3) - (q1 + q4)) + jnp.abs(u) * ((q4 - q1) - 3.0 * (q3 - q2))
    return flux * (1.0 / 12.0)


def lane_roll(value, shift):
    shift = shift % value.shape[-1]
    return value if shift == 0 else pltpu.roll(value, shift, 1)


def column_pack(value, east_v):
    rows, cols = value.shape
    lane = lax.broadcasted_iota(jnp.int32, (8, cols), 1)
    pack = jnp.zeros((8, cols), jnp.float32)
    for a in range(rows // 8):
        part = lane_roll(value[8 * a:8 * a + 8], 4 * a)
        lo_lane = (4 * a - 2) % cols
        pack = jnp.where((lane >= 4 * a) & (lane < 4 * a + 2), part, pack)
        pack = jnp.where((lane >= lo_lane) & (lane < lo_lane + 2), part, pack)
        pack = jnp.where(lane == 64 + 4 * a, lane_roll(east_v[8 * a:8 * a + 8], 4 * a + 65), pack)
    return pack


def column_unpack(from_east, from_west, with_velocity):
    cols = from_east.shape[-1]
    lane = lax.broadcasted_iota(jnp.int32, (8, cols), 1)
    both = jnp.where(lane % 4 < 2, from_east, from_west)
    return both, [lane_roll(both, -4 * a) for a in range(8)]


def sub_roll(value, shift):
    shift = shift % value.shape[0]
    return value if shift == 0 else pltpu.roll(value, shift, 0)


def write_rows(value, north_v, ypack_ref, f, k):
    rows, cols = value.shape
    ypack_ref[f, k, 0:2, :] = value[0:2]
    ypack_ref[f, k, 2:4, :] = value[rows - 2:rows]
    ypack_ref[f, k, 4:5, :] = north_v[rows - 1:rows]
    ypack_ref[f, k, 5:8, :] = jnp.zeros((3, cols), jnp.float32)


def edge_kernel(bl_ref, nt_ref, ns_ref, ue_ref, vn_ref, xpack_ref, ypack_ref):
    levels, rows, cols = nt_ref.shape

    def level(k, carry):
        m = (k < bl_ref[...]).astype(jnp.float32)
        for f, ref in enumerate((nt_ref, ns_ref)):
            value = ref[k] * m
            xpack_ref[f, k] = column_pack(value, ue_ref[k])
            write_rows(value, vn_ref[k], ypack_ref, f, k)
        return carry

    lax.fori_loop(0, levels, level, 0, unroll=True)


def step_kernel(mask_inputs, final, bl_ref, nt_ref, ns_ref, bt_ref, bs_ref, xe_ref, xw_ref, yh_ref,
                ue_ref, vn_ref, *rest):
    outs, fv = rest[:-1], rest[-1]
    levels, rows, cols = nt_ref.shape
    lane = lax.broadcasted_iota(jnp.int32, (rows, cols), 1)
    row = lax.broadcasted_iota(jnp.int32, (rows, cols), 0)
    now_refs, bef_refs = (nt_ref, ns_ref), (bt_ref, bs_ref)

    def mask(k):
        return (k < bl_ref[...]).astype(jnp.float32)

    def depth(k):
        return level_depth * (k.astype(jnp.float32) + 0.5)

    def load(ref, k, m):
        v = ref[k]
        return v * m if mask_inputs else v

    zero = jnp.zeros((rows, cols), jnp.float32)
    for f in range(2):
        fv[f, 0] = zero
        fv[f, levels] = zero

    def mixing(k, carry):
        m0, m1 = mask(k), mask(k + 1)
        e0 = density_at(load(nt_ref, k, m0), load(ns_ref, k, m0), depth(k))
        e1 = density_at(load(nt_ref, k + 1, m1), load(ns_ref, k + 1, m1), depth(k + 1))
        rates = (nu_base + nu_conv * jax.nn.sigmoid(-4.0 * (e1 - e0))) * m1
        for f in range(2):
            fv[f, k + 1] = rates * (load(bef_refs[f], k + 1, m1) - load(bef_refs[f], k, m0))
        return carry

    lax.fori_loop(0, levels - 1, mixing, 0)

    strips = rows // 8
    lane8 = lax.broadcasted_iota(jnp.int32, (8, cols), 1)
    sub8 = lax.broadcasted_iota(jnp.int32, (8, cols), 0)

    def split(value):
        return [value[8 * a:8 * a + 8] for a in range(strips)]

    def level(k, carry, fields=(0, 1)):
        m = split(mask(k))
        ue, vn = split(ue_ref[k]), split(vn_ref[k])
        south_v = jnp.where(sub8 == 7, jnp.broadcast_to(yh_ref[0, k][4:5], (8, cols)), 0.0)
        depth_k = depth(k)
        afters = [[None] * strips for _ in range(2)]
        for f in fields:
            q = split(load(now_refs[f], k, mask(k)))
            b = split(load(bef_refs[f], k, mask(k)))
            from_west = xw_ref[f, k]
            both, hs = column_unpack(xe_ref[f, k], from_west, False)
            own = jnp.zeros((8, cols), jnp.float32)
            for a in range(strips):
                own = jnp.where((lane8 >= 4 * a) & (lane8 < 4 * a + 2), lane_roll(q[a], 4 * a), own)
            west_face = face_flux(lane_roll(from_west, -64), lane_roll(both, 2), lane_roll(both, 1),
                                  own, lane_roll(own, -1))
            yh = yh_ref[f, k]
            below = jnp.where(sub8 == 6, jnp.broadcast_to(yh[0:1], (8, cols)),
                              jnp.broadcast_to(yh[1:2], (8, cols)))
            above = jnp.where(sub8 == 0, jnp.broadcast_to(yh[2:3], (8, cols)),
                              jnp.broadcast_to(yh[3:4], (8, cols)))
            qx = q + [above]
            north_prev = face_flux(south_v, sub_roll(below, 1), below, sub_roll(q[0], 7), sub_roll(q[0], 6))
            lo = below
            fv_lo, fv_hi = split(fv[f, k]), split(fv[f, k + 1])
            for a in range(strips):
                qa, ha, hi = q[a], hs[a], qx[a + 1]
                qm1 = lane_roll(jnp.where(lane8 == cols - 1, ha, qa), 1)
                qp1 = lane_roll(jnp.where(lane8 < 1, ha, qa), -1)
                qp2 = lane_roll(jnp.where(lane8 < 2, ha, qa), -2)
                east_f = face_flux(ue[a], qm1, qa, qp1, qp2)
                west_f = jnp.where(lane8 < 1, lane_roll(west_face, -4 * a), lane_roll(east_f, 1))
                qs1 = sub_roll(jnp.where(sub8 == 7, lo, qa), 1)
                qn1 = sub_roll(jnp.where(sub8 < 1, hi, qa), 7)
                qn2 = sub_roll(jnp.where(sub8 < 2, hi, qa), 6)
                north_f = face_flux(vn[a], qs1, qa, qn1, qn2)
                south_f = sub_roll(jnp.where(sub8 == 7, north_prev, north_f), 1)
                north_prev, lo = north_f, qa
                div_x = east_f - west_f
                div_y = north_f - south_f
                change = -(div_x + div_y)
                change = change + (fv_hi[a] - fv_lo[a])
                after = (b[a] + 2.0 * change) * m[a]
                afters[f][a] = after
                rs = pl.ds(8 * a, 8)
                if not final:
                    outs[f][k, rs, :] = qa + asselin_gamma * (b[a] - 2.0 * qa + after)
                    outs[2 + f][k, rs, :] = after
                else:
                    outs[f][k, rs, :] = after
            if not final:
                whole = jnp.concatenate(afters[f], 0)
                outs[4][f, k] = column_pack(whole, ue_ref[k])
                write_rows(whole, vn_ref[k], outs[5], f, k)
        if final:
            for a in range(strips):
                outs[2][k, pl.ds(8 * a, 8), :] = density_at(afters[0][a], afters[1][a], depth_k) * m[a]
        return carry

    if final:
        lax.fori_loop(0, levels, level, 0, unroll=2)
    else:
        for f in range(2):
            lax.fori_loop(0, levels, functools.partial(level, fields=(f,)), 0, unroll=3)


VMEM_SPEC = pl.BlockSpec(memory_space=pltpu.VMEM)


def pack_shapes(levels, rows, cols):
    return (jax.ShapeDtypeStruct((2, levels, 8, cols), jnp.float32),
            jax.ShapeDtypeStruct((2, levels, 8, cols), jnp.float32))


def edge_call(bl, nt, ns, ue, vn):
    levels, rows, cols = nt.shape
    return pl.pallas_call(
        edge_kernel,
        out_shape=pack_shapes(levels, rows, cols),
        in_specs=[VMEM_SPEC] * 5,
        out_specs=(VMEM_SPEC, VMEM_SPEC),
        cost_estimate=pl.CostEstimate(
            flops=2 * 2 * levels * 8 * rows * cols, transcendentals=0,
            bytes_accessed=4 * levels * rows * cols * 5),
    )(bl, nt, ns, ue, vn)


def step_call(mask_inputs, final, bl, nt, ns, bt, bs, xe, xw, yh, ue, vn):
    levels, rows, cols = nt.shape
    field = jax.ShapeDtypeStruct(nt.shape, jnp.float32)
    out_shape = (field,) * 3 if final else (field,) * 4 + pack_shapes(levels, rows, cols)
    return pl.pallas_call(
        functools.partial(step_kernel, mask_inputs, final),
        out_shape=out_shape,
        in_specs=[VMEM_SPEC] * 10,
        out_specs=tuple([VMEM_SPEC] * len(out_shape)),
        scratch_shapes=[pltpu.VMEM((2, levels + 1, rows, cols), jnp.float32)],
        compiler_params=pltpu.CompilerParams(vmem_limit_bytes=48 * 1024 * 1024),
        cost_estimate=pl.CostEstimate(
            flops=400 * 2 * levels * rows * cols, transcendentals=levels * rows * cols,
            bytes_accessed=4 * levels * rows * cols * (9 + len(out_shape))),
    )(bl, nt, ns, bt, bs, xe, xw, yh, ue, vn)


def exchange(xpack, ypack, at_fold):
    lon_count, lat_count = (lax.axis_size("lon"), lax.axis_size("lat"))
    from_east = lax.ppermute(xpack, "lon", [(i, (i - 1) % lon_count) for i in range(lon_count)])
    from_west = lax.ppermute(xpack, "lon", [(i, (i + 1) % lon_count) for i in range(lon_count)])
    from_north = lax.ppermute(ypack, "lat", [(i, i - 1) for i in range(1, lat_count)])
    from_south = lax.ppermute(ypack, "lat", [(i, i + 1) for i in range(lat_count - 1)])
    top = lat_count - 1
    fold_pairs = [(d * lat_count + top, (lon_count - 1 - d) * lat_count + top) for d in range(lon_count)]
    partner = lax.ppermute(ypack, ("lon", "lat"), fold_pairs)[:, :, 2:4]
    cols = ypack.shape[-1]
    flip = (jnp.arange(cols)[:, None] + jnp.arange(cols)[None, :] == cols - 1).astype(jnp.float32)
    flipped = jnp.einsum("fkrc,cd->fkrd", partner, flip, precision=lax.Precision.HIGHEST)
    mirror = jnp.concatenate([flipped[:, :, 1:2], flipped[:, :, 0:1]], 2)
    north = jnp.where(at_fold, mirror, from_north[:, :, 0:2])
    two, levels = xpack.shape[:2]
    halo_y = jnp.concatenate(
        [from_south[:, :, 2:4], north,
         from_south[:, :, 4:5], jnp.zeros((two, levels, 3, cols), jnp.float32)], 2)
    return from_east, from_west, halo_y


def on_device(
    temp_before, temp_now, salt_before, salt_now, east_velocity, north_velocity, bottom_level
):
    at_fold = lax.axis_index("lat") == lax.axis_size("lat") - 1
    xpack, ypack = edge_call(bottom_level, temp_now, salt_now, east_velocity, north_velocity)
    from_east, from_west, halo_y = exchange(xpack, ypack, at_fold)
    ft, fs, at, as_, xpack, ypack = step_call(
        True, False, bottom_level, temp_now, salt_now, temp_before, salt_before,
        from_east, from_west, halo_y, east_velocity, north_velocity)
    from_east, from_west, halo_y = exchange(xpack, ypack, at_fold)
    return step_call(False, True, bottom_level, at, as_, ft, fs, from_east, from_west, halo_y,
                     east_velocity, north_velocity)


def solution(mesh):
    return jax.shard_map(
        on_device,
        mesh=mesh,
        in_specs=(
            P(None, "lat", "lon"),
            P(None, "lat", "lon"),
            P(None, "lat", "lon"),
            P(None, "lat", "lon"),
            P(None, "lat", "lon"),
            P(None, "lat", "lon"),
            P("lat", "lon"),
        ),
        out_specs=(P(None, "lat", "lon"), P(None, "lat", "lon"), P(None, "lat", "lon")),
        check_vma=False,
    )
```

```python
import functools
import jax
import jax.numpy as jnp
from jax import lax
from jax.experimental import pallas as pl
from jax.experimental.pallas import tpu as pltpu
from jax.sharding import PartitionSpec as P

asselin_gamma = 0.1
nu_base = 0.05
nu_conv = 0.2
level_depth = 160.0
alpha_zero = 0.1655
beta_zero = 0.76554
lambda_one = 0.05952
lambda_two = 0.00054914
mu_one = 0.0001497
mu_two = 1.109e-05
nu_cross = 0.0024341


def density_at(temp, salt, depth):
    warm = -alpha_zero * (1.0 + 0.5 * lambda_one * temp + mu_one * depth) * temp
    salty = beta_zero * (1.0 - 0.5 * lambda_two * salt - mu_two * depth) * salt
    return warm + salty - nu_cross * temp * salt


def face_flux(u, q1, q2, q3, q4):
    flux = u * (7.0 * (q2 + q3) - (q1 + q4)) + jnp.abs(u) * ((q4 - q1) - 3.0 * (q3 - q2))
    return flux * (1.0 / 12.0)


def lane_roll(value, shift):
    shift = shift % value.shape[-1]
    return value if shift == 0 else pltpu.roll(value, shift, 1)


def column_pack(value, east_v):
    rows, cols = value.shape
    lane = lax.broadcasted_iota(jnp.int32, (8, cols), 1)
    pack = jnp.zeros((8, cols), jnp.float32)
    for a in range(rows // 8):
        part = lane_roll(value[8 * a:8 * a + 8], 4 * a)
        lo_lane = (4 * a - 2) % cols
        pack = jnp.where((lane >= 4 * a) & (lane < 4 * a + 2), part, pack)
        pack = jnp.where((lane >= lo_lane) & (lane < lo_lane + 2), part, pack)
        if east_v is not None:
            pack = jnp.where(lane == 64 + 4 * a, lane_roll(east_v[8 * a:8 * a + 8], 4 * a + 65), pack)
    return pack


def column_unpack(from_east, from_west, with_velocity):
    cols = from_east.shape[-1]
    lane = lax.broadcasted_iota(jnp.int32, (8, cols), 1)
    both = jnp.where(lane % 4 < 2, from_east, from_west)
    return both, [lane_roll(both, -4 * a) for a in range(8)]


def sub_roll(value, shift):
    shift = shift % value.shape[0]
    return value if shift == 0 else pltpu.roll(value, shift, 0)


def write_rows(value, north_v, ypack_ref, f, k):
    rows, cols = value.shape
    ypack_ref[f, k, 0:2, :] = value[0:2]
    ypack_ref[f, k, 2:4, :] = value[rows - 2:rows]
    ypack_ref[f, k, 4:5, :] = north_v[rows - 1:rows]
    ypack_ref[f, k, 5:8, :] = jnp.zeros((3, cols), jnp.float32)


def edge_kernel(bl_ref, nt_ref, ns_ref, ue_ref, vn_ref, xpack_ref, ypack_ref):
    levels, rows, cols = nt_ref.shape

    def level(k, carry):
        m = (k < bl_ref[...]).astype(jnp.float32)
        for f, ref in enumerate((nt_ref, ns_ref)):
            value = ref[k] * m
            xpack_ref[f, k] = column_pack(value, ue_ref[k] if f == 0 else None)
            write_rows(value, vn_ref[k], ypack_ref, f, k)
        return carry

    lax.fori_loop(0, levels, level, 0, unroll=True)


def step_kernel(mask_inputs, final, bl_ref, nt_ref, ns_ref, bt_ref, bs_ref, xe_ref, xw_ref, yh_ref,
                ue_ref, vn_ref, *rest):
    outs, fv = rest[:-1], rest[-1]
    levels, rows, cols = nt_ref.shape
    lane = lax.broadcasted_iota(jnp.int32, (rows, cols), 1)
    row = lax.broadcasted_iota(jnp.int32, (rows, cols), 0)
    now_refs, bef_refs = (nt_ref, ns_ref), (bt_ref, bs_ref)

    def mask(k):
        return (k < bl_ref[...]).astype(jnp.float32)

    def depth(k):
        return level_depth * (k.astype(jnp.float32) + 0.5)

    def load(ref, k, m):
        v = ref[k]
        return v * m if mask_inputs else v

    zero = jnp.zeros((rows, cols), jnp.float32)
    for f in range(2):
        fv[f, 0] = zero
        fv[f, levels] = zero

    def mixing(k, carry):
        m0, m1 = mask(k), mask(k + 1)
        e0 = density_at(load(nt_ref, k, m0), load(ns_ref, k, m0), depth(k))
        e1 = density_at(load(nt_ref, k + 1, m1), load(ns_ref, k + 1, m1), depth(k + 1))
        rates = (nu_base + nu_conv * jax.nn.sigmoid(-4.0 * (e1 - e0))) * m1
        for f in range(2):
            fv[f, k + 1] = rates * (load(bef_refs[f], k + 1, m1) - load(bef_refs[f], k, m0))
        return carry

    lax.fori_loop(0, levels - 1, mixing, 0)

    strips = rows // 8
    lane8 = lax.broadcasted_iota(jnp.int32, (8, cols), 1)
    sub8 = lax.broadcasted_iota(jnp.int32, (8, cols), 0)

    def split(value):
        return [value[8 * a:8 * a + 8] for a in range(strips)]

    def level(k, carry, fields=(0, 1)):
        m = split(mask(k))
        ue, vn = split(ue_ref[k]), split(vn_ref[k])
        south_v = jnp.where(sub8 == 7, jnp.broadcast_to(yh_ref[0, k][4:5], (8, cols)), 0.0)
        depth_k = depth(k)
        afters = [[None] * strips for _ in range(2)]
        for f in fields:
            q = split(load(now_refs[f], k, mask(k)))
            b = split(load(bef_refs[f], k, mask(k)))
            from_west = xw_ref[f, k]
            both, hs = column_unpack(xe_ref[f, k], from_west, False)
            own = jnp.zeros((8, cols), jnp.float32)
            for a in range(strips):
                own = jnp.where((lane8 >= 4 * a) & (lane8 < 4 * a + 2), lane_roll(q[a], 4 * a), own)
            west_face = face_flux(lane_roll(xw_ref[0, k], -64), lane_roll(both, 2), lane_roll(both, 1),
                                  own, lane_roll(own, -1))
            yh = yh_ref[f, k]
            below = jnp.where(sub8 == 6, jnp.broadcast_to(yh[0:1], (8, cols)),
                              jnp.broadcast_to(yh[1:2], (8, cols)))
            above = jnp.where(sub8 == 0, jnp.broadcast_to(yh[2:3], (8, cols)),
                              jnp.broadcast_to(yh[3:4], (8, cols)))
            qx = q + [above]
            north_prev = face_flux(south_v, sub_roll(below, 1), below, sub_roll(q[0], 7), sub_roll(q[0], 6))
            lo = below
            fv_lo, fv_hi = split(fv[f, k]), split(fv[f, k + 1])
            for a in range(strips):
                qa, ha, hi = q[a], hs[a], qx[a + 1]
                qm1 = lane_roll(jnp.where(lane8 == cols - 1, ha, qa), 1)
                qp1 = lane_roll(jnp.where(lane8 < 1, ha, qa), -1)
                qp2 = lane_roll(jnp.where(lane8 < 2, ha, qa), -2)
                east_f = face_flux(ue[a], qm1, qa, qp1, qp2)
                west_f = jnp.where(lane8 < 1, lane_roll(west_face, -4 * a), lane_roll(east_f, 1))
                qs1 = sub_roll(jnp.where(sub8 == 7, lo, qa), 1)
                qn1 = sub_roll(jnp.where(sub8 < 1, hi, qa), 7)
                qn2 = sub_roll(jnp.where(sub8 < 2, hi, qa), 6)
                north_f = face_flux(vn[a], qs1, qa, qn1, qn2)
                south_f = sub_roll(jnp.where(sub8 == 7, north_prev, north_f), 1)
                north_prev, lo = north_f, qa
                div_x = east_f - west_f
                div_y = north_f - south_f
                change = -(div_x + div_y)
                change = change + (fv_hi[a] - fv_lo[a])
                after = (b[a] + 2.0 * change) * m[a]
                afters[f][a] = after
                rs = pl.ds(8 * a, 8)
                if not final:
                    outs[f][k, rs, :] = qa + asselin_gamma * (b[a] - 2.0 * qa + after)
                    outs[2 + f][k, rs, :] = after
                else:
                    outs[f][k, rs, :] = after
            if not final:
                whole = jnp.concatenate(afters[f], 0)
                outs[4][f, k] = column_pack(whole, ue_ref[k] if f == 0 else None)
                write_rows(whole, vn_ref[k], outs[5], f, k)
        if final:
            for a in range(strips):
                outs[2][k, pl.ds(8 * a, 8), :] = density_at(afters[0][a], afters[1][a], depth_k) * m[a]
        return carry

    if final:
        lax.fori_loop(0, levels, level, 0, unroll=2)
    else:
        for f in range(2):
            lax.fori_loop(0, levels, functools.partial(level, fields=(f,)), 0, unroll=3)


VMEM_SPEC = pl.BlockSpec(memory_space=pltpu.VMEM)


def pack_shapes(levels, rows, cols):
    return (jax.ShapeDtypeStruct((2, levels, 8, cols), jnp.float32),
            jax.ShapeDtypeStruct((2, levels, 8, cols), jnp.float32))


def edge_call(bl, nt, ns, ue, vn):
    levels, rows, cols = nt.shape
    return pl.pallas_call(
        edge_kernel,
        out_shape=pack_shapes(levels, rows, cols),
        in_specs=[VMEM_SPEC] * 5,
        out_specs=(VMEM_SPEC, VMEM_SPEC),
        cost_estimate=pl.CostEstimate(
            flops=2 * 2 * levels * 8 * rows * cols, transcendentals=0,
            bytes_accessed=4 * levels * rows * cols * 5),
    )(bl, nt, ns, ue, vn)


def step_call(mask_inputs, final, bl, nt, ns, bt, bs, xe, xw, yh, ue, vn):
    levels, rows, cols = nt.shape
    field = jax.ShapeDtypeStruct(nt.shape, jnp.float32)
    out_shape = (field,) * 3 if final else (field,) * 4 + pack_shapes(levels, rows, cols)
    return pl.pallas_call(
        functools.partial(step_kernel, mask_inputs, final),
        out_shape=out_shape,
        in_specs=[VMEM_SPEC] * 10,
        out_specs=tuple([VMEM_SPEC] * len(out_shape)),
        scratch_shapes=[pltpu.VMEM((2, levels + 1, rows, cols), jnp.float32)],
        compiler_params=pltpu.CompilerParams(vmem_limit_bytes=48 * 1024 * 1024),
        cost_estimate=pl.CostEstimate(
            flops=400 * 2 * levels * rows * cols, transcendentals=levels * rows * cols,
            bytes_accessed=4 * levels * rows * cols * (9 + len(out_shape))),
    )(bl, nt, ns, bt, bs, xe, xw, yh, ue, vn)


def exchange(xpack, ypack, at_fold):
    lon_count, lat_count = (lax.axis_size("lon"), lax.axis_size("lat"))
    from_east = lax.ppermute(xpack, "lon", [(i, (i - 1) % lon_count) for i in range(lon_count)])
    from_west = lax.ppermute(xpack, "lon", [(i, (i + 1) % lon_count) for i in range(lon_count)])
    from_north = lax.ppermute(ypack, "lat", [(i, i - 1) for i in range(1, lat_count)])
    from_south = lax.ppermute(ypack, "lat", [(i, i + 1) for i in range(lat_count - 1)])
    top = lat_count - 1
    fold_pairs = [(d * lat_count + top, (lon_count - 1 - d) * lat_count + top) for d in range(lon_count)]
    partner = lax.ppermute(ypack, ("lon", "lat"), fold_pairs)[:, :, 2:4]
    cols = ypack.shape[-1]
    flip = (jnp.arange(cols)[:, None] + jnp.arange(cols)[None, :] == cols - 1).astype(jnp.float32)
    flipped = jnp.einsum("fkrc,cd->fkrd", partner, flip, precision=lax.Precision.HIGHEST)
    mirror = jnp.concatenate([flipped[:, :, 1:2], flipped[:, :, 0:1]], 2)
    north = jnp.where(at_fold, mirror, from_north[:, :, 0:2])
    two, levels = xpack.shape[:2]
    halo_y = jnp.concatenate(
        [from_south[:, :, 2:4], north,
         from_south[:, :, 4:5], jnp.zeros((two, levels, 3, cols), jnp.float32)], 2)
    return from_east, from_west, halo_y


def on_device(
    temp_before, temp_now, salt_before, salt_now, east_velocity, north_velocity, bottom_level
):
    at_fold = lax.axis_index("lat") == lax.axis_size("lat") - 1
    xpack, ypack = edge_call(bottom_level, temp_now, salt_now, east_velocity, north_velocity)
    from_east, from_west, halo_y = exchange(xpack, ypack, at_fold)
    ft, fs, at, as_, xpack, ypack = step_call(
        True, False, bottom_level, temp_now, salt_now, temp_before, salt_before,
        from_east, from_west, halo_y, east_velocity, north_velocity)
    from_east, from_west, halo_y = exchange(xpack, ypack, at_fold)
    return step_call(False, True, bottom_level, at, as_, ft, fs, from_east, from_west, halo_y,
                     east_velocity, north_velocity)


def solution(mesh):
    return jax.shard_map(
        on_device,
        mesh=mesh,
        in_specs=(
            P(None, "lat", "lon"),
            P(None, "lat", "lon"),
            P(None, "lat", "lon"),
            P(None, "lat", "lon"),
            P(None, "lat", "lon"),
            P(None, "lat", "lon"),
            P("lat", "lon"),
        ),
        out_specs=(P(None, "lat", "lon"), P(None, "lat", "lon"), P(None, "lat", "lon")),
        check_vma=False,
    )
```

```python
import functools
import jax
import jax.numpy as jnp
from jax import lax
from jax.experimental import pallas as pl
from jax.experimental.pallas import tpu as pltpu
from jax.sharding import PartitionSpec as P

asselin_gamma = 0.1
nu_base = 0.05
nu_conv = 0.2
level_depth = 160.0
alpha_zero = 0.1655
beta_zero = 0.76554
lambda_one = 0.05952
lambda_two = 0.00054914
mu_one = 0.0001497
mu_two = 1.109e-05
nu_cross = 0.0024341


def density_at(temp, salt, depth):
    warm = -alpha_zero * (1.0 + 0.5 * lambda_one * temp + mu_one * depth) * temp
    salty = beta_zero * (1.0 - 0.5 * lambda_two * salt - mu_two * depth) * salt
    return warm + salty - nu_cross * temp * salt


def face_flux(u, q1, q2, q3, q4):
    flux = u * (7.0 * (q2 + q3) - (q1 + q4)) + jnp.abs(u) * ((q4 - q1) - 3.0 * (q3 - q2))
    return flux * (1.0 / 12.0)


def lane_roll(value, shift):
    shift = shift % value.shape[-1]
    return value if shift == 0 else pltpu.roll(value, shift, 1)


def column_pack(value, east_v):
    rows, cols = value.shape
    lane = lax.broadcasted_iota(jnp.int32, (8, cols), 1)
    pack = jnp.zeros((8, cols), jnp.float32)
    for a in range(rows // 8):
        part = lane_roll(value[8 * a:8 * a + 8], 4 * a)
        lo_lane = (4 * a - 2) % cols
        pack = jnp.where((lane >= 4 * a) & (lane < 4 * a + 2), part, pack)
        pack = jnp.where((lane >= lo_lane) & (lane < lo_lane + 2), part, pack)
        if east_v is not None:
            pack = jnp.where(lane == 64 + 4 * a, lane_roll(east_v[8 * a:8 * a + 8], 4 * a + 65), pack)
    return pack


def column_unpack(from_east, from_west, with_velocity):
    cols = from_east.shape[-1]
    lane = lax.broadcasted_iota(jnp.int32, (8, cols), 1)
    both = jnp.where(lane % 4 < 2, from_east, from_west)
    return both, [lane_roll(both, -4 * a) for a in range(8)]


def sub_roll(value, shift):
    shift = shift % value.shape[0]
    return value if shift == 0 else pltpu.roll(value, shift, 0)


def write_rows(value, north_v, ypack_ref, f, k):
    rows, cols = value.shape
    ypack_ref[f, k, 0:2, :] = value[0:2]
    ypack_ref[f, k, 2:4, :] = value[rows - 2:rows]
    ypack_ref[f, k, 4:5, :] = north_v[rows - 1:rows]
    ypack_ref[f, k, 5:8, :] = jnp.zeros((3, cols), jnp.float32)


def edge_kernel(bl_ref, nt_ref, ns_ref, ue_ref, vn_ref, xpack_ref, ypack_ref):
    levels, rows, cols = nt_ref.shape

    def level(k, carry):
        m = (k < bl_ref[...]).astype(jnp.float32)
        for f, ref in enumerate((nt_ref, ns_ref)):
            value = ref[k] * m
            xpack_ref[f, k] = column_pack(value, ue_ref[k] if f == 0 else None)
            write_rows(value, vn_ref[k], ypack_ref, f, k)
        return carry

    lax.fori_loop(0, levels, level, 0, unroll=True)


def step_kernel(mask_inputs, final, bl_ref, nt_ref, ns_ref, bt_ref, bs_ref, xe_ref, xw_ref, yh_ref,
                ue_ref, vn_ref, *rest):
    outs, fv = rest[:-1], rest[-1]
    levels, rows, cols = nt_ref.shape
    lane = lax.broadcasted_iota(jnp.int32, (rows, cols), 1)
    row = lax.broadcasted_iota(jnp.int32, (rows, cols), 0)
    now_refs, bef_refs = (nt_ref, ns_ref), (bt_ref, bs_ref)

    def mask(k):
        return (k < bl_ref[...]).astype(jnp.float32)

    def depth(k):
        return level_depth * (k.astype(jnp.float32) + 0.5)

    def load(ref, k, m):
        v = ref[k]
        return v * m if mask_inputs else v

    zero = jnp.zeros((rows, cols), jnp.float32)
    for f in range(2):
        fv[f, 0] = zero
        fv[f, levels] = zero

    def mixing(k, carry):
        m0, m1 = mask(k), mask(k + 1)
        e0 = density_at(load(nt_ref, k, m0), load(ns_ref, k, m0), depth(k))
        e1 = density_at(load(nt_ref, k + 1, m1), load(ns_ref, k + 1, m1), depth(k + 1))
        rates = (nu_base + nu_conv * jax.nn.sigmoid(-4.0 * (e1 - e0))) * m1
        for f in range(2):
            fv[f, k + 1] = rates * (load(bef_refs[f], k + 1, m1) - load(bef_refs[f], k, m0))
        return carry

    lax.fori_loop(0, levels - 1, mixing, 0, unroll=2)

    strips = rows // 8
    lane8 = lax.broadcasted_iota(jnp.int32, (8, cols), 1)
    sub8 = lax.broadcasted_iota(jnp.int32, (8, cols), 0)

    def split(value):
        return [value[8 * a:8 * a + 8] for a in range(strips)]

    def level(k, carry, fields=(0, 1)):
        m = split(mask(k))
        ue, vn = split(ue_ref[k]), split(vn_ref[k])
        south_v = jnp.where(sub8 == 7, jnp.broadcast_to(yh_ref[0, k][4:5], (8, cols)), 0.0)
        depth_k = depth(k)
        afters = [[None] * strips for _ in range(2)]
        for f in fields:
            q = split(load(now_refs[f], k, mask(k)))
            b = split(load(bef_refs[f], k, mask(k)))
            from_west = xw_ref[f, k]
            both, hs = column_unpack(xe_ref[f, k], from_west, False)
            own = jnp.zeros((8, cols), jnp.float32)
            for a in range(strips):
                own = jnp.where((lane8 >= 4 * a) & (lane8 < 4 * a + 2), lane_roll(q[a], 4 * a), own)
            west_face = face_flux(lane_roll(xw_ref[0, k], -64), lane_roll(both, 2), lane_roll(both, 1),
                                  own, lane_roll(own, -1))
            yh = yh_ref[f, k]
            below = jnp.where(sub8 == 6, jnp.broadcast_to(yh[0:1], (8, cols)),
                              jnp.broadcast_to(yh[1:2], (8, cols)))
            above = jnp.where(sub8 == 0, jnp.broadcast_to(yh[2:3], (8, cols)),
                              jnp.broadcast_to(yh[3:4], (8, cols)))
            qx = q + [above]
            north_prev = face_flux(south_v, sub_roll(below, 1), below, sub_roll(q[0], 7), sub_roll(q[0], 6))
            lo = below
            fv_lo, fv_hi = split(fv[f, k]), split(fv[f, k + 1])
            for a in range(strips):
                qa, ha, hi = q[a], hs[a], qx[a + 1]
                qm1 = lane_roll(jnp.where(lane8 == cols - 1, ha, qa), 1)
                qp1 = lane_roll(jnp.where(lane8 < 1, ha, qa), -1)
                qp2 = lane_roll(jnp.where(lane8 < 2, ha, qa), -2)
                east_f = face_flux(ue[a], qm1, qa, qp1, qp2)
                west_f = jnp.where(lane8 < 1, lane_roll(west_face, -4 * a), lane_roll(east_f, 1))
                qs1 = sub_roll(jnp.where(sub8 == 7, lo, qa), 1)
                qn1 = sub_roll(jnp.where(sub8 < 1, hi, qa), 7)
                qn2 = sub_roll(jnp.where(sub8 < 2, hi, qa), 6)
                north_f = face_flux(vn[a], qs1, qa, qn1, qn2)
                south_f = sub_roll(jnp.where(sub8 == 7, north_prev, north_f), 1)
                north_prev, lo = north_f, qa
                div_x = east_f - west_f
                div_y = north_f - south_f
                change = -(div_x + div_y)
                change = change + (fv_hi[a] - fv_lo[a])
                after = (b[a] + 2.0 * change) * m[a]
                afters[f][a] = after
                rs = pl.ds(8 * a, 8)
                if not final:
                    outs[f][k, rs, :] = qa + asselin_gamma * (b[a] - 2.0 * qa + after)
                    outs[2 + f][k, rs, :] = after
                else:
                    outs[f][k, rs, :] = after
            if not final:
                whole = jnp.concatenate(afters[f], 0)
                outs[4][f, k] = column_pack(whole, ue_ref[k] if f == 0 else None)
                write_rows(whole, vn_ref[k], outs[5], f, k)
        if final:
            for a in range(strips):
                outs[2][k, pl.ds(8 * a, 8), :] = density_at(afters[0][a], afters[1][a], depth_k) * m[a]
        return carry

    if final:
        lax.fori_loop(0, levels, level, 0, unroll=2)
    else:
        for f in range(2):
            lax.fori_loop(0, levels, functools.partial(level, fields=(f,)), 0, unroll=3)


VMEM_SPEC = pl.BlockSpec(memory_space=pltpu.VMEM)


def pack_shapes(levels, rows, cols):
    return (jax.ShapeDtypeStruct((2, levels, 8, cols), jnp.float32),
            jax.ShapeDtypeStruct((2, levels, 8, cols), jnp.float32))


def edge_call(bl, nt, ns, ue, vn):
    levels, rows, cols = nt.shape
    return pl.pallas_call(
        edge_kernel,
        out_shape=pack_shapes(levels, rows, cols),
        in_specs=[VMEM_SPEC] * 5,
        out_specs=(VMEM_SPEC, VMEM_SPEC),
        cost_estimate=pl.CostEstimate(
            flops=2 * 2 * levels * 8 * rows * cols, transcendentals=0,
            bytes_accessed=4 * levels * rows * cols * 5),
    )(bl, nt, ns, ue, vn)


def step_call(mask_inputs, final, bl, nt, ns, bt, bs, xe, xw, yh, ue, vn):
    levels, rows, cols = nt.shape
    field = jax.ShapeDtypeStruct(nt.shape, jnp.float32)
    out_shape = (field,) * 3 if final else (field,) * 4 + pack_shapes(levels, rows, cols)
    return pl.pallas_call(
        functools.partial(step_kernel, mask_inputs, final),
        out_shape=out_shape,
        in_specs=[VMEM_SPEC] * 10,
        out_specs=tuple([VMEM_SPEC] * len(out_shape)),
        scratch_shapes=[pltpu.VMEM((2, levels + 1, rows, cols), jnp.float32)],
        compiler_params=pltpu.CompilerParams(vmem_limit_bytes=48 * 1024 * 1024),
        cost_estimate=pl.CostEstimate(
            flops=400 * 2 * levels * rows * cols, transcendentals=levels * rows * cols,
            bytes_accessed=4 * levels * rows * cols * (9 + len(out_shape))),
    )(bl, nt, ns, bt, bs, xe, xw, yh, ue, vn)


def exchange(xpack, ypack, at_fold):
    lon_count, lat_count = (lax.axis_size("lon"), lax.axis_size("lat"))
    from_east = lax.ppermute(xpack, "lon", [(i, (i - 1) % lon_count) for i in range(lon_count)])
    from_west = lax.ppermute(xpack, "lon", [(i, (i + 1) % lon_count) for i in range(lon_count)])
    from_north = lax.ppermute(ypack, "lat", [(i, i - 1) for i in range(1, lat_count)])
    from_south = lax.ppermute(ypack, "lat", [(i, i + 1) for i in range(lat_count - 1)])
    top = lat_count - 1
    fold_pairs = [(d * lat_count + top, (lon_count - 1 - d) * lat_count + top) for d in range(lon_count)]
    partner = lax.ppermute(ypack, ("lon", "lat"), fold_pairs)[:, :, 2:4]
    cols = ypack.shape[-1]
    flip = (jnp.arange(cols)[:, None] + jnp.arange(cols)[None, :] == cols - 1).astype(jnp.float32)
    flipped = jnp.einsum("fkrc,cd->fkrd", partner, flip, precision=lax.Precision.HIGHEST)
    mirror = jnp.concatenate([flipped[:, :, 1:2], flipped[:, :, 0:1]], 2)
    north = jnp.where(at_fold, mirror, from_north[:, :, 0:2])
    two, levels = xpack.shape[:2]
    halo_y = jnp.concatenate(
        [from_south[:, :, 2:4], north,
         from_south[:, :, 4:5], jnp.zeros((two, levels, 3, cols), jnp.float32)], 2)
    return from_east, from_west, halo_y


def on_device(
    temp_before, temp_now, salt_before, salt_now, east_velocity, north_velocity, bottom_level
):
    at_fold = lax.axis_index("lat") == lax.axis_size("lat") - 1
    xpack, ypack = edge_call(bottom_level, temp_now, salt_now, east_velocity, north_velocity)
    from_east, from_west, halo_y = exchange(xpack, ypack, at_fold)
    ft, fs, at, as_, xpack, ypack = step_call(
        True, False, bottom_level, temp_now, salt_now, temp_before, salt_before,
        from_east, from_west, halo_y, east_velocity, north_velocity)
    from_east, from_west, halo_y = exchange(xpack, ypack, at_fold)
    return step_call(False, True, bottom_level, at, as_, ft, fs, from_east, from_west, halo_y,
                     east_velocity, north_velocity)


def solution(mesh):
    return jax.shard_map(
        on_device,
        mesh=mesh,
        in_specs=(
            P(None, "lat", "lon"),
            P(None, "lat", "lon"),
            P(None, "lat", "lon"),
            P(None, "lat", "lon"),
            P(None, "lat", "lon"),
            P(None, "lat", "lon"),
            P("lat", "lon"),
        ),
        out_specs=(P(None, "lat", "lon"), P(None, "lat", "lon"), P(None, "lat", "lon")),
        check_vma=False,
    )
```

```python
import functools
import jax
import jax.numpy as jnp
from jax import lax
from jax.experimental import pallas as pl
from jax.experimental.pallas import tpu as pltpu
from jax.sharding import PartitionSpec as P

asselin_gamma = 0.1
nu_base = 0.05
nu_conv = 0.2
level_depth = 160.0
alpha_zero = 0.1655
beta_zero = 0.76554
lambda_one = 0.05952
lambda_two = 0.00054914
mu_one = 0.0001497
mu_two = 1.109e-05
nu_cross = 0.0024341


def density_at(temp, salt, depth):
    warm = -alpha_zero * (1.0 + 0.5 * lambda_one * temp + mu_one * depth) * temp
    salty = beta_zero * (1.0 - 0.5 * lambda_two * salt - mu_two * depth) * salt
    return warm + salty - nu_cross * temp * salt


def face_flux(u, q1, q2, q3, q4):
    flux = u * (7.0 * (q2 + q3) - (q1 + q4)) + jnp.abs(u) * ((q4 - q1) - 3.0 * (q3 - q2))
    return flux * (1.0 / 12.0)


def lane_roll(value, shift):
    shift = shift % value.shape[-1]
    return value if shift == 0 else pltpu.roll(value, shift, 1)


def column_pack(value, east_v):
    rows, cols = value.shape
    lane = lax.broadcasted_iota(jnp.int32, (8, cols), 1)
    pack = jnp.zeros((8, cols), jnp.float32)
    for a in range(rows // 8):
        part = lane_roll(value[8 * a:8 * a + 8], 4 * a)
        lo_lane = (4 * a - 2) % cols
        pack = jnp.where((lane >= 4 * a) & (lane < 4 * a + 2), part, pack)
        pack = jnp.where((lane >= lo_lane) & (lane < lo_lane + 2), part, pack)
        if east_v is not None:
            pack = jnp.where(lane == 64 + 4 * a, lane_roll(east_v[8 * a:8 * a + 8], 4 * a + 65), pack)
    return pack


def column_unpack(from_east, from_west, with_velocity):
    cols = from_east.shape[-1]
    lane = lax.broadcasted_iota(jnp.int32, (8, cols), 1)
    both = jnp.where(lane % 4 < 2, from_east, from_west)
    return both, [lane_roll(both, -4 * a) for a in range(8)]


def sub_roll(value, shift):
    shift = shift % value.shape[0]
    return value if shift == 0 else pltpu.roll(value, shift, 0)


def write_rows(value, north_v, ypack_ref, f, k):
    rows, cols = value.shape
    ypack_ref[f, k, 0:2, :] = value[0:2]
    ypack_ref[f, k, 2:4, :] = value[rows - 2:rows]
    if f == 0:
        ypack_ref[f, k, 4:5, :] = north_v[rows - 1:rows]
        ypack_ref[f, k, 5:8, :] = jnp.zeros((3, cols), jnp.float32)
    else:
        ypack_ref[f, k, 4:8, :] = jnp.zeros((4, cols), jnp.float32)


def edge_kernel(bl_ref, nt_ref, ns_ref, ue_ref, vn_ref, xpack_ref, ypack_ref):
    levels, rows, cols = nt_ref.shape

    def level(k, carry):
        m = (k < bl_ref[...]).astype(jnp.float32)
        for f, ref in enumerate((nt_ref, ns_ref)):
            value = ref[k] * m
            xpack_ref[f, k] = column_pack(value, ue_ref[k] if f == 0 else None)
            write_rows(value, vn_ref[k], ypack_ref, f, k)
        return carry

    lax.fori_loop(0, levels, level, 0, unroll=True)


def step_kernel(mask_inputs, final, bl_ref, nt_ref, ns_ref, bt_ref, bs_ref, xe_ref, xw_ref, yh_ref,
                ue_ref, vn_ref, *rest):
    outs, fv = rest[:-1], rest[-1]
    levels, rows, cols = nt_ref.shape
    lane = lax.broadcasted_iota(jnp.int32, (rows, cols), 1)
    row = lax.broadcasted_iota(jnp.int32, (rows, cols), 0)
    now_refs, bef_refs = (nt_ref, ns_ref), (bt_ref, bs_ref)

    def mask(k):
        return (k < bl_ref[...]).astype(jnp.float32)

    def depth(k):
        return level_depth * (k.astype(jnp.float32) + 0.5)

    def load(ref, k, m):
        v = ref[k]
        return v * m if mask_inputs else v

    zero = jnp.zeros((rows, cols), jnp.float32)
    for f in range(2):
        fv[f, 0] = zero
        fv[f, levels] = zero

    def mixing(k, carry):
        m0, m1 = mask(k), mask(k + 1)
        e0 = density_at(load(nt_ref, k, m0), load(ns_ref, k, m0), depth(k))
        e1 = density_at(load(nt_ref, k + 1, m1), load(ns_ref, k + 1, m1), depth(k + 1))
        rates = (nu_base + nu_conv * jax.nn.sigmoid(-4.0 * (e1 - e0))) * m1
        for f in range(2):
            fv[f, k + 1] = rates * (load(bef_refs[f], k + 1, m1) - load(bef_refs[f], k, m0))
        return carry

    lax.fori_loop(0, levels - 1, mixing, 0, unroll=2)

    strips = rows // 8
    lane8 = lax.broadcasted_iota(jnp.int32, (8, cols), 1)
    sub8 = lax.broadcasted_iota(jnp.int32, (8, cols), 0)

    def split(value):
        return [value[8 * a:8 * a + 8] for a in range(strips)]

    def level(k, carry, fields=(0, 1)):
        m = split(mask(k))
        ue, vn = split(ue_ref[k]), split(vn_ref[k])
        south_v = jnp.where(sub8 == 7, jnp.broadcast_to(yh_ref[0, k][4:5], (8, cols)), 0.0)
        depth_k = depth(k)
        afters = [[None] * strips for _ in range(2)]
        for f in fields:
            q = split(load(now_refs[f], k, mask(k)))
            b = split(load(bef_refs[f], k, mask(k)))
            from_west = xw_ref[f, k]
            both, hs = column_unpack(xe_ref[f, k], from_west, False)
            own = jnp.zeros((8, cols), jnp.float32)
            for a in range(strips):
                own = jnp.where((lane8 >= 4 * a) & (lane8 < 4 * a + 2), lane_roll(q[a], 4 * a), own)
            west_face = face_flux(lane_roll(xw_ref[0, k], -64), lane_roll(both, 2), lane_roll(both, 1),
                                  own, lane_roll(own, -1))
            yh = yh_ref[f, k]
            below = jnp.where(sub8 == 6, jnp.broadcast_to(yh[0:1], (8, cols)),
                              jnp.broadcast_to(yh[1:2], (8, cols)))
            above = jnp.where(sub8 == 0, jnp.broadcast_to(yh[2:3], (8, cols)),
                              jnp.broadcast_to(yh[3:4], (8, cols)))
            qx = q + [above]
            north_prev = face_flux(south_v, sub_roll(below, 1), below, sub_roll(q[0], 7), sub_roll(q[0], 6))
            lo = below
            fv_lo, fv_hi = split(fv[f, k]), split(fv[f, k + 1])
            for a in range(strips):
                qa, ha, hi = q[a], hs[a], qx[a + 1]
                qm1 = lane_roll(jnp.where(lane8 == cols - 1, ha, qa), 1)
                qp1 = lane_roll(jnp.where(lane8 < 1, ha, qa), -1)
                qp2 = lane_roll(jnp.where(lane8 < 2, ha, qa), -2)
                east_f = face_flux(ue[a], qm1, qa, qp1, qp2)
                west_f = jnp.where(lane8 < 1, lane_roll(west_face, -4 * a), lane_roll(east_f, 1))
                qs1 = sub_roll(jnp.where(sub8 == 7, lo, qa), 1)
                qn1 = sub_roll(jnp.where(sub8 < 1, hi, qa), 7)
                qn2 = sub_roll(jnp.where(sub8 < 2, hi, qa), 6)
                north_f = face_flux(vn[a], qs1, qa, qn1, qn2)
                south_f = sub_roll(jnp.where(sub8 == 7, north_prev, north_f), 1)
                north_prev, lo = north_f, qa
                div_x = east_f - west_f
                div_y = north_f - south_f
                change = -(div_x + div_y)
                change = change + (fv_hi[a] - fv_lo[a])
                after = (b[a] + 2.0 * change) * m[a]
                afters[f][a] = after
                rs = pl.ds(8 * a, 8)
                if not final:
                    outs[f][k, rs, :] = qa + asselin_gamma * (b[a] - 2.0 * qa + after)
                    outs[2 + f][k, rs, :] = after
                else:
                    outs[f][k, rs, :] = after
            if not final:
                whole = jnp.concatenate(afters[f], 0)
                outs[4][f, k] = column_pack(whole, ue_ref[k] if f == 0 else None)
                write_rows(whole, vn_ref[k], outs[5], f, k)
        if final:
            for a in range(strips):
                outs[2][k, pl.ds(8 * a, 8), :] = density_at(afters[0][a], afters[1][a], depth_k) * m[a]
        return carry

    if final:
        lax.fori_loop(0, levels, level, 0, unroll=2)
    else:
        for f in range(2):
            lax.fori_loop(0, levels, functools.partial(level, fields=(f,)), 0, unroll=3)


VMEM_SPEC = pl.BlockSpec(memory_space=pltpu.VMEM)


def pack_shapes(levels, rows, cols):
    return (jax.ShapeDtypeStruct((2, levels, 8, cols), jnp.float32),
            jax.ShapeDtypeStruct((2, levels, 8, cols), jnp.float32))


def edge_call(bl, nt, ns, ue, vn):
    levels, rows, cols = nt.shape
    return pl.pallas_call(
        edge_kernel,
        out_shape=pack_shapes(levels, rows, cols),
        in_specs=[VMEM_SPEC] * 5,
        out_specs=(VMEM_SPEC, VMEM_SPEC),
        cost_estimate=pl.CostEstimate(
            flops=2 * 2 * levels * 8 * rows * cols, transcendentals=0,
            bytes_accessed=4 * levels * rows * cols * 5),
    )(bl, nt, ns, ue, vn)


def step_call(mask_inputs, final, bl, nt, ns, bt, bs, xe, xw, yh, ue, vn):
    levels, rows, cols = nt.shape
    field = jax.ShapeDtypeStruct(nt.shape, jnp.float32)
    out_shape = (field,) * 3 if final else (field,) * 4 + pack_shapes(levels, rows, cols)
    return pl.pallas_call(
        functools.partial(step_kernel, mask_inputs, final),
        out_shape=out_shape,
        in_specs=[VMEM_SPEC] * 10,
        out_specs=tuple([VMEM_SPEC] * len(out_shape)),
        scratch_shapes=[pltpu.VMEM((2, levels + 1, rows, cols), jnp.float32)],
        compiler_params=pltpu.CompilerParams(vmem_limit_bytes=48 * 1024 * 1024),
        cost_estimate=pl.CostEstimate(
            flops=400 * 2 * levels * rows * cols, transcendentals=levels * rows * cols,
            bytes_accessed=4 * levels * rows * cols * (9 + len(out_shape))),
    )(bl, nt, ns, bt, bs, xe, xw, yh, ue, vn)


def exchange(xpack, ypack, at_fold):
    lon_count, lat_count = (lax.axis_size("lon"), lax.axis_size("lat"))
    from_east = lax.ppermute(xpack, "lon", [(i, (i - 1) % lon_count) for i in range(lon_count)])
    from_west = lax.ppermute(xpack, "lon", [(i, (i + 1) % lon_count) for i in range(lon_count)])
    from_north = lax.ppermute(ypack, "lat", [(i, i - 1) for i in range(1, lat_count)])
    from_south = lax.ppermute(ypack, "lat", [(i, i + 1) for i in range(lat_count - 1)])
    top = lat_count - 1
    fold_pairs = [(d * lat_count + top, (lon_count - 1 - d) * lat_count + top) for d in range(lon_count)]
    partner = lax.ppermute(ypack, ("lon", "lat"), fold_pairs)[:, :, 2:4]
    cols = ypack.shape[-1]
    flip = (jnp.arange(cols)[:, None] + jnp.arange(cols)[None, :] == cols - 1).astype(jnp.float32)
    flipped = jnp.einsum("fkrc,cd->fkrd", partner, flip, precision=lax.Precision.HIGHEST)
    mirror = jnp.concatenate([flipped[:, :, 1:2], flipped[:, :, 0:1]], 2)
    north = jnp.where(at_fold, mirror, from_north[:, :, 0:2])
    two, levels = xpack.shape[:2]
    halo_y = jnp.concatenate(
        [from_south[:, :, 2:4], north,
         from_south[:, :, 4:5], jnp.zeros((two, levels, 3, cols), jnp.float32)], 2)
    return from_east, from_west, halo_y


def on_device(
    temp_before, temp_now, salt_before, salt_now, east_velocity, north_velocity, bottom_level
):
    at_fold = lax.axis_index("lat") == lax.axis_size("lat") - 1
    xpack, ypack = edge_call(bottom_level, temp_now, salt_now, east_velocity, north_velocity)
    from_east, from_west, halo_y = exchange(xpack, ypack, at_fold)
    ft, fs, at, as_, xpack, ypack = step_call(
        True, False, bottom_level, temp_now, salt_now, temp_before, salt_before,
        from_east, from_west, halo_y, east_velocity, north_velocity)
    from_east, from_west, halo_y = exchange(xpack, ypack, at_fold)
    return step_call(False, True, bottom_level, at, as_, ft, fs, from_east, from_west, halo_y,
                     east_velocity, north_velocity)


def solution(mesh):
    return jax.shard_map(
        on_device,
        mesh=mesh,
        in_specs=(
            P(None, "lat", "lon"),
            P(None, "lat", "lon"),
            P(None, "lat", "lon"),
            P(None, "lat", "lon"),
            P(None, "lat", "lon"),
            P(None, "lat", "lon"),
            P("lat", "lon"),
        ),
        out_specs=(P(None, "lat", "lon"), P(None, "lat", "lon"), P(None, "lat", "lon")),
        check_vma=False,
    )
```

```python
import functools
import jax
import jax.numpy as jnp
from jax import lax
from jax.experimental import pallas as pl
from jax.experimental.pallas import tpu as pltpu
from jax.sharding import PartitionSpec as P

asselin_gamma = 0.1
nu_base = 0.05
nu_conv = 0.2
level_depth = 160.0
alpha_zero = 0.1655
beta_zero = 0.76554
lambda_one = 0.05952
lambda_two = 0.00054914
mu_one = 0.0001497
mu_two = 1.109e-05
nu_cross = 0.0024341


def density_at(temp, salt, depth):
    warm = -alpha_zero * (1.0 + 0.5 * lambda_one * temp + mu_one * depth) * temp
    salty = beta_zero * (1.0 - 0.5 * lambda_two * salt - mu_two * depth) * salt
    return warm + salty - nu_cross * temp * salt


def face_flux(u, q1, q2, q3, q4):
    flux = u * (7.0 * (q2 + q3) - (q1 + q4)) + jnp.abs(u) * ((q4 - q1) - 3.0 * (q3 - q2))
    return flux * (1.0 / 12.0)


def lane_roll(value, shift):
    shift = shift % value.shape[-1]
    return value if shift == 0 else pltpu.roll(value, shift, 1)


def column_pack(value, east_v):
    rows, cols = value.shape
    lane = lax.broadcasted_iota(jnp.int32, (8, cols), 1)
    pack = jnp.zeros((8, cols), jnp.float32)
    for a in range(rows // 8):
        part = lane_roll(value[8 * a:8 * a + 8], 4 * a)
        lo_lane = (4 * a - 2) % cols
        pack = jnp.where((lane >= 4 * a) & (lane < 4 * a + 2), part, pack)
        pack = jnp.where((lane >= lo_lane) & (lane < lo_lane + 2), part, pack)
        if east_v is not None:
            pack = jnp.where(lane == 64 + 4 * a, lane_roll(east_v[8 * a:8 * a + 8], 4 * a + 65), pack)
    return pack


def column_unpack(from_east, from_west, with_velocity):
    cols = from_east.shape[-1]
    lane = lax.broadcasted_iota(jnp.int32, (8, cols), 1)
    both = jnp.where(lane % 4 < 2, from_east, from_west)
    return both, [lane_roll(both, -4 * a) for a in range(8)]


def sub_roll(value, shift):
    shift = shift % value.shape[0]
    return value if shift == 0 else pltpu.roll(value, shift, 0)


def write_rows(value, north_v, ypack_ref, f, k):
    rows, cols = value.shape
    ypack_ref[f, k, 0:2, :] = value[0:2]
    ypack_ref[f, k, 2:4, :] = value[rows - 2:rows]
    if f == 0:
        ypack_ref[f, k, 4:5, :] = north_v[rows - 1:rows]


def edge_kernel(bl_ref, nt_ref, ns_ref, ue_ref, vn_ref, xpack_ref, ypack_ref):
    levels, rows, cols = nt_ref.shape

    def level(k, carry):
        m = (k < bl_ref[...]).astype(jnp.float32)
        for f, ref in enumerate((nt_ref, ns_ref)):
            value = ref[k] * m
            xpack_ref[f, k] = column_pack(value, ue_ref[k] if f == 0 else None)
            write_rows(value, vn_ref[k], ypack_ref, f, k)
        return carry

    lax.fori_loop(0, levels, level, 0, unroll=True)


def step_kernel(mask_inputs, final, bl_ref, nt_ref, ns_ref, bt_ref, bs_ref, xe_ref, xw_ref, yh_ref,
                ue_ref, vn_ref, *rest):
    outs, fv = rest[:-1], rest[-1]
    levels, rows, cols = nt_ref.shape
    lane = lax.broadcasted_iota(jnp.int32, (rows, cols), 1)
    row = lax.broadcasted_iota(jnp.int32, (rows, cols), 0)
    now_refs, bef_refs = (nt_ref, ns_ref), (bt_ref, bs_ref)

    def mask(k):
        return (k < bl_ref[...]).astype(jnp.float32)

    def depth(k):
        return level_depth * (k.astype(jnp.float32) + 0.5)

    def load(ref, k, m):
        v = ref[k]
        return v * m if mask_inputs else v

    zero = jnp.zeros((rows, cols), jnp.float32)
    for f in range(2):
        fv[f, 0] = zero
        fv[f, levels] = zero

    def mixing(k, carry):
        m0, m1 = mask(k), mask(k + 1)
        e0 = density_at(load(nt_ref, k, m0), load(ns_ref, k, m0), depth(k))
        e1 = density_at(load(nt_ref, k + 1, m1), load(ns_ref, k + 1, m1), depth(k + 1))
        rates = (nu_base + nu_conv * jax.nn.sigmoid(-4.0 * (e1 - e0))) * m1
        for f in range(2):
            fv[f, k + 1] = rates * (load(bef_refs[f], k + 1, m1) - load(bef_refs[f], k, m0))
        return carry

    lax.fori_loop(0, levels - 1, mixing, 0, unroll=2)

    strips = rows // 8
    lane8 = lax.broadcasted_iota(jnp.int32, (8, cols), 1)
    sub8 = lax.broadcasted_iota(jnp.int32, (8, cols), 0)

    def split(value):
        return [value[8 * a:8 * a + 8] for a in range(strips)]

    def level(k, carry, fields=(0, 1)):
        m = split(mask(k))
        ue, vn = split(ue_ref[k]), split(vn_ref[k])
        south_v = jnp.where(sub8 == 7, jnp.broadcast_to(yh_ref[0, k][4:5], (8, cols)), 0.0)
        depth_k = depth(k)
        afters = [[None] * strips for _ in range(2)]
        for f in fields:
            q = split(load(now_refs[f], k, mask(k)))
            b = split(load(bef_refs[f], k, mask(k)))
            from_west = xw_ref[f, k]
            both, hs = column_unpack(xe_ref[f, k], from_west, False)
            own = jnp.zeros((8, cols), jnp.float32)
            for a in range(strips):
                own = jnp.where((lane8 >= 4 * a) & (lane8 < 4 * a + 2), lane_roll(q[a], 4 * a), own)
            west_face = face_flux(lane_roll(xw_ref[0, k], -64), lane_roll(both, 2), lane_roll(both, 1),
                                  own, lane_roll(own, -1))
            yh = yh_ref[f, k]
            below = jnp.where(sub8 == 6, jnp.broadcast_to(yh[0:1], (8, cols)),
                              jnp.broadcast_to(yh[1:2], (8, cols)))
            above = jnp.where(sub8 == 0, jnp.broadcast_to(yh[2:3], (8, cols)),
                              jnp.broadcast_to(yh[3:4], (8, cols)))
            qx = q + [above]
            north_prev = face_flux(south_v, sub_roll(below, 1), below, sub_roll(q[0], 7), sub_roll(q[0], 6))
            lo = below
            fv_lo, fv_hi = split(fv[f, k]), split(fv[f, k + 1])
            for a in range(strips):
                qa, ha, hi = q[a], hs[a], qx[a + 1]
                qm1 = lane_roll(jnp.where(lane8 == cols - 1, ha, qa), 1)
                qp1 = lane_roll(jnp.where(lane8 < 1, ha, qa), -1)
                qp2 = lane_roll(jnp.where(lane8 < 2, ha, qa), -2)
                east_f = face_flux(ue[a], qm1, qa, qp1, qp2)
                west_f = jnp.where(lane8 < 1, lane_roll(west_face, -4 * a), lane_roll(east_f, 1))
                qs1 = sub_roll(jnp.where(sub8 == 7, lo, qa), 1)
                qn1 = sub_roll(jnp.where(sub8 < 1, hi, qa), 7)
                qn2 = sub_roll(jnp.where(sub8 < 2, hi, qa), 6)
                north_f = face_flux(vn[a], qs1, qa, qn1, qn2)
                south_f = sub_roll(jnp.where(sub8 == 7, north_prev, north_f), 1)
                north_prev, lo = north_f, qa
                div_x = east_f - west_f
                div_y = north_f - south_f
                change = -(div_x + div_y)
                change = change + (fv_hi[a] - fv_lo[a])
                after = (b[a] + 2.0 * change) * m[a]
                afters[f][a] = after
                rs = pl.ds(8 * a, 8)
                if not final:
                    outs[f][k, rs, :] = qa + asselin_gamma * (b[a] - 2.0 * qa + after)
                    outs[2 + f][k, rs, :] = after
                else:
                    outs[f][k, rs, :] = after
            if not final:
                whole = jnp.concatenate(afters[f], 0)
                outs[4][f, k] = column_pack(whole, ue_ref[k] if f == 0 else None)
                write_rows(whole, vn_ref[k], outs[5], f, k)
        if final:
            for a in range(strips):
                outs[2][k, pl.ds(8 * a, 8), :] = density_at(afters[0][a], afters[1][a], depth_k) * m[a]
        return carry

    if final:
        lax.fori_loop(0, levels, level, 0, unroll=2)
    else:
        for f in range(2):
            lax.fori_loop(0, levels, functools.partial(level, fields=(f,)), 0, unroll=3)


VMEM_SPEC = pl.BlockSpec(memory_space=pltpu.VMEM)


def pack_shapes(levels, rows, cols):
    return (jax.ShapeDtypeStruct((2, levels, 8, cols), jnp.float32),
            jax.ShapeDtypeStruct((2, levels, 8, cols), jnp.float32))


def edge_call(bl, nt, ns, ue, vn):
    levels, rows, cols = nt.shape
    return pl.pallas_call(
        edge_kernel,
        out_shape=pack_shapes(levels, rows, cols),
        in_specs=[VMEM_SPEC] * 5,
        out_specs=(VMEM_SPEC, VMEM_SPEC),
        cost_estimate=pl.CostEstimate(
            flops=2 * 2 * levels * 8 * rows * cols, transcendentals=0,
            bytes_accessed=4 * levels * rows * cols * 5),
    )(bl, nt, ns, ue, vn)


def step_call(mask_inputs, final, bl, nt, ns, bt, bs, xe, xw, yh, ue, vn):
    levels, rows, cols = nt.shape
    field = jax.ShapeDtypeStruct(nt.shape, jnp.float32)
    out_shape = (field,) * 3 if final else (field,) * 4 + pack_shapes(levels, rows, cols)
    return pl.pallas_call(
        functools.partial(step_kernel, mask_inputs, final),
        out_shape=out_shape,
        in_specs=[VMEM_SPEC] * 10,
        out_specs=tuple([VMEM_SPEC] * len(out_shape)),
        scratch_shapes=[pltpu.VMEM((2, levels + 1, rows, cols), jnp.float32)],
        compiler_params=pltpu.CompilerParams(vmem_limit_bytes=48 * 1024 * 1024),
        cost_estimate=pl.CostEstimate(
            flops=400 * 2 * levels * rows * cols, transcendentals=levels * rows * cols,
            bytes_accessed=4 * levels * rows * cols * (9 + len(out_shape))),
    )(bl, nt, ns, bt, bs, xe, xw, yh, ue, vn)


def exchange(xpack, ypack, at_fold):
    lon_count, lat_count = (lax.axis_size("lon"), lax.axis_size("lat"))
    from_east = lax.ppermute(xpack, "lon", [(i, (i - 1) % lon_count) for i in range(lon_count)])
    from_west = lax.ppermute(xpack, "lon", [(i, (i + 1) % lon_count) for i in range(lon_count)])
    from_north = lax.ppermute(ypack, "lat", [(i, i - 1) for i in range(1, lat_count)])
    from_south = lax.ppermute(ypack, "lat", [(i, i + 1) for i in range(lat_count - 1)])
    top = lat_count - 1
    fold_pairs = [(d * lat_count + top, (lon_count - 1 - d) * lat_count + top) for d in range(lon_count)]
    partner = lax.ppermute(ypack, ("lon", "lat"), fold_pairs)[:, :, 2:4]
    cols = ypack.shape[-1]
    flip = (jnp.arange(cols)[:, None] + jnp.arange(cols)[None, :] == cols - 1).astype(jnp.float32)
    flipped = jnp.einsum("fkrc,cd->fkrd", partner, flip, precision=lax.Precision.HIGHEST)
    mirror = jnp.concatenate([flipped[:, :, 1:2], flipped[:, :, 0:1]], 2)
    north = jnp.where(at_fold, mirror, from_north[:, :, 0:2])
    two, levels = xpack.shape[:2]
    halo_y = jnp.concatenate(
        [from_south[:, :, 2:4], north,
         from_south[:, :, 4:5], jnp.zeros((two, levels, 3, cols), jnp.float32)], 2)
    return from_east, from_west, halo_y


def on_device(
    temp_before, temp_now, salt_before, salt_now, east_velocity, north_velocity, bottom_level
):
    at_fold = lax.axis_index("lat") == lax.axis_size("lat") - 1
    xpack, ypack = edge_call(bottom_level, temp_now, salt_now, east_velocity, north_velocity)
    from_east, from_west, halo_y = exchange(xpack, ypack, at_fold)
    ft, fs, at, as_, xpack, ypack = step_call(
        True, False, bottom_level, temp_now, salt_now, temp_before, salt_before,
        from_east, from_west, halo_y, east_velocity, north_velocity)
    from_east, from_west, halo_y = exchange(xpack, ypack, at_fold)
    return step_call(False, True, bottom_level, at, as_, ft, fs, from_east, from_west, halo_y,
                     east_velocity, north_velocity)


def solution(mesh):
    return jax.shard_map(
        on_device,
        mesh=mesh,
        in_specs=(
            P(None, "lat", "lon"),
            P(None, "lat", "lon"),
            P(None, "lat", "lon"),
            P(None, "lat", "lon"),
            P(None, "lat", "lon"),
            P(None, "lat", "lon"),
            P("lat", "lon"),
        ),
        out_specs=(P(None, "lat", "lon"), P(None, "lat", "lon"), P(None, "lat", "lon")),
        check_vma=False,
    )
```
